32 devices in a mesh: dp: 4 (over y, x), fsdp: 8 (over z, core).
Axes of the slice: x: 2, y: 2, z: 4, core: 2. Of those that a mesh axis runs over, the one named last changes fastest.
Arguments:
- token_ids: int32 [32, 128], P(('dp', 'fsdp')), may hold values from 0 to 8191
- target_ids: int32 [32, 128], P(('dp', 'fsdp')), may hold values from 0 to 8191
- domain_ids: int32 [32, 1], P(('dp', 'fsdp')), may hold values from 0 to 21
- in_embed: bfloat16 [8192, 128], P('fsdp'), may hold values from -6 to 6
- out_embed: bfloat16 [8192, 128], P('fsdp'), may hold values from -42.426407 to 42.426407
- ref_norm1: bfloat16 [128], P('fsdp'), may hold values from 0.5 to 1.5
- ref_gate: bfloat16 [512, 128], P('fsdp'), may hold values from -0.5 to 0.5
- ref_up: bfloat16 [512, 128], P('fsdp'), may hold values from -0.5 to 0.5
- ref_down: bfloat16 [512, 128], P('fsdp'), may hold values from -0.25 to 0.25
- ref_norm2: bfloat16 [128], P('fsdp'), may hold values from 0.5 to 1.5
- prx_norm1: bfloat16 [128], P('fsdp'), may hold values from 0.5 to 1.5
- prx_gate: bfloat16 [512, 128], P('fsdp'), may hold values from -0.5 to 0.5
- prx_up: bfloat16 [512, 128], P('fsdp'), may hold values from -0.5 to 0.5
- prx_down: bfloat16 [512, 128], P('fsdp'), may hold values from -0.25 to 0.25
- prx_norm2: bfloat16 [128], P('fsdp'), may hold values from 0.5 to 1.5
- alpha_prev: float32 [22], replicated, may hold values from 0.01 to 0.1
Outputs:
- alpha_new: float32 [22], replicated
- grad_gate: float32 [512, 128], P('fsdp')
- grad_up: float32 [512, 128], P('fsdp')
- grad_down: float32 [512, 128], P('fsdp')
The draws below stay inside these ranges and needn't reach their ends.
Inputs may be any that keep to these rules, and one draw needn't show every extreme that they name: `domain_ids`: every one of the 22 domains is the domain of at least one row.
All inputs are finite; a program needn't handle non-finite values.
Results may differ from the reference program's by a relative error of at most 0.0075.
The reference program's roundings to bfloat16 on the way count: a program that leaves them out, or rounds other values in their place, can miss the bound.
Values may be sent and summed in bfloat16 or wider, within the bound.
No kernel may reach another device: no remote copies, remote signals or barrier semaphores. Data moves between devices by JAX's collectives and lax.ppermute only.
A program may use at most 64 MiB of HBM per device.

```python
import math
import jax
import jax.numpy as jnp
import numpy as np
from jax import lax

D = 128
FF = 512
DOMAINS = 22
SEQ = 128
ROWS_DEV = 1
VOC = 8192
ROWS = 32
N_DP = 4
N_FSDP = 8


def draw_out_embed(key, part):
    first_key = jax.random.fold_in(jax.random.fold_in(key, 11), 0)
    base = jnp.clip(jax.random.normal(first_key, (VOC, D), jnp.float32), -4.0, 4.0)
    return (base * (3.0 / math.sqrt(D))).astype(jnp.bfloat16)


def touch_ends(drawn, stream_key, least, high):
    dims = drawn.shape
    place = [jax.random.randint(jax.random.fold_in(stream_key, axis), (), 0, dims[axis]) for axis in range(len(dims))]
    drawn = drawn.at[tuple(place)].set(least)
    longest = dims.index(max(dims))
    place[longest] = (place[longest] + 1) % dims[longest]
    return drawn.at[tuple(place)].set(high)


def levels(own_key, extent, shards, low, top_value):
    def one(dim, shards_of):
        steps = jax.random.uniform(jax.random.fold_in(jax.random.fold_in(own_key, 6), dim), (shards_of,), jnp.float32, low / len(shards), top_value / len(shards))
        return jnp.repeat(jnp.exp(steps), extent[dim] // shards_of).reshape((-1,) + (1,) * (len(extent) - dim - 1))

    factor_of = one(*shards[0])
    for cut in shards[1:]:
        factor_of = factor_of * one(*cut)
    return factor_of


def rank_table(amount, skew):
    weights = [(1 << 20) // math.isqrt(grade ** skew) + 1 for grade in range(1, amount + 1)]
    width = 1 + sum(weights) // (1 << 30)
    return np.cumsum(np.array([max(1, weight // width) for weight in weights]))


def ranked(rng, dims, amount, slope):
    table = rank_table(amount, slope)
    ticket = jax.random.randint(jax.random.fold_in(rng, 1), dims, 0, int(table[amount - 1]))
    rank = jnp.searchsorted(jnp.asarray(table, jnp.int32), ticket, side="right")
    return jax.random.permutation(jax.random.fold_in(rng, 2), amount)[rank].astype(jnp.int32)


def choose_distinct(own_key, rows, count, top, lift):
    ranking = jax.random.permutation(jax.random.fold_in(own_key, 1), count)
    boost = ranking
    for power in range(3):
        boost = boost * boost // count
    boost = boost * lift // count
    lots = jax.random.randint(jax.random.fold_in(own_key, 2), (rows, count), 0, 4096) + boost
    holders = jax.random.permutation(jax.random.fold_in(own_key, 3), rows)[jnp.arange(count) % rows]
    lots = jnp.where(jnp.arange(rows)[:, None] == holders[None, :], 1 << 14, lots)
    priority = lots * count + jnp.arange(count)
    return lax.top_k(priority.astype(jnp.int32), top)[1].astype(jnp.int32)


def normal_values(key, extent, deviation, bound, shards=(), kind=jnp.bfloat16):
    drawn = deviation * jax.random.normal(key, extent, jnp.float32)
    if shards:
        drawn = drawn * levels(key, extent, shards, -0.22, 0.18)
    return jnp.clip(drawn, -bound, bound).astype(kind)


def setup_inputs(seed: int = 0) -> dict:
    streams_of = jax.random.split(jax.random.key(seed), 17)
    return {
        "token_ids": touch_ends(ranked(streams_of[0], (ROWS, SEQ), VOC, 2), jax.random.fold_in(streams_of[0], 3), 0, VOC - 1).astype(jnp.int32),
        "target_ids": touch_ends(ranked(streams_of[1], (ROWS, SEQ), VOC, 2), jax.random.fold_in(streams_of[1], 3), 0, VOC - 1).astype(jnp.int32),
        "domain_ids": choose_distinct(streams_of[2], ROWS, DOMAINS, 1, 744),
        "in_embed": normal_values(streams_of[3], (VOC, D), 1.0, 6.0, ((0, 8),)),
        "out_embed": draw_out_embed(jax.random.fold_in(streams_of[16], 71), 0),
        "ref_norm1": jnp.clip(1.0 + 0.1 * jax.random.normal(streams_of[5], (D,), jnp.float32), 0.5, 1.5).astype(jnp.bfloat16),
        "ref_gate": normal_values(streams_of[6], (FF, D), D ** -0.5, 0.5, ((0, 8),)),
        "ref_up": normal_values(streams_of[7], (FF, D), D ** -0.5, 0.5, ((0, 8),)),
        "ref_down": normal_values(streams_of[8], (FF, D), FF ** -0.5, 0.25, ((0, 8),)),
        "ref_norm2": jnp.clip(1.0 + 0.1 * jax.random.normal(streams_of[9], (D,), jnp.float32), 0.5, 1.5).astype(jnp.bfloat16),
        "prx_norm1": jnp.clip(1.0 + 0.1 * jax.random.normal(streams_of[10], (D,), jnp.float32), 0.5, 1.5).astype(jnp.bfloat16),
        "prx_gate": normal_values(streams_of[11], (FF, D), D ** -0.5, 0.5, ((0, 8),)),
        "prx_up": normal_values(streams_of[12], (FF, D), D ** -0.5, 0.5, ((0, 8),)),
        "prx_down": normal_values(streams_of[13], (FF, D), FF ** -0.5, 0.25, ((0, 8),)),
        "prx_norm2": jnp.clip(1.0 + 0.1 * jax.random.normal(streams_of[14], (D,), jnp.float32), 0.5, 1.5).astype(jnp.bfloat16),
        "alpha_prev": jnp.clip(jnp.exp(jax.random.uniform(streams_of[15], (DOMAINS,), jnp.float32, math.log(0.01), math.log(0.1))), 0.01, 0.1),
    }


EPSILON = 1e-05
SMOOTHING = 0.001

def rms_scale(values):
    return lax.rsqrt(lax.optimization_barrier(jnp.mean(values * values, axis=1, keepdims=True)) + EPSILON)

def contract_last(left_side, right_side):
    return lax.dot_general(left_side, right_side, (((1,), (1,)), ((), ())), preferred_element_type=jnp.float32)

def contract_first(left_side, right_side):
    return lax.dot_general(left_side, right_side, (((0,), (0,)), ((), ())), preferred_element_type=jnp.float32)

def feed_forward(embedded, normed, gate_weight, up_weight, down_weight, norm_first, norm_second):
    first_in = (normed * norm_first.astype(jnp.float32)).astype(jnp.bfloat16)
    gate_act = contract_last(first_in, gate_weight)
    up_act = contract_last(first_in, up_weight)
    hidden = (gate_act * jax.nn.sigmoid(gate_act) * up_act).astype(jnp.bfloat16)
    stream = embedded + jnp.dot(hidden, down_weight, preferred_element_type=jnp.float32)
    second_scale = rms_scale(stream)
    unit_stream = stream * second_scale
    second_in = (unit_stream * norm_second.astype(jnp.float32)).astype(jnp.bfloat16)
    return (second_in, (first_in, gate_act, up_act, hidden, second_scale, unit_stream))

def reference(token_ids, target_ids, domain_ids, in_embed, out_embed, ref_norm1, ref_gate, ref_up, ref_down, ref_norm2, prx_norm1, prx_gate, prx_up, prx_down, prx_norm2, alpha_prev):
    blocks = N_DP * N_FSDP
    per_block = ROWS_DEV * SEQ
    id_blocks = token_ids.reshape(blocks, per_block)
    target_blocks = target_ids.reshape(blocks, per_block)
    domain_blocks = jnp.repeat(domain_ids[:, 0], SEQ).reshape(blocks, per_block)
    vocab_range = jnp.arange(VOC, dtype=jnp.int32)
    domain_range = jnp.arange(DOMAINS, dtype=jnp.int32)

    def embed_rows(block_ids):
        embedded = jnp.take(in_embed, block_ids, axis=0).astype(jnp.float32)
        return (embedded, embedded * rms_scale(embedded))

    def head_stats(second_in, block_targets):
        logits = contract_last(second_in, out_embed)
        top_logit = lax.optimization_barrier(jnp.max(logits, axis=1, keepdims=True))
        log_total = (top_logit + jnp.log(lax.optimization_barrier(jnp.sum(jnp.exp(logits - top_logit), axis=1, keepdims=True))))[:, 0]
        picked = lax.optimization_barrier(jnp.sum(jnp.where(block_targets[:, None] == vocab_range[None, :], logits, 0.0), axis=1))
        return (logits, log_total, picked)

    def loss_step(carry, block_data):
        embedded, normed = embed_rows(block_data[0])
        ref_in = feed_forward(embedded, normed, ref_gate, ref_up, ref_down, ref_norm1, ref_norm2)[0]
        prx_in = feed_forward(embedded, normed, prx_gate, prx_up, prx_down, prx_norm1, prx_norm2)[0]
        unused_ref, ref_total, ref_pick = head_stats(ref_in, block_data[1])
        unused_prx, prx_total, prx_pick = head_stats(prx_in, block_data[1])
        excess = jnp.maximum(prx_total - prx_pick - (ref_total - ref_pick), 0.0)
        return (carry, (excess, prx_total))
    unused_carry, scanned = lax.scan(loss_step, jnp.zeros((), jnp.float32), (id_blocks, target_blocks))
    excess, prx_totals = scanned
    dom_hits = (domain_blocks[:, :, None] == domain_range[None, None, :]).astype(jnp.float32)
    domain_sums = lax.optimization_barrier(jnp.sum(dom_hits * excess[:, :, None], axis=(0, 1)))
    domain_counts = lax.optimization_barrier(jnp.sum(dom_hits, axis=(0, 1)))
    softmax_mix = jax.nn.softmax(jnp.log(alpha_prev) + domain_sums / domain_counts)
    alpha_new = (1.0 - SMOOTHING) * softmax_mix + SMOOTHING / DOMAINS
    token_ratio = math.sqrt(blocks * per_block) * alpha_new / domain_counts

    def grad_step(grad_total, block_data):
        block_ids, block_targets, block_hits, block_total = block_data
        embedded, normed = embed_rows(block_ids)
        second_in, saved_state = feed_forward(embedded, normed, prx_gate, prx_up, prx_down, prx_norm1, prx_norm2)
        first_in, gate_act, up_act, hidden, second_scale, unit_stream = saved_state
        logits = contract_last(second_in, out_embed)
        probs = jnp.exp(logits - block_total[:, None])
        hits = (block_targets[:, None] == vocab_range[None, :]).astype(jnp.float32)
        token_weight = lax.optimization_barrier(jnp.sum(block_hits * token_ratio[None, :], axis=1))
        d_logits = (token_weight[:, None] * (probs - hits)).astype(jnp.bfloat16)
        d_second = jnp.dot(d_logits, out_embed, preferred_element_type=jnp.float32)
        d_unit = d_second * prx_norm2.astype(jnp.float32)
        d_branch = (second_scale * (d_unit - unit_stream * lax.optimization_barrier(jnp.mean(d_unit * unit_stream, axis=1, keepdims=True)))).astype(jnp.bfloat16)
        d_hidden = contract_last(d_branch, prx_down)
        sigmoid_gate = jax.nn.sigmoid(gate_act)
        d_gate = (d_hidden * up_act * sigmoid_gate * (1.0 + gate_act * (1.0 - sigmoid_gate))).astype(jnp.bfloat16)
        d_up = (d_hidden * gate_act * sigmoid_gate).astype(jnp.bfloat16)
        partial_grad = jnp.concatenate([contract_first(d_gate, first_in), contract_first(d_up, first_in), contract_first(hidden, d_branch)], axis=1)
        rounded = lax.optimization_barrier(partial_grad.astype(jnp.bfloat16))
        return (grad_total + rounded.astype(jnp.float32), None)
    grad_total, unused_out = lax.scan(grad_step, jnp.zeros((FF, 3 * D), jnp.float32), (id_blocks, target_blocks, dom_hits, prx_totals))
    return (alpha_new, grad_total[:, :D], grad_total[:, D:2 * D], grad_total[:, 2 * D:])
```

```python
import math

import jax
import jax.numpy as jnp
from jax import lax
from jax.sharding import PartitionSpec as P

EPSILON = 1e-05
SMOOTHING = 0.001
FAN_OUT_MAX = 8
ID_BASE = 128


def rms_scale(values):
    return lax.rsqrt(jnp.mean(values * values, axis=1, keepdims=True) + EPSILON)


def contract_last(left_side, right_side):
    return lax.dot_general(
        left_side, right_side, (((1,), (1,)), ((), ())), preferred_element_type=jnp.float32
    )


def contract_first(left_side, right_side):
    return lax.dot_general(
        left_side, right_side, (((0,), (0,)), ((), ())), preferred_element_type=jnp.float32
    )


def shift_pairs(size, shift):
    return [(source, (source + shift) % size) for source in range(size)]


def gather_relative(value, axis):
    size = lax.axis_size(axis)
    if size <= FAN_OUT_MAX:
        pieces = [value] + [
            lax.ppermute(value, axis, shift_pairs(size, shift)) for shift in range(1, size)
        ]
        return jnp.stack(pieces)
    here = lax.axis_index(axis)
    stacked = lax.all_gather(value, axis)
    return jnp.take(stacked, (here - jnp.arange(size)) % size, axis=0)


def to_absolute(stack, axis):
    return jnp.roll(stack[::-1], lax.axis_index(axis) + 1, axis=0)


def exchange_relative(blocks, axis):
    size = lax.axis_size(axis)
    if size <= FAN_OUT_MAX:
        pieces = [blocks[0]] + [
            lax.ppermute(blocks[(-shift) % size], axis, shift_pairs(size, shift))
            for shift in range(1, size)
        ]
        return jnp.stack(pieces)
    here = lax.axis_index(axis)
    ordered = jnp.take(blocks, (here - jnp.arange(size)) % size, axis=0)
    return lax.all_to_all(ordered, axis, 0, 0, tiled=True)


def feed_forward(embedded, normed, weights):
    gate_weight, up_weight, down_weight, norm_first, norm_second = weights
    first_in = (normed * norm_first.astype(jnp.float32)).astype(jnp.bfloat16)
    gate_act = contract_last(first_in, gate_weight)
    up_act = contract_last(first_in, up_weight)
    hidden = (gate_act * jax.nn.sigmoid(gate_act) * up_act).astype(jnp.bfloat16)
    stream = embedded + jnp.dot(hidden, down_weight, preferred_element_type=jnp.float32)
    second_scale = rms_scale(stream)
    unit_stream = stream * second_scale
    second_in = (unit_stream * norm_second.astype(jnp.float32)).astype(jnp.bfloat16)
    return (second_in, (first_in, gate_act, up_act, hidden, second_scale, unit_stream))


def block_rows_of(total):
    return math.gcd(total, 1024)


def vocab_stats(inputs, table, targets):
    total = inputs.shape[0]
    rows = block_rows_of(total)
    columns = jnp.arange(table.shape[0], dtype=jnp.int32)

    def one_block(block):
        block_in, block_target = block
        logits = contract_last(block_in, table)
        top_logit = jnp.max(logits, axis=1)
        exp_total = jnp.sum(jnp.exp(logits - top_logit[:, None]), axis=1)
        picked = jnp.sum(jnp.where(block_target[:, None] == columns[None, :], logits, 0.0), axis=1)
        return jnp.stack([top_logit, exp_total, picked])

    if rows == total:
        return one_block((inputs, targets))
    result = lax.map(
        one_block, (inputs.reshape(total // rows, rows, -1), targets.reshape(total // rows, rows))
    )
    return jnp.moveaxis(result, 1, 0).reshape(3, total)


def head_gradient(inputs, table, log_total, weight, targets):
    total = inputs.shape[0]
    rows = block_rows_of(total)
    columns = jnp.arange(table.shape[0], dtype=jnp.int32)

    def one_block(block):
        block_in, block_total, block_weight, block_target = block
        logits = contract_last(block_in, table)
        probs = jnp.exp(logits - block_total[:, None])
        hits = (block_target[:, None] == columns[None, :]).astype(jnp.float32)
        d_logits = (block_weight[:, None] * (probs - hits)).astype(jnp.bfloat16)
        return jnp.dot(d_logits, table, preferred_element_type=jnp.float32)

    if rows == total:
        return one_block((inputs, log_total, weight, targets))
    count = total // rows
    result = lax.map(
        one_block,
        (
            inputs.reshape(count, rows, -1),
            log_total.reshape(count, rows),
            weight.reshape(count, rows),
            targets.reshape(count, rows),
        ),
    )
    return result.reshape(total, -1)


def body(
    token_ids,
    target_ids,
    domain_ids,
    in_embed,
    out_embed,
    ref_norm1,
    ref_gate,
    ref_up,
    ref_down,
    ref_norm2,
    prx_norm1,
    prx_gate,
    prx_up,
    prx_down,
    prx_norm2,
    alpha_prev,
):
    domain_total = alpha_prev.shape[0]
    rows_here, seq_len = token_ids.shape
    per_device = rows_here * seq_len
    vocab_here, width = in_embed.shape
    fsdp_size = lax.axis_size("fsdp")
    group_total = per_device * fsdp_size
    vocab_start = lax.axis_index("fsdp") * vocab_here
    unit_rows = ref_gate.shape[0]
    gain_here = ref_norm1.shape[0]

    tokens = token_ids.reshape(-1)
    targets = target_ids.reshape(-1)
    id_parts = jnp.stack(
        [tokens // ID_BASE, tokens % ID_BASE, targets // ID_BASE, targets % ID_BASE]
    ).astype(jnp.bfloat16)
    matrices = (ref_gate, ref_up, ref_down, prx_gate, prx_up, prx_down)
    gains = (ref_norm1, ref_norm2, prx_norm1, prx_norm2)
    packed = jnp.concatenate(
        [id_parts.reshape(-1), domain_ids.reshape(-1).astype(jnp.bfloat16)]
        + [item.reshape(-1) for item in matrices]
        + [item.reshape(-1) for item in gains]
    )
    gathered = gather_relative(packed, "fsdp")
    offset = 4 * per_device
    group_ids = gathered[:, :offset].astype(jnp.int32).reshape(fsdp_size, 4, per_device)
    group_tokens = (group_ids[:, 0] * ID_BASE + group_ids[:, 1]).reshape(-1)
    group_targets = (group_ids[:, 2] * ID_BASE + group_ids[:, 3]).reshape(-1)
    group_domains = gathered[:, offset : offset + rows_here].astype(jnp.int32)
    offset += rows_here
    matrix_size = unit_rows * width
    full_matrices = []
    for _ in matrices:
        full_matrices.append(
            gathered[:, offset : offset + matrix_size].reshape(fsdp_size * unit_rows, width)
        )
        offset += matrix_size
    full_gains = []
    for _ in gains:
        piece = gathered[:, offset : offset + gain_here]
        full_gains.append(to_absolute(piece, "fsdp").reshape(-1))
        offset += gain_here
    ref_weights = (*full_matrices[:3], full_gains[0], full_gains[1])
    prx_weights = (*full_matrices[3:], full_gains[2], full_gains[3])

    token_local = group_tokens - vocab_start
    inside = (token_local >= 0) & (token_local < vocab_here)
    picked_rows = jnp.where(
        inside[:, None], jnp.take(in_embed, jnp.clip(token_local, 0, vocab_here - 1), axis=0), 0
    ).astype(jnp.bfloat16)
    arrived = exchange_relative(picked_rows.reshape(fsdp_size, per_device, width), "fsdp")
    embedded = jnp.sum(arrived.astype(jnp.float32), axis=0)

    normed = embedded * rms_scale(embedded)
    ref_own = feed_forward(embedded, normed, ref_weights)[0]
    prx_own, saved_state = feed_forward(embedded, normed, prx_weights)

    group_features = gather_relative(jnp.concatenate([ref_own, prx_own], axis=1), "fsdp")
    group_features = group_features.reshape(group_total, 2 * width)
    ref_group = group_features[:, :width]
    prx_group = group_features[:, width:]

    target_local = group_targets - vocab_start
    ref_stats = vocab_stats(ref_group, out_embed, target_local)
    prx_stats = vocab_stats(prx_group, out_embed, target_local)

    local_stats = jnp.concatenate([ref_stats, prx_stats]).reshape(6, fsdp_size, per_device)
    local_stats = to_absolute(jnp.swapaxes(local_stats, 0, 1), "fsdp")
    all_stats = to_absolute(gather_relative(local_stats, "fsdp"), "fsdp")
    tops = all_stats[:, :, 0::3]
    exp_totals = all_stats[:, :, 1::3]
    picks = all_stats[:, :, 2::3]
    top_logit = jnp.max(tops, axis=0)
    exp_total = jnp.sum(exp_totals * jnp.exp(tops - top_logit[None]), axis=0)
    pick_total = jnp.sum(picks, axis=0)
    log_total = top_logit + jnp.log(exp_total)
    losses = log_total - pick_total
    excess = jnp.maximum(losses[:, 1] - losses[:, 0], 0.0)
    relative_order = (lax.axis_index("fsdp") - jnp.arange(fsdp_size)) % fsdp_size
    prx_log_total = jnp.take(log_total[:, 1], relative_order, axis=0).reshape(-1)

    row_excess = jnp.sum(excess.reshape(fsdp_size * rows_here, seq_len), axis=1)
    row_domains = to_absolute(group_domains, "fsdp").reshape(-1)
    domain_range = jnp.arange(domain_total, dtype=jnp.int32)
    row_hits = (row_domains[:, None] == domain_range[None, :]).astype(jnp.float32)
    group_sums = jnp.sum(row_hits * row_excess[:, None], axis=0)
    group_counts = jnp.sum(row_hits, axis=0) * seq_len

    summed = jnp.sum(
        to_absolute(gather_relative(jnp.stack([group_sums, group_counts]), "dp"), "dp"), axis=0
    )
    total_sums = summed[0]
    domain_counts = summed[1]
    softmax_mix = jax.nn.softmax(jnp.log(alpha_prev) + total_sums / domain_counts)
    alpha_new = (1.0 - SMOOTHING) * softmax_mix + SMOOTHING / domain_total
    device_total = group_total * lax.axis_size("dp")
    token_ratio = math.sqrt(device_total) * alpha_new / domain_counts
    group_rows = group_domains.reshape(-1)
    row_weight = jnp.take(token_ratio, group_rows)
    token_weight = jnp.repeat(row_weight, seq_len)

    d_second_part = head_gradient(prx_group, out_embed, prx_log_total, token_weight, target_local)

    d_second = jnp.sum(
        exchange_relative(d_second_part.reshape(fsdp_size, per_device, width), "fsdp"), axis=0
    )
    first_in, gate_act, up_act, hidden, second_scale, unit_stream = saved_state
    d_unit = d_second * prx_weights[4].astype(jnp.float32)
    d_branch = (
        second_scale
        * (d_unit - unit_stream * jnp.mean(d_unit * unit_stream, axis=1, keepdims=True))
    ).astype(jnp.bfloat16)
    d_hidden = contract_last(d_branch, prx_weights[2])
    sigmoid_gate = jax.nn.sigmoid(gate_act)
    d_gate = (d_hidden * up_act * sigmoid_gate * (1.0 + gate_act * (1.0 - sigmoid_gate))).astype(
        jnp.bfloat16
    )
    d_up = (d_hidden * gate_act * sigmoid_gate).astype(jnp.bfloat16)
    partial_grad = jnp.concatenate(
        [
            contract_first(d_gate, first_in),
            contract_first(d_up, first_in),
            contract_first(hidden, d_branch),
        ],
        axis=1,
    ).astype(jnp.bfloat16)

    arrived_grad = exchange_relative(
        partial_grad.reshape(fsdp_size, unit_rows, 3 * width), "fsdp"
    )
    local_grad = jnp.sum(arrived_grad.astype(jnp.float32), axis=0)

    grad_shard = jnp.sum(to_absolute(gather_relative(local_grad, "dp"), "dp"), axis=0)
    return (
        alpha_new,
        grad_shard[:, :width],
        grad_shard[:, width : 2 * width],
        grad_shard[:, 2 * width :],
    )


def solution(mesh):
    placed = (
        P(("dp", "fsdp"), None),
        P(("dp", "fsdp"), None),
        P(("dp", "fsdp"), None),
        P("fsdp", None),
        P("fsdp", None),
        P("fsdp"),
        P("fsdp", None),
        P("fsdp", None),
        P("fsdp", None),
        P("fsdp"),
        P("fsdp"),
        P("fsdp", None),
        P("fsdp", None),
        P("fsdp", None),
        P("fsdp"),
        P(),
    )
    return jax.shard_map(
        body,
        mesh=mesh,
        in_specs=placed,
        out_specs=(P(), P("fsdp", None), P("fsdp", None), P("fsdp", None)),
        check_vma=False,
    )
```

```python
import math

import jax
import jax.numpy as jnp
from jax import lax
from jax.sharding import PartitionSpec as P

EPSILON = 1e-05
SMOOTHING = 0.001
FAN_OUT_MAX = 8
ID_BASE = 128


def rms_scale(values):
    return lax.rsqrt(jnp.mean(values * values, axis=1, keepdims=True) + EPSILON)


def contract_last(left_side, right_side):
    return lax.dot_general(
        left_side, right_side, (((1,), (1,)), ((), ())), preferred_element_type=jnp.float32
    )


def contract_first(left_side, right_side):
    return lax.dot_general(
        left_side, right_side, (((0,), (0,)), ((), ())), preferred_element_type=jnp.float32
    )


def shift_pairs(size, shift):
    return [(source, (source + shift) % size) for source in range(size)]


def gather_relative(value, axis):
    size = lax.axis_size(axis)
    if size <= FAN_OUT_MAX:
        pieces = [value] + [
            lax.ppermute(value, axis, shift_pairs(size, shift)) for shift in range(1, size)
        ]
        return jnp.stack(pieces)
    here = lax.axis_index(axis)
    stacked = lax.all_gather(value, axis)
    return jnp.take(stacked, (here - jnp.arange(size)) % size, axis=0)


def to_absolute(stack, axis):
    return jnp.roll(stack[::-1], lax.axis_index(axis) + 1, axis=0)


def exchange_relative(blocks, axis):
    size = lax.axis_size(axis)
    if size <= FAN_OUT_MAX:
        pieces = [blocks[0]] + [
            lax.ppermute(blocks[(-shift) % size], axis, shift_pairs(size, shift))
            for shift in range(1, size)
        ]
        return jnp.stack(pieces)
    here = lax.axis_index(axis)
    ordered = jnp.take(blocks, (here - jnp.arange(size)) % size, axis=0)
    return lax.all_to_all(ordered, axis, 0, 0, tiled=True)


def feed_forward(embedded, normed, weights):
    gate_weight, up_weight, down_weight, norm_first, norm_second = weights
    first_in = (normed * norm_first.astype(jnp.float32)).astype(jnp.bfloat16)
    gate_act = contract_last(first_in, gate_weight)
    up_act = contract_last(first_in, up_weight)
    hidden = (gate_act * jax.nn.sigmoid(gate_act) * up_act).astype(jnp.bfloat16)
    stream = embedded + jnp.dot(hidden, down_weight, preferred_element_type=jnp.float32)
    second_scale = rms_scale(stream)
    unit_stream = stream * second_scale
    second_in = (unit_stream * norm_second.astype(jnp.float32)).astype(jnp.bfloat16)
    return (second_in, (first_in, gate_act, up_act, hidden, second_scale, unit_stream))


def block_rows_of(total):
    return math.gcd(total, 1024)


def vocab_stats(inputs, table, targets):
    total = inputs.shape[0]
    rows = block_rows_of(total)
    columns = jnp.arange(table.shape[0], dtype=jnp.int32)

    def one_block(block):
        block_in, block_target = block
        logits = contract_last(block_in, table)
        top_logit = jnp.max(logits, axis=1)
        exp_total = jnp.sum(jnp.exp(logits - top_logit[:, None]), axis=1)
        picked = jnp.sum(jnp.where(block_target[:, None] == columns[None, :], logits, 0.0), axis=1)
        return jnp.stack([top_logit, exp_total, picked])

    if rows == total:
        return one_block((inputs, targets))
    result = lax.map(
        one_block, (inputs.reshape(total // rows, rows, -1), targets.reshape(total // rows, rows))
    )
    return jnp.moveaxis(result, 1, 0).reshape(3, total)


def head_gradient(inputs, table, log_total, weight, targets):
    total = inputs.shape[0]
    rows = block_rows_of(total)
    columns = jnp.arange(table.shape[0], dtype=jnp.int32)

    def one_block(block):
        block_in, block_total, block_weight, block_target = block
        logits = contract_last(block_in, table)
        probs = jnp.exp(logits - block_total[:, None])
        hits = (block_target[:, None] == columns[None, :]).astype(jnp.float32)
        d_logits = (block_weight[:, None] * (probs - hits)).astype(jnp.bfloat16)
        return jnp.dot(d_logits, table, preferred_element_type=jnp.float32)

    if rows == total:
        return one_block((inputs, log_total, weight, targets))
    count = total // rows
    result = lax.map(
        one_block,
        (
            inputs.reshape(count, rows, -1),
            log_total.reshape(count, rows),
            weight.reshape(count, rows),
            targets.reshape(count, rows),
        ),
    )
    return result.reshape(total, -1)


def body(
    token_ids,
    target_ids,
    domain_ids,
    in_embed,
    out_embed,
    ref_norm1,
    ref_gate,
    ref_up,
    ref_down,
    ref_norm2,
    prx_norm1,
    prx_gate,
    prx_up,
    prx_down,
    prx_norm2,
    alpha_prev,
):
    domain_total = alpha_prev.shape[0]
    rows_here, seq_len = token_ids.shape
    per_device = rows_here * seq_len
    vocab_here, width = in_embed.shape
    fsdp_size = lax.axis_size("fsdp")
    group_total = per_device * fsdp_size
    vocab_start = lax.axis_index("fsdp") * vocab_here
    unit_rows = ref_gate.shape[0]
    gain_here = ref_norm1.shape[0]

    tokens = token_ids.reshape(-1)
    targets = target_ids.reshape(-1)
    id_parts = jnp.stack(
        [tokens // ID_BASE, tokens % ID_BASE, targets // ID_BASE, targets % ID_BASE]
    ).astype(jnp.bfloat16)
    matrices = (ref_gate, ref_up, ref_down, prx_gate, prx_up, prx_down)
    gains = (ref_norm1, ref_norm2, prx_norm1, prx_norm2)
    packed = jnp.concatenate(
        [id_parts.reshape(-1), domain_ids.reshape(-1).astype(jnp.bfloat16)]
        + [item.reshape(-1) for item in gains]
    )
    gathered = gather_relative(packed, "fsdp")
    gathered_matrices = gather_relative(jnp.concatenate(matrices, axis=0), "fsdp")
    offset = 4 * per_device
    group_ids = gathered[:, :offset].astype(jnp.int32).reshape(fsdp_size, 4, per_device)
    group_tokens = (group_ids[:, 0] * ID_BASE + group_ids[:, 1]).reshape(-1)
    group_targets = (group_ids[:, 2] * ID_BASE + group_ids[:, 3]).reshape(-1)
    group_domains = gathered[:, offset : offset + rows_here].astype(jnp.int32)
    offset += rows_here
    full_gains = []
    for _ in gains:
        piece = gathered[:, offset : offset + gain_here]
        full_gains.append(to_absolute(piece, "fsdp").reshape(-1))
        offset += gain_here
    full_matrices = [
        gathered_matrices[:, index * unit_rows : (index + 1) * unit_rows].reshape(-1, width)
        for index in range(len(matrices))
    ]
    ref_weights = (*full_matrices[:3], full_gains[0], full_gains[1])
    prx_weights = (*full_matrices[3:], full_gains[2], full_gains[3])

    token_local = group_tokens - vocab_start
    vocab_range = jnp.arange(vocab_here, dtype=jnp.int32)
    token_hits = (token_local[:, None] == vocab_range[None, :]).astype(jnp.bfloat16)
    picked_rows = jnp.dot(token_hits, in_embed, preferred_element_type=jnp.float32).astype(
        jnp.bfloat16
    )
    arrived = exchange_relative(picked_rows.reshape(fsdp_size, per_device, width), "fsdp")
    embedded = jnp.sum(arrived.astype(jnp.float32), axis=0)

    normed = embedded * rms_scale(embedded)
    ref_own = feed_forward(embedded, normed, ref_weights)[0]
    prx_own, saved_state = feed_forward(embedded, normed, prx_weights)

    group_features = gather_relative(jnp.concatenate([ref_own, prx_own], axis=1), "fsdp")
    group_features = group_features.reshape(group_total, 2 * width)
    ref_group = group_features[:, :width]
    prx_group = group_features[:, width:]

    target_local = group_targets - vocab_start
    ref_stats = vocab_stats(ref_group, out_embed, target_local)
    prx_stats = vocab_stats(prx_group, out_embed, target_local)

    local_stats = jnp.concatenate([ref_stats, prx_stats]).reshape(6, fsdp_size, per_device)
    local_stats = to_absolute(jnp.swapaxes(local_stats, 0, 1), "fsdp")
    all_stats = to_absolute(gather_relative(local_stats, "fsdp"), "fsdp")
    tops = all_stats[:, :, 0::3]
    exp_totals = all_stats[:, :, 1::3]
    picks = all_stats[:, :, 2::3]
    top_logit = jnp.max(tops, axis=0)
    exp_total = jnp.sum(exp_totals * jnp.exp(tops - top_logit[None]), axis=0)
    pick_total = jnp.sum(picks, axis=0)
    log_total = top_logit + jnp.log(exp_total)
    losses = log_total - pick_total
    excess = jnp.maximum(losses[:, 1] - losses[:, 0], 0.0)
    relative_order = (lax.axis_index("fsdp") - jnp.arange(fsdp_size)) % fsdp_size
    prx_log_total = jnp.take(log_total[:, 1], relative_order, axis=0).reshape(-1)

    row_excess = jnp.sum(excess.reshape(fsdp_size * rows_here, seq_len), axis=1)
    row_domains = to_absolute(group_domains, "fsdp").reshape(-1)
    domain_range = jnp.arange(domain_total, dtype=jnp.int32)
    row_hits = (row_domains[:, None] == domain_range[None, :]).astype(jnp.float32)
    group_sums = jnp.sum(row_hits * row_excess[:, None], axis=0)
    group_counts = jnp.sum(row_hits, axis=0) * seq_len

    summed = jnp.sum(
        to_absolute(gather_relative(jnp.stack([group_sums, group_counts]), "dp"), "dp"), axis=0
    )
    total_sums = summed[0]
    domain_counts = summed[1]
    softmax_mix = jax.nn.softmax(jnp.log(alpha_prev) + total_sums / domain_counts)
    alpha_new = (1.0 - SMOOTHING) * softmax_mix + SMOOTHING / domain_total
    device_total = group_total * lax.axis_size("dp")
    token_ratio = math.sqrt(device_total) * alpha_new / domain_counts
    group_rows = group_domains.reshape(-1)
    row_weight = jnp.take(token_ratio, group_rows)
    token_weight = jnp.repeat(row_weight, seq_len)

    d_second_part = head_gradient(prx_group, out_embed, prx_log_total, token_weight, target_local)

    d_second = jnp.sum(
        exchange_relative(d_second_part.reshape(fsdp_size, per_device, width), "fsdp"), axis=0
    )
    first_in, gate_act, up_act, hidden, second_scale, unit_stream = saved_state
    d_unit = d_second * prx_weights[4].astype(jnp.float32)
    d_branch = (
        second_scale
        * (d_unit - unit_stream * jnp.mean(d_unit * unit_stream, axis=1, keepdims=True))
    ).astype(jnp.bfloat16)
    d_hidden = contract_last(d_branch, prx_weights[2])
    sigmoid_gate = jax.nn.sigmoid(gate_act)
    d_gate = (d_hidden * up_act * sigmoid_gate * (1.0 + gate_act * (1.0 - sigmoid_gate))).astype(
        jnp.bfloat16
    )
    d_up = (d_hidden * gate_act * sigmoid_gate).astype(jnp.bfloat16)
    partial_grad = jnp.concatenate(
        [
            contract_first(d_gate, first_in),
            contract_first(d_up, first_in),
            contract_first(hidden, d_branch),
        ],
        axis=1,
    ).astype(jnp.bfloat16)

    arrived_grad = exchange_relative(
        partial_grad.reshape(fsdp_size, unit_rows, 3 * width), "fsdp"
    )
    local_grad = jnp.sum(arrived_grad.astype(jnp.float32), axis=0)

    grad_shard = jnp.sum(to_absolute(gather_relative(local_grad, "dp"), "dp"), axis=0)
    return (
        alpha_new,
        grad_shard[:, :width],
        grad_shard[:, width : 2 * width],
        grad_shard[:, 2 * width :],
    )


def solution(mesh):
    placed = (
        P(("dp", "fsdp"), None),
        P(("dp", "fsdp"), None),
        P(("dp", "fsdp"), None),
        P("fsdp", None),
        P("fsdp", None),
        P("fsdp"),
        P("fsdp", None),
        P("fsdp", None),
        P("fsdp", None),
        P("fsdp"),
        P("fsdp"),
        P("fsdp", None),
        P("fsdp", None),
        P("fsdp", None),
        P("fsdp"),
        P(),
    )
    return jax.shard_map(
        body,
        mesh=mesh,
        in_specs=placed,
        out_specs=(P(), P("fsdp", None), P("fsdp", None), P("fsdp", None)),
        check_vma=False,
    )
```

```python
import math

import jax
import jax.numpy as jnp
from jax import lax
from jax.sharding import PartitionSpec as P

EPSILON = 1e-05
SMOOTHING = 0.001
FAN_OUT_MAX = 8
ID_BASE = 128


def rms_scale(values):
    return lax.rsqrt(jnp.mean(values * values, axis=1, keepdims=True) + EPSILON)


def contract_last(left_side, right_side):
    return lax.dot_general(
        left_side, right_side, (((1,), (1,)), ((), ())), preferred_element_type=jnp.float32
    )


def contract_first(left_side, right_side):
    return lax.dot_general(
        left_side, right_side, (((0,), (0,)), ((), ())), preferred_element_type=jnp.float32
    )


def shift_pairs(size, shift):
    return [(source, (source + shift) % size) for source in range(size)]


def to_absolute(stack, axis):
    return jnp.roll(stack[::-1], lax.axis_index(axis) + 1, axis=0)


def gather_ordered(value, axis, native):
    size = lax.axis_size(axis)
    if native or size > FAN_OUT_MAX:
        return lax.all_gather(value, axis)
    pieces = [value] + [
        lax.ppermute(value, axis, shift_pairs(size, shift)) for shift in range(1, size)
    ]
    return to_absolute(jnp.stack(pieces), axis)


def exchange_ordered(blocks, axis, native):
    size = lax.axis_size(axis)
    if native or size > FAN_OUT_MAX:
        return lax.all_to_all(blocks, axis, 0, 0, tiled=True)
    here = lax.axis_index(axis)
    pieces = [lax.dynamic_index_in_dim(blocks, here, keepdims=False)] + [
        lax.ppermute(
            lax.dynamic_index_in_dim(blocks, (here + shift) % size, keepdims=False),
            axis,
            shift_pairs(size, shift),
        )
        for shift in range(1, size)
    ]
    return to_absolute(jnp.stack(pieces), axis)


def feed_forward(embedded, normed, weights):
    gate_weight, up_weight, down_weight, norm_first, norm_second = weights
    first_in = (normed * norm_first.astype(jnp.float32)).astype(jnp.bfloat16)
    gate_act = contract_last(first_in, gate_weight)
    up_act = contract_last(first_in, up_weight)
    hidden = (gate_act * jax.nn.sigmoid(gate_act) * up_act).astype(jnp.bfloat16)
    stream = embedded + jnp.dot(hidden, down_weight, preferred_element_type=jnp.float32)
    second_scale = rms_scale(stream)
    unit_stream = stream * second_scale
    second_in = (unit_stream * norm_second.astype(jnp.float32)).astype(jnp.bfloat16)
    return (second_in, (first_in, gate_act, up_act, hidden, second_scale, unit_stream))


def block_rows_of(total):
    return math.gcd(total, 1024)


def vocab_stats(inputs, table, targets):
    total = inputs.shape[0]
    rows = block_rows_of(total)
    columns = jnp.arange(table.shape[0], dtype=jnp.int32)

    def one_block(block):
        block_in, block_target = block
        logits = contract_last(block_in, table)
        top_logit = jnp.max(logits, axis=1)
        exp_total = jnp.sum(jnp.exp(logits - top_logit[:, None]), axis=1)
        picked = jnp.sum(jnp.where(block_target[:, None] == columns[None, :], logits, 0.0), axis=1)
        return jnp.stack([top_logit, exp_total, picked])

    if rows == total:
        return one_block((inputs, targets))
    result = lax.map(
        one_block, (inputs.reshape(total // rows, rows, -1), targets.reshape(total // rows, rows))
    )
    return jnp.moveaxis(result, 1, 0).reshape(3, total)


def head_gradient(inputs, table, log_total, weight, targets):
    total = inputs.shape[0]
    rows = block_rows_of(total)
    columns = jnp.arange(table.shape[0], dtype=jnp.int32)

    def one_block(block):
        block_in, block_total, block_weight, block_target = block
        logits = contract_last(block_in, table)
        probs = jnp.exp(logits - block_total[:, None])
        hits = (block_target[:, None] == columns[None, :]).astype(jnp.float32)
        d_logits = (block_weight[:, None] * (probs - hits)).astype(jnp.bfloat16)
        return jnp.dot(d_logits, table, preferred_element_type=jnp.float32)

    if rows == total:
        return one_block((inputs, log_total, weight, targets))
    count = total // rows
    result = lax.map(
        one_block,
        (
            inputs.reshape(count, rows, -1),
            log_total.reshape(count, rows),
            weight.reshape(count, rows),
            targets.reshape(count, rows),
        ),
    )
    return result.reshape(total, -1)


def body(
    token_ids,
    target_ids,
    domain_ids,
    in_embed,
    out_embed,
    ref_norm1,
    ref_gate,
    ref_up,
    ref_down,
    ref_norm2,
    prx_norm1,
    prx_gate,
    prx_up,
    prx_down,
    prx_norm2,
    alpha_prev,
):
    domain_total = alpha_prev.shape[0]
    rows_here, seq_len = token_ids.shape
    per_device = rows_here * seq_len
    vocab_here, width = in_embed.shape
    fsdp_size = lax.axis_size("fsdp")
    group_total = per_device * fsdp_size
    vocab_start = lax.axis_index("fsdp") * vocab_here
    unit_rows = ref_gate.shape[0]
    gain_here = ref_norm1.shape[0]

    tokens = token_ids.reshape(-1)
    targets = target_ids.reshape(-1)
    id_parts = jnp.stack(
        [tokens // ID_BASE, tokens % ID_BASE, targets // ID_BASE, targets % ID_BASE]
    ).astype(jnp.bfloat16)
    matrices = (ref_gate, ref_up, ref_down, prx_gate, prx_up, prx_down)
    gains = (ref_norm1, ref_norm2, prx_norm1, prx_norm2)
    small = jnp.concatenate(
        [id_parts.reshape(-1), domain_ids.reshape(-1).astype(jnp.bfloat16)]
        + [item.reshape(-1) for item in gains]
    )
    small_rows = -(-small.shape[0] // width)
    small = jnp.pad(small, (0, small_rows * width - small.shape[0])).reshape(small_rows, width)
    matrix_rows = len(matrices) * unit_rows
    packed = jnp.concatenate(list(matrices) + [small], axis=0)
    gathered = gather_ordered(packed, "fsdp", True)
    full_matrices = [
        gathered[:, index * unit_rows : (index + 1) * unit_rows].reshape(-1, width)
        for index in range(len(matrices))
    ]
    small_all = gathered[:, matrix_rows:].reshape(fsdp_size, -1)
    offset = 4 * per_device
    group_ids = small_all[:, :offset].astype(jnp.int32).reshape(fsdp_size, 4, per_device)
    group_tokens = (group_ids[:, 0] * ID_BASE + group_ids[:, 1]).reshape(-1)
    group_targets = (group_ids[:, 2] * ID_BASE + group_ids[:, 3]).reshape(-1)
    group_domains = small_all[:, offset : offset + rows_here].astype(jnp.int32)
    offset += rows_here
    full_gains = []
    for _ in gains:
        full_gains.append(small_all[:, offset : offset + gain_here].reshape(-1))
        offset += gain_here
    ref_weights = (*full_matrices[:3], full_gains[0], full_gains[1])
    prx_weights = (*full_matrices[3:], full_gains[2], full_gains[3])

    token_local = group_tokens - vocab_start
    vocab_range = jnp.arange(vocab_here, dtype=jnp.int32)
    token_hits = (token_local[:, None] == vocab_range[None, :]).astype(jnp.bfloat16)
    picked_rows = jnp.dot(token_hits, in_embed, preferred_element_type=jnp.float32).astype(
        jnp.bfloat16
    )
    arrived = exchange_ordered(picked_rows.reshape(fsdp_size, per_device, width), "fsdp", True)
    embedded = jnp.sum(arrived.astype(jnp.float32), axis=0)

    normed = embedded * rms_scale(embedded)
    ref_own = feed_forward(embedded, normed, ref_weights)[0]
    prx_own, saved_state = feed_forward(embedded, normed, prx_weights)

    group_features = gather_ordered(jnp.concatenate([ref_own, prx_own], axis=1), "fsdp", False)
    group_features = group_features.reshape(group_total, 2 * width)
    ref_group = group_features[:, :width]
    prx_group = group_features[:, width:]

    target_local = group_targets - vocab_start
    ref_stats = vocab_stats(ref_group, out_embed, target_local)
    prx_stats = vocab_stats(prx_group, out_embed, target_local)

    all_stats = gather_ordered(jnp.concatenate([ref_stats, prx_stats]), "fsdp", False)
    tops = all_stats[:, 0::3]
    exp_totals = all_stats[:, 1::3]
    picks = all_stats[:, 2::3]
    top_logit = jnp.max(tops, axis=0)
    exp_total = jnp.sum(exp_totals * jnp.exp(tops - top_logit[None]), axis=0)
    pick_total = jnp.sum(picks, axis=0)
    log_total = top_logit + jnp.log(exp_total)
    losses = log_total - pick_total
    excess = jnp.maximum(losses[1] - losses[0], 0.0)

    row_excess = jnp.sum(excess.reshape(fsdp_size * rows_here, seq_len), axis=1)
    row_domains = group_domains.reshape(-1)
    domain_range = jnp.arange(domain_total, dtype=jnp.int32)
    row_hits = (row_domains[:, None] == domain_range[None, :]).astype(jnp.float32)
    group_sums = jnp.sum(row_hits * row_excess[:, None], axis=0)
    group_counts = jnp.sum(row_hits, axis=0) * seq_len

    summed = jnp.sum(gather_ordered(jnp.stack([group_sums, group_counts]), "dp", False), axis=0)
    total_sums = summed[0]
    domain_counts = summed[1]
    softmax_mix = jax.nn.softmax(jnp.log(alpha_prev) + total_sums / domain_counts)
    alpha_new = (1.0 - SMOOTHING) * softmax_mix + SMOOTHING / domain_total
    device_total = group_total * lax.axis_size("dp")
    token_ratio = math.sqrt(device_total) * alpha_new / domain_counts
    row_weight = jnp.take(token_ratio, row_domains)
    token_weight = jnp.repeat(row_weight, seq_len)

    d_second_part = head_gradient(prx_group, out_embed, log_total[1], token_weight, target_local)

    d_second = jnp.sum(
        exchange_ordered(d_second_part.reshape(fsdp_size, per_device, width), "fsdp", False),
        axis=0,
    )
    first_in, gate_act, up_act, hidden, second_scale, unit_stream = saved_state
    d_unit = d_second * prx_weights[4].astype(jnp.float32)
    d_branch = (
        second_scale
        * (d_unit - unit_stream * jnp.mean(d_unit * unit_stream, axis=1, keepdims=True))
    ).astype(jnp.bfloat16)
    d_hidden = contract_last(d_branch, prx_weights[2])
    sigmoid_gate = jax.nn.sigmoid(gate_act)
    d_gate = (d_hidden * up_act * sigmoid_gate * (1.0 + gate_act * (1.0 - sigmoid_gate))).astype(
        jnp.bfloat16
    )
    d_up = (d_hidden * gate_act * sigmoid_gate).astype(jnp.bfloat16)
    partial_grad = jnp.concatenate(
        [
            contract_first(d_gate, first_in),
            contract_first(d_up, first_in),
            contract_first(hidden, d_branch),
        ],
        axis=1,
    ).astype(jnp.bfloat16)

    arrived_grad = exchange_ordered(
        partial_grad.reshape(fsdp_size, unit_rows, 3 * width), "fsdp", True
    )
    local_grad = jnp.sum(arrived_grad.astype(jnp.float32), axis=0)

    grad_shard = jnp.sum(gather_ordered(local_grad, "dp", False), axis=0)
    return (
        alpha_new,
        grad_shard[:, :width],
        grad_shard[:, width : 2 * width],
        grad_shard[:, 2 * width :],
    )


def solution(mesh):
    placed = (
        P(("dp", "fsdp"), None),
        P(("dp", "fsdp"), None),
        P(("dp", "fsdp"), None),
        P("fsdp", None),
        P("fsdp", None),
        P("fsdp"),
        P("fsdp", None),
        P("fsdp", None),
        P("fsdp", None),
        P("fsdp"),
        P("fsdp"),
        P("fsdp", None),
        P("fsdp", None),
        P("fsdp", None),
        P("fsdp"),
        P(),
    )
    return jax.shard_map(
        body,
        mesh=mesh,
        in_specs=placed,
        out_specs=(P(), P("fsdp", None), P("fsdp", None), P("fsdp", None)),
        check_vma=False,
    )
```

```python
import math

import jax
import jax.numpy as jnp
from jax import lax
from jax.sharding import PartitionSpec as P

EPSILON = 1e-05
SMOOTHING = 0.001
FAN_OUT_MAX = 8
ID_BASE = 128


def rms_scale(values):
    return lax.rsqrt(jnp.mean(values * values, axis=1, keepdims=True) + EPSILON)


def contract_last(left_side, right_side):
    return lax.dot_general(
        left_side, right_side, (((1,), (1,)), ((), ())), preferred_element_type=jnp.float32
    )


def contract_first(left_side, right_side):
    return lax.dot_general(
        left_side, right_side, (((0,), (0,)), ((), ())), preferred_element_type=jnp.float32
    )


def shift_pairs(size, shift):
    return [(source, (source + shift) % size) for source in range(size)]


def to_absolute(stack, axis):
    return jnp.roll(stack[::-1], lax.axis_index(axis) + 1, axis=0)


def gather_ordered(value, axis, native):
    size = lax.axis_size(axis)
    if native or size > FAN_OUT_MAX:
        return lax.all_gather(value, axis)
    pieces = [value] + [
        lax.ppermute(value, axis, shift_pairs(size, shift)) for shift in range(1, size)
    ]
    return to_absolute(jnp.stack(pieces), axis)


def exchange_ordered(blocks, axis, native):
    size = lax.axis_size(axis)
    if native or size > FAN_OUT_MAX:
        return lax.all_to_all(blocks, axis, 0, 0, tiled=True)
    here = lax.axis_index(axis)
    pieces = [lax.dynamic_index_in_dim(blocks, here, keepdims=False)] + [
        lax.ppermute(
            lax.dynamic_index_in_dim(blocks, (here + shift) % size, keepdims=False),
            axis,
            shift_pairs(size, shift),
        )
        for shift in range(1, size)
    ]
    return to_absolute(jnp.stack(pieces), axis)


def feed_forward(embedded, normed, weights):
    gate_weight, up_weight, down_weight, norm_first, norm_second = weights
    first_in = (normed * norm_first.astype(jnp.float32)).astype(jnp.bfloat16)
    gate_act = contract_last(first_in, gate_weight)
    up_act = contract_last(first_in, up_weight)
    hidden = (gate_act * jax.nn.sigmoid(gate_act) * up_act).astype(jnp.bfloat16)
    stream = embedded + jnp.dot(hidden, down_weight, preferred_element_type=jnp.float32)
    second_scale = rms_scale(stream)
    unit_stream = stream * second_scale
    second_in = (unit_stream * norm_second.astype(jnp.float32)).astype(jnp.bfloat16)
    return (second_in, (first_in, gate_act, up_act, hidden, second_scale, unit_stream))


def block_rows_of(total):
    return math.gcd(total, 1024)


def vocab_stats(inputs, table, targets):
    total = inputs.shape[0]
    rows = block_rows_of(total)
    columns = jnp.arange(table.shape[0], dtype=jnp.int32)

    def one_block(block):
        block_in, block_target = block
        logits = contract_last(block_in, table)
        top_logit = jnp.max(logits, axis=1)
        exp_total = jnp.sum(jnp.exp(logits - top_logit[:, None]), axis=1)
        picked = jnp.sum(jnp.where(block_target[:, None] == columns[None, :], logits, 0.0), axis=1)
        return jnp.stack([top_logit, exp_total, picked])

    if rows == total:
        return one_block((inputs, targets))
    result = lax.map(
        one_block, (inputs.reshape(total // rows, rows, -1), targets.reshape(total // rows, rows))
    )
    return jnp.moveaxis(result, 1, 0).reshape(3, total)


def head_gradient(inputs, table, log_total, weight, targets):
    total = inputs.shape[0]
    rows = block_rows_of(total)
    columns = jnp.arange(table.shape[0], dtype=jnp.int32)

    def one_block(block):
        block_in, block_total, block_weight, block_target = block
        logits = contract_last(block_in, table)
        probs = jnp.exp(logits - block_total[:, None])
        hits = (block_target[:, None] == columns[None, :]).astype(jnp.float32)
        d_logits = (block_weight[:, None] * (probs - hits)).astype(jnp.bfloat16)
        return jnp.dot(d_logits, table, preferred_element_type=jnp.float32)

    if rows == total:
        return one_block((inputs, log_total, weight, targets))
    count = total // rows
    result = lax.map(
        one_block,
        (
            inputs.reshape(count, rows, -1),
            log_total.reshape(count, rows),
            weight.reshape(count, rows),
            targets.reshape(count, rows),
        ),
    )
    return result.reshape(total, -1)


def body(
    token_ids,
    target_ids,
    domain_ids,
    in_embed,
    out_embed,
    ref_norm1,
    ref_gate,
    ref_up,
    ref_down,
    ref_norm2,
    prx_norm1,
    prx_gate,
    prx_up,
    prx_down,
    prx_norm2,
    alpha_prev,
):
    domain_total = alpha_prev.shape[0]
    rows_here, seq_len = token_ids.shape
    per_device = rows_here * seq_len
    vocab_here, width = in_embed.shape
    fsdp_size = lax.axis_size("fsdp")
    group_total = per_device * fsdp_size
    vocab_start = lax.axis_index("fsdp") * vocab_here
    unit_rows = ref_gate.shape[0]
    gain_here = ref_norm1.shape[0]

    tokens = token_ids.reshape(-1)
    targets = target_ids.reshape(-1)
    id_parts = jnp.stack(
        [tokens // ID_BASE, tokens % ID_BASE, targets // ID_BASE, targets % ID_BASE]
    ).astype(jnp.bfloat16)
    matrices = (ref_gate, ref_up, ref_down, prx_gate, prx_up, prx_down)
    gains = (ref_norm1, ref_norm2, prx_norm1, prx_norm2)
    id_rows = id_parts.reshape(-1, width)
    extra = [domain_ids.reshape(-1).astype(jnp.bfloat16)] + list(gains)
    extra_size = rows_here + len(gains) * gain_here
    extra_rows = -(-extra_size // width)
    extra.append(jnp.zeros((extra_rows * width - extra_size,), jnp.bfloat16))
    extra_rows = jnp.concatenate(extra).reshape(extra_rows, width)
    matrix_rows = len(matrices) * unit_rows
    packed = jnp.concatenate(list(matrices) + [id_rows, extra_rows], axis=0)
    gathered = gather_ordered(packed, "fsdp", True)
    full_matrices = [
        gathered[:, index * unit_rows : (index + 1) * unit_rows].reshape(-1, width)
        for index in range(len(matrices))
    ]
    offset = matrix_rows
    id_count = id_rows.shape[0]
    group_ids = gathered[:, offset : offset + id_count].astype(jnp.int32)
    group_ids = group_ids.reshape(fsdp_size, 4, per_device)
    group_tokens = (group_ids[:, 0] * ID_BASE + group_ids[:, 1]).reshape(-1)
    group_targets = (group_ids[:, 2] * ID_BASE + group_ids[:, 3]).reshape(-1)
    offset += id_count
    extra_all = gathered[:, offset:].reshape(fsdp_size, -1)
    group_domains = extra_all[:, :rows_here].astype(jnp.int32)
    full_gains = [
        extra_all[:, rows_here + index * gain_here : rows_here + (index + 1) * gain_here].reshape(-1)
        for index in range(len(gains))
    ]
    ref_weights = (*full_matrices[:3], full_gains[0], full_gains[1])
    prx_weights = (*full_matrices[3:], full_gains[2], full_gains[3])

    token_local = group_tokens - vocab_start
    vocab_range = jnp.arange(vocab_here, dtype=jnp.int32)
    token_hits = (token_local[:, None] == vocab_range[None, :]).astype(jnp.bfloat16)
    picked_rows = jnp.dot(token_hits, in_embed, preferred_element_type=jnp.float32).astype(
        jnp.bfloat16
    )
    arrived = exchange_ordered(picked_rows.reshape(fsdp_size, per_device, width), "fsdp", True)
    embedded = jnp.sum(arrived.astype(jnp.float32), axis=0)

    normed = embedded * rms_scale(embedded)
    ref_own = feed_forward(embedded, normed, ref_weights)[0]
    prx_own, saved_state = feed_forward(embedded, normed, prx_weights)

    group_features = gather_ordered(jnp.concatenate([ref_own, prx_own], axis=1), "fsdp", False)
    group_features = group_features.reshape(group_total, 2 * width)
    ref_group = group_features[:, :width]
    prx_group = group_features[:, width:]

    target_local = group_targets - vocab_start
    ref_stats = vocab_stats(ref_group, out_embed, target_local)
    prx_stats = vocab_stats(prx_group, out_embed, target_local)

    all_stats = gather_ordered(jnp.concatenate([ref_stats, prx_stats]), "fsdp", False)
    tops = all_stats[:, 0::3]
    exp_totals = all_stats[:, 1::3]
    picks = all_stats[:, 2::3]
    top_logit = jnp.max(tops, axis=0)
    exp_total = jnp.sum(exp_totals * jnp.exp(tops - top_logit[None]), axis=0)
    pick_total = jnp.sum(picks, axis=0)
    log_total = top_logit + jnp.log(exp_total)
    losses = log_total - pick_total
    excess = jnp.maximum(losses[1] - losses[0], 0.0)

    row_excess = jnp.sum(excess.reshape(fsdp_size * rows_here, seq_len), axis=1)
    row_domains = group_domains.reshape(-1)
    domain_range = jnp.arange(domain_total, dtype=jnp.int32)
    row_hits = (row_domains[:, None] == domain_range[None, :]).astype(jnp.float32)
    group_sums = jnp.sum(row_hits * row_excess[:, None], axis=0)
    group_counts = jnp.sum(row_hits, axis=0) * seq_len

    summed = jnp.sum(gather_ordered(jnp.stack([group_sums, group_counts]), "dp", False), axis=0)
    total_sums = summed[0]
    domain_counts = summed[1]
    softmax_mix = jax.nn.softmax(jnp.log(alpha_prev) + total_sums / domain_counts)
    alpha_new = (1.0 - SMOOTHING) * softmax_mix + SMOOTHING / domain_total
    device_total = group_total * lax.axis_size("dp")
    token_ratio = math.sqrt(device_total) * alpha_new / domain_counts
    row_weight = jnp.take(token_ratio, row_domains)
    token_weight = jnp.repeat(row_weight, seq_len)

    d_second_part = head_gradient(prx_group, out_embed, log_total[1], token_weight, target_local)

    d_second = jnp.sum(
        exchange_ordered(d_second_part.reshape(fsdp_size, per_device, width), "fsdp", False),
        axis=0,
    )
    first_in, gate_act, up_act, hidden, second_scale, unit_stream = saved_state
    d_unit = d_second * prx_weights[4].astype(jnp.float32)
    d_branch = (
        second_scale
        * (d_unit - unit_stream * jnp.mean(d_unit * unit_stream, axis=1, keepdims=True))
    ).astype(jnp.bfloat16)
    d_hidden = contract_last(d_branch, prx_weights[2])
    sigmoid_gate = jax.nn.sigmoid(gate_act)
    d_gate = (d_hidden * up_act * sigmoid_gate * (1.0 + gate_act * (1.0 - sigmoid_gate))).astype(
        jnp.bfloat16
    )
    d_up = (d_hidden * gate_act * sigmoid_gate).astype(jnp.bfloat16)
    partial_grad = jnp.concatenate(
        [
            contract_first(d_gate, first_in),
            contract_first(d_up, first_in),
            contract_first(hidden, d_branch),
        ],
        axis=1,
    ).astype(jnp.bfloat16)

    arrived_grad = exchange_ordered(
        partial_grad.reshape(fsdp_size, unit_rows, 3 * width), "fsdp", True
    )
    local_grad = jnp.sum(arrived_grad.astype(jnp.float32), axis=0)

    grad_shard = jnp.sum(gather_ordered(local_grad, "dp", False), axis=0)
    return (
        alpha_new,
        grad_shard[:, :width],
        grad_shard[:, width : 2 * width],
        grad_shard[:, 2 * width :],
    )


def solution(mesh):
    placed = (
        P(("dp", "fsdp"), None),
        P(("dp", "fsdp"), None),
        P(("dp", "fsdp"), None),
        P("fsdp", None),
        P("fsdp", None),
        P("fsdp"),
        P("fsdp", None),
        P("fsdp", None),
        P("fsdp", None),
        P("fsdp"),
        P("fsdp"),
        P("fsdp", None),
        P("fsdp", None),
        P("fsdp", None),
        P("fsdp"),
        P(),
    )
    return jax.shard_map(
        body,
        mesh=mesh,
        in_specs=placed,
        out_specs=(P(), P("fsdp", None), P("fsdp", None), P("fsdp", None)),
        check_vma=False,
    )
```

```python
import math

import jax
import jax.numpy as jnp
from jax import lax
from jax.sharding import PartitionSpec as P

EPSILON = 1e-05
SMOOTHING = 0.001
FAN_OUT_MAX = 8
ID_BASE = 128


def rms_scale(values):
    return lax.rsqrt(jnp.mean(values * values, axis=1, keepdims=True) + EPSILON)


def contract_last(left_side, right_side):
    return lax.dot_general(
        left_side, right_side, (((1,), (1,)), ((), ())), preferred_element_type=jnp.float32
    )


def contract_first(left_side, right_side):
    return lax.dot_general(
        left_side, right_side, (((0,), (0,)), ((), ())), preferred_element_type=jnp.float32
    )


def shift_pairs(size, shift):
    return [(source, (source + shift) % size) for source in range(size)]


def to_absolute(stack, axis):
    return jnp.roll(stack[::-1], lax.axis_index(axis) + 1, axis=0)


def gather_ordered(value, axis, native):
    size = lax.axis_size(axis)
    if native or size > FAN_OUT_MAX:
        return lax.all_gather(value, axis)
    pieces = [value] + [
        lax.ppermute(value, axis, shift_pairs(size, shift)) for shift in range(1, size)
    ]
    return to_absolute(jnp.stack(pieces), axis)


def exchange_ordered(blocks, axis, native):
    size = lax.axis_size(axis)
    if native or size > FAN_OUT_MAX:
        return lax.all_to_all(blocks, axis, 0, 0, tiled=True)
    here = lax.axis_index(axis)
    pieces = [lax.dynamic_index_in_dim(blocks, here, keepdims=False)] + [
        lax.ppermute(
            lax.dynamic_index_in_dim(blocks, (here + shift) % size, keepdims=False),
            axis,
            shift_pairs(size, shift),
        )
        for shift in range(1, size)
    ]
    return to_absolute(jnp.stack(pieces), axis)


def feed_forward(embedded, normed, weights):
    gate_weight, up_weight, down_weight, norm_first, norm_second = weights
    first_in = (normed * norm_first.astype(jnp.float32)).astype(jnp.bfloat16)
    gate_act = contract_last(first_in, gate_weight)
    up_act = contract_last(first_in, up_weight)
    hidden = (gate_act * jax.nn.sigmoid(gate_act) * up_act).astype(jnp.bfloat16)
    stream = embedded + jnp.dot(hidden, down_weight, preferred_element_type=jnp.float32)
    second_scale = rms_scale(stream)
    unit_stream = stream * second_scale
    second_in = (unit_stream * norm_second.astype(jnp.float32)).astype(jnp.bfloat16)
    return (second_in, (first_in, gate_act, up_act, hidden, second_scale, unit_stream))


def block_rows_of(total):
    return math.gcd(total, 1024)


def vocab_stats(inputs, table, targets):
    total = inputs.shape[0]
    rows = block_rows_of(total)
    columns = jnp.arange(table.shape[0], dtype=jnp.int32)

    def one_block(block):
        block_in, block_target = block
        logits = contract_last(block_in, table)
        top_logit = jnp.max(logits, axis=1)
        exp_total = jnp.sum(jnp.exp(logits - top_logit[:, None]), axis=1)
        picked = jnp.sum(jnp.where(block_target[:, None] == columns[None, :], logits, 0.0), axis=1)
        return jnp.stack([top_logit, exp_total, picked])

    if rows == total:
        return one_block((inputs, targets))
    result = lax.map(
        one_block, (inputs.reshape(total // rows, rows, -1), targets.reshape(total // rows, rows))
    )
    return jnp.moveaxis(result, 1, 0).reshape(3, total)


def head_gradient(inputs, table, log_total, weight, targets):
    total = inputs.shape[0]
    rows = block_rows_of(total)
    columns = jnp.arange(table.shape[0], dtype=jnp.int32)

    def one_block(block):
        block_in, block_total, block_weight, block_target = block
        logits = contract_last(block_in, table)
        probs = jnp.exp(logits - block_total[:, None])
        hits = (block_target[:, None] == columns[None, :]).astype(jnp.float32)
        d_logits = (block_weight[:, None] * (probs - hits)).astype(jnp.bfloat16)
        return jnp.dot(d_logits, table, preferred_element_type=jnp.float32)

    if rows == total:
        return one_block((inputs, log_total, weight, targets))
    count = total // rows
    result = lax.map(
        one_block,
        (
            inputs.reshape(count, rows, -1),
            log_total.reshape(count, rows),
            weight.reshape(count, rows),
            targets.reshape(count, rows),
        ),
    )
    return result.reshape(total, -1)


def body(
    token_ids,
    target_ids,
    domain_ids,
    in_embed,
    out_embed,
    ref_norm1,
    ref_gate,
    ref_up,
    ref_down,
    ref_norm2,
    prx_norm1,
    prx_gate,
    prx_up,
    prx_down,
    prx_norm2,
    alpha_prev,
):
    domain_total = alpha_prev.shape[0]
    rows_here, seq_len = token_ids.shape
    per_device = rows_here * seq_len
    vocab_here, width = in_embed.shape
    fsdp_size = lax.axis_size("fsdp")
    group_total = per_device * fsdp_size
    vocab_start = lax.axis_index("fsdp") * vocab_here
    unit_rows = ref_gate.shape[0]
    gain_here = ref_norm1.shape[0]

    tokens = token_ids.reshape(-1)
    targets = target_ids.reshape(-1)
    matrices = (ref_gate, ref_up, ref_down, prx_gate, prx_up, prx_down)
    gains = (ref_norm1, ref_norm2, prx_norm1, prx_norm2)
    id_count = 4 * per_device // width
    extra_size = rows_here + len(gains) * gain_here
    extra_count = -(-extra_size // width)
    small_count = id_count + extra_count
    id_pieces = (tokens // ID_BASE, tokens % ID_BASE, targets // ID_BASE, targets % ID_BASE)
    small = jnp.zeros((small_count * width,), jnp.bfloat16)
    start = 0
    for piece in id_pieces + (domain_ids.reshape(-1),) + gains:
        piece = piece.astype(jnp.bfloat16)
        small = small + jnp.pad(piece, (start, small_count * width - start - piece.shape[0]))
        start += piece.shape[0]
    id_rows = small.reshape(small_count, width)[:id_count]
    extra_rows = small.reshape(small_count, width)[id_count:]
    matrix_rows = len(matrices) * unit_rows
    packed = jnp.concatenate(list(matrices) + [small.reshape(small_count, width)], axis=0)
    gathered = gather_ordered(packed, "fsdp", True)
    full_matrices = [
        gathered[:, index * unit_rows : (index + 1) * unit_rows].reshape(-1, width)
        for index in range(len(matrices))
    ]
    offset = matrix_rows
    group_ids = gathered[:, offset : offset + id_count].astype(jnp.int32)
    group_ids = group_ids.reshape(fsdp_size, 4, per_device)
    group_tokens = (group_ids[:, 0] * ID_BASE + group_ids[:, 1]).reshape(-1)
    group_targets = (group_ids[:, 2] * ID_BASE + group_ids[:, 3]).reshape(-1)
    offset += id_count
    extra_all = gathered[:, offset:].reshape(fsdp_size, -1)
    group_domains = extra_all[:, :rows_here].astype(jnp.int32)
    full_gains = [
        extra_all[:, rows_here + index * gain_here : rows_here + (index + 1) * gain_here].reshape(-1)
        for index in range(len(gains))
    ]
    ref_weights = (*full_matrices[:3], full_gains[0], full_gains[1])
    prx_weights = (*full_matrices[3:], full_gains[2], full_gains[3])

    token_local = group_tokens - vocab_start
    vocab_range = jnp.arange(vocab_here, dtype=jnp.int32)
    token_hits = (token_local[:, None] == vocab_range[None, :]).astype(jnp.bfloat16)
    picked_rows = jnp.dot(token_hits, in_embed, preferred_element_type=jnp.float32).astype(
        jnp.bfloat16
    )
    arrived = exchange_ordered(picked_rows.reshape(fsdp_size, per_device, width), "fsdp", True)
    embedded = jnp.sum(arrived.astype(jnp.float32), axis=0)

    normed = embedded * rms_scale(embedded)
    ref_own = feed_forward(embedded, normed, ref_weights)[0]
    prx_own, saved_state = feed_forward(embedded, normed, prx_weights)

    group_features = gather_ordered(jnp.concatenate([ref_own, prx_own], axis=1), "fsdp", False)
    group_features = group_features.reshape(group_total, 2 * width)
    ref_group = group_features[:, :width]
    prx_group = group_features[:, width:]

    target_local = group_targets - vocab_start
    ref_stats = vocab_stats(ref_group, out_embed, target_local)
    prx_stats = vocab_stats(prx_group, out_embed, target_local)

    all_stats = gather_ordered(jnp.concatenate([ref_stats, prx_stats]), "fsdp", False)
    tops = all_stats[:, 0::3]
    exp_totals = all_stats[:, 1::3]
    picks = all_stats[:, 2::3]
    top_logit = jnp.max(tops, axis=0)
    exp_total = jnp.sum(exp_totals * jnp.exp(tops - top_logit[None]), axis=0)
    pick_total = jnp.sum(picks, axis=0)
    log_total = top_logit + jnp.log(exp_total)
    losses = log_total - pick_total
    excess = jnp.maximum(losses[1] - losses[0], 0.0)

    row_excess = jnp.sum(excess.reshape(fsdp_size * rows_here, seq_len), axis=1)
    row_domains = group_domains.reshape(-1)
    domain_range = jnp.arange(domain_total, dtype=jnp.int32)
    row_hits = (row_domains[:, None] == domain_range[None, :]).astype(jnp.float32)
    group_sums = jnp.sum(row_hits * row_excess[:, None], axis=0)
    group_counts = jnp.sum(row_hits, axis=0) * seq_len

    summed = jnp.sum(gather_ordered(jnp.stack([group_sums, group_counts]), "dp", False), axis=0)
    total_sums = summed[0]
    domain_counts = summed[1]
    softmax_mix = jax.nn.softmax(jnp.log(alpha_prev) + total_sums / domain_counts)
    alpha_new = (1.0 - SMOOTHING) * softmax_mix + SMOOTHING / domain_total
    device_total = group_total * lax.axis_size("dp")
    token_ratio = math.sqrt(device_total) * alpha_new / domain_counts
    row_weight = jnp.take(token_ratio, row_domains)
    token_weight = jnp.repeat(row_weight, seq_len)

    d_second_part = head_gradient(prx_group, out_embed, log_total[1], token_weight, target_local)

    d_second = jnp.sum(
        exchange_ordered(d_second_part.reshape(fsdp_size, per_device, width), "fsdp", False),
        axis=0,
    )
    first_in, gate_act, up_act, hidden, second_scale, unit_stream = saved_state
    d_unit = d_second * prx_weights[4].astype(jnp.float32)
    d_branch = (
        second_scale
        * (d_unit - unit_stream * jnp.mean(d_unit * unit_stream, axis=1, keepdims=True))
    ).astype(jnp.bfloat16)
    d_hidden = contract_last(d_branch, prx_weights[2])
    sigmoid_gate = jax.nn.sigmoid(gate_act)
    d_gate = (d_hidden * up_act * sigmoid_gate * (1.0 + gate_act * (1.0 - sigmoid_gate))).astype(
        jnp.bfloat16
    )
    d_up = (d_hidden * gate_act * sigmoid_gate).astype(jnp.bfloat16)
    partial_grad = jnp.concatenate(
        [
            contract_first(d_gate, first_in),
            contract_first(d_up, first_in),
            contract_first(hidden, d_branch),
        ],
        axis=1,
    ).astype(jnp.bfloat16)

    arrived_grad = exchange_ordered(
        partial_grad.reshape(fsdp_size, unit_rows, 3 * width), "fsdp", True
    )
    local_grad = jnp.sum(arrived_grad.astype(jnp.float32), axis=0)

    grad_shard = jnp.sum(gather_ordered(local_grad, "dp", False), axis=0)
    return (
        alpha_new,
        grad_shard[:, :width],
        grad_shard[:, width : 2 * width],
        grad_shard[:, 2 * width :],
    )


def solution(mesh):
    placed = (
        P(("dp", "fsdp"), None),
        P(("dp", "fsdp"), None),
        P(("dp", "fsdp"), None),
        P("fsdp", None),
        P("fsdp", None),
        P("fsdp"),
        P("fsdp", None),
        P("fsdp", None),
        P("fsdp", None),
        P("fsdp"),
        P("fsdp"),
        P("fsdp", None),
        P("fsdp", None),
        P("fsdp", None),
        P("fsdp"),
        P(),
    )
    return jax.shard_map(
        body,
        mesh=mesh,
        in_specs=placed,
        out_specs=(P(), P("fsdp", None), P("fsdp", None), P("fsdp", None)),
        check_vma=False,
    )
```

```python
import math

import jax
import jax.numpy as jnp
from jax import lax
from jax.sharding import PartitionSpec as P

EPSILON = 1e-05
SMOOTHING = 0.001
FAN_OUT_MAX = 8
ID_BASE = 128


def rms_scale(values):
    return lax.rsqrt(jnp.mean(values * values, axis=1, keepdims=True) + EPSILON)


def contract_last(left_side, right_side):
    return lax.dot_general(
        left_side, right_side, (((1,), (1,)), ((), ())), preferred_element_type=jnp.float32
    )


def contract_first(left_side, right_side):
    return lax.dot_general(
        left_side, right_side, (((0,), (0,)), ((), ())), preferred_element_type=jnp.float32
    )


def shift_pairs(size, shift):
    return [(source, (source + shift) % size) for source in range(size)]


def to_absolute(stack, axis):
    return jnp.roll(stack[::-1], lax.axis_index(axis) + 1, axis=0)


def gather_ordered(value, axis, native):
    size = lax.axis_size(axis)
    if native or size > FAN_OUT_MAX:
        return lax.all_gather(value, axis)
    pieces = [value] + [
        lax.ppermute(value, axis, shift_pairs(size, shift)) for shift in range(1, size)
    ]
    return to_absolute(jnp.stack(pieces), axis)


def exchange_ordered(blocks, axis, native):
    size = lax.axis_size(axis)
    if native or size > FAN_OUT_MAX:
        return lax.all_to_all(blocks, axis, 0, 0, tiled=True)
    here = lax.axis_index(axis)
    pieces = [lax.dynamic_index_in_dim(blocks, here, keepdims=False)] + [
        lax.ppermute(
            lax.dynamic_index_in_dim(blocks, (here + shift) % size, keepdims=False),
            axis,
            shift_pairs(size, shift),
        )
        for shift in range(1, size)
    ]
    return to_absolute(jnp.stack(pieces), axis)


def feed_forward(embedded, normed, weights):
    gate_weight, up_weight, down_weight, norm_first, norm_second = weights
    first_in = (normed * norm_first.astype(jnp.float32)).astype(jnp.bfloat16)
    gate_act = contract_last(first_in, gate_weight)
    up_act = contract_last(first_in, up_weight)
    hidden = (gate_act * jax.nn.sigmoid(gate_act) * up_act).astype(jnp.bfloat16)
    stream = embedded + jnp.dot(hidden, down_weight, preferred_element_type=jnp.float32)
    second_scale = rms_scale(stream)
    unit_stream = stream * second_scale
    second_in = (unit_stream * norm_second.astype(jnp.float32)).astype(jnp.bfloat16)
    return (second_in, (first_in, gate_act, up_act, hidden, second_scale, unit_stream))


def block_rows_of(total):
    return math.gcd(total, 1024)


def vocab_stats(inputs, table, targets):
    total = inputs.shape[0]
    rows = block_rows_of(total)
    columns = jnp.arange(table.shape[0], dtype=jnp.int32)

    def one_block(block):
        block_in, block_target = block
        logits = contract_last(block_in, table)
        top_logit = jnp.max(logits, axis=1)
        exp_total = jnp.sum(jnp.exp(logits - top_logit[:, None]), axis=1)
        picked = jnp.sum(jnp.where(block_target[:, None] == columns[None, :], logits, 0.0), axis=1)
        return jnp.stack([top_logit, exp_total, picked])

    if rows == total:
        return one_block((inputs, targets))
    result = lax.map(
        one_block, (inputs.reshape(total // rows, rows, -1), targets.reshape(total // rows, rows))
    )
    return jnp.moveaxis(result, 1, 0).reshape(3, total)


def head_gradient(inputs, table, log_total, weight, targets):
    total = inputs.shape[0]
    rows = block_rows_of(total)
    columns = jnp.arange(table.shape[0], dtype=jnp.int32)

    def one_block(block):
        block_in, block_total, block_weight, block_target = block
        logits = contract_last(block_in, table)
        probs = jnp.exp(logits - block_total[:, None])
        hits = (block_target[:, None] == columns[None, :]).astype(jnp.float32)
        d_logits = (block_weight[:, None] * (probs - hits)).astype(jnp.bfloat16)
        return jnp.dot(d_logits, table, preferred_element_type=jnp.float32)

    if rows == total:
        return one_block((inputs, log_total, weight, targets))
    count = total // rows
    result = lax.map(
        one_block,
        (
            inputs.reshape(count, rows, -1),
            log_total.reshape(count, rows),
            weight.reshape(count, rows),
            targets.reshape(count, rows),
        ),
    )
    return result.reshape(total, -1)


def body(
    token_ids,
    target_ids,
    domain_ids,
    in_embed,
    out_embed,
    ref_norm1,
    ref_gate,
    ref_up,
    ref_down,
    ref_norm2,
    prx_norm1,
    prx_gate,
    prx_up,
    prx_down,
    prx_norm2,
    alpha_prev,
):
    domain_total = alpha_prev.shape[0]
    rows_here, seq_len = token_ids.shape
    per_device = rows_here * seq_len
    vocab_here, width = in_embed.shape
    fsdp_size = lax.axis_size("fsdp")
    group_total = per_device * fsdp_size
    vocab_start = lax.axis_index("fsdp") * vocab_here
    unit_rows = ref_gate.shape[0]
    gain_here = ref_norm1.shape[0]

    tokens = token_ids.reshape(-1)
    targets = target_ids.reshape(-1)
    matrices = (ref_gate, ref_up, ref_down, prx_gate, prx_up, prx_down)
    gains = (ref_norm1, ref_norm2, prx_norm1, prx_norm2)
    id_count = 4 * per_device // width
    extra_size = rows_here + len(gains) * gain_here
    extra_count = -(-extra_size // width)
    small_count = id_count + extra_count
    id_pieces = (tokens // ID_BASE, tokens % ID_BASE, targets // ID_BASE, targets % ID_BASE)
    small = jnp.zeros((small_count * width,), jnp.bfloat16)
    start = 0
    for piece in id_pieces + (domain_ids.reshape(-1),) + gains:
        piece = piece.astype(jnp.bfloat16)
        small = small + jnp.pad(piece, (start, small_count * width - start - piece.shape[0]))
        start += piece.shape[0]
    id_rows = small.reshape(small_count, width)[:id_count]
    extra_rows = small.reshape(small_count, width)[id_count:]
    matrix_rows = len(matrices) * unit_rows
    packed = jnp.concatenate(list(matrices) + [small.reshape(small_count, width)], axis=0)
    gathered = gather_ordered(packed, "fsdp", True)
    full_matrices = [
        gathered[:, index * unit_rows : (index + 1) * unit_rows].reshape(-1, width)
        for index in range(len(matrices))
    ]
    offset = matrix_rows
    group_ids = gathered[:, offset : offset + id_count].astype(jnp.int32)
    group_ids = group_ids.reshape(fsdp_size, 4, per_device)
    group_tokens = (group_ids[:, 0] * ID_BASE + group_ids[:, 1]).reshape(-1)
    group_targets = (group_ids[:, 2] * ID_BASE + group_ids[:, 3]).reshape(-1)
    offset += id_count
    extra_all = gathered[:, offset:].reshape(fsdp_size, -1)
    group_domains = extra_all[:, :rows_here].astype(jnp.int32)
    full_gains = [
        extra_all[:, rows_here + index * gain_here : rows_here + (index + 1) * gain_here].reshape(-1)
        for index in range(len(gains))
    ]
    ref_weights = (*full_matrices[:3], full_gains[0], full_gains[1])
    prx_weights = (*full_matrices[3:], full_gains[2], full_gains[3])

    token_local = group_tokens - vocab_start
    vocab_range = jnp.arange(vocab_here, dtype=jnp.int32)
    token_hits = (token_local[:, None] == vocab_range[None, :]).astype(jnp.bfloat16)
    picked_rows = jnp.dot(token_hits, in_embed, preferred_element_type=jnp.float32).astype(
        jnp.bfloat16
    )
    arrived = exchange_ordered(picked_rows.reshape(fsdp_size, per_device, width), "fsdp", True)
    embedded = jnp.sum(arrived.astype(jnp.float32), axis=0)

    normed = embedded * rms_scale(embedded)
    ref_own = feed_forward(embedded, normed, ref_weights)[0]
    prx_own, saved_state = feed_forward(embedded, normed, prx_weights)

    group_features = gather_ordered(jnp.concatenate([ref_own, prx_own], axis=1), "fsdp", False)
    group_features = group_features.reshape(group_total, 2 * width)
    ref_group = group_features[:, :width]
    prx_group = group_features[:, width:]

    target_local = group_targets - vocab_start
    ref_stats = vocab_stats(ref_group, out_embed, target_local)
    prx_stats = vocab_stats(prx_group, out_embed, target_local)

    all_stats = gather_ordered(jnp.concatenate([ref_stats, prx_stats]), "fsdp", False)
    tops = all_stats[:, 0::3]
    exp_totals = all_stats[:, 1::3]
    picks = all_stats[:, 2::3]
    top_logit = jnp.max(tops, axis=0)
    exp_total = jnp.sum(exp_totals * jnp.exp(tops - top_logit[None]), axis=0)
    pick_total = jnp.sum(picks, axis=0)
    log_total = top_logit + jnp.log(exp_total)
    losses = log_total - pick_total
    excess = jnp.maximum(losses[1] - losses[0], 0.0)

    row_excess = jnp.sum(excess.reshape(fsdp_size * rows_here, seq_len), axis=1)
    row_domains = group_domains.reshape(-1)
    domain_range = jnp.arange(domain_total, dtype=jnp.int32)
    row_hits = (row_domains[:, None] == domain_range[None, :]).astype(jnp.float32)
    group_sums = jnp.sum(row_hits * row_excess[:, None], axis=0)
    group_counts = jnp.sum(row_hits, axis=0) * seq_len

    summed = jnp.sum(gather_ordered(jnp.stack([group_sums, group_counts]), "dp", False), axis=0)
    total_sums = summed[0]
    domain_counts = summed[1]
    softmax_mix = jax.nn.softmax(jnp.log(alpha_prev) + total_sums / domain_counts)
    alpha_new = (1.0 - SMOOTHING) * softmax_mix + SMOOTHING / domain_total
    device_total = group_total * lax.axis_size("dp")
    token_ratio = math.sqrt(device_total) * alpha_new / domain_counts
    row_weight = jnp.take(token_ratio, row_domains)
    token_weight = jnp.repeat(row_weight, seq_len)

    d_second_part = head_gradient(prx_group, out_embed, log_total[1], token_weight, target_local)

    d_second = jnp.sum(
        exchange_ordered(d_second_part.reshape(fsdp_size, per_device, width), "fsdp", False),
        axis=0,
    )
    first_in, gate_act, up_act, hidden, second_scale, unit_stream = saved_state
    d_unit = d_second * prx_weights[4].astype(jnp.float32)
    d_branch = (
        second_scale
        * (d_unit - unit_stream * jnp.mean(d_unit * unit_stream, axis=1, keepdims=True))
    ).astype(jnp.bfloat16)
    d_hidden = contract_last(d_branch, prx_weights[2])
    sigmoid_gate = jax.nn.sigmoid(gate_act)
    d_gate = (d_hidden * up_act * sigmoid_gate * (1.0 + gate_act * (1.0 - sigmoid_gate))).astype(
        jnp.bfloat16
    )
    d_up = (d_hidden * gate_act * sigmoid_gate).astype(jnp.bfloat16)
    partial_grad = jnp.concatenate(
        [
            contract_first(d_gate, first_in),
            contract_first(d_up, first_in),
            contract_first(hidden, d_branch),
        ],
        axis=1,
    ).astype(jnp.bfloat16)

    arrived_grad = exchange_ordered(
        partial_grad.reshape(fsdp_size, unit_rows, 3 * width), "fsdp", False
    )
    local_grad = jnp.sum(arrived_grad.astype(jnp.float32), axis=0)

    grad_shard = jnp.sum(gather_ordered(local_grad, "dp", False), axis=0)
    return (
        alpha_new,
        grad_shard[:, :width],
        grad_shard[:, width : 2 * width],
        grad_shard[:, 2 * width :],
    )


def solution(mesh):
    placed = (
        P(("dp", "fsdp"), None),
        P(("dp", "fsdp"), None),
        P(("dp", "fsdp"), None),
        P("fsdp", None),
        P("fsdp", None),
        P("fsdp"),
        P("fsdp", None),
        P("fsdp", None),
        P("fsdp", None),
        P("fsdp"),
        P("fsdp"),
        P("fsdp", None),
        P("fsdp", None),
        P("fsdp", None),
        P("fsdp"),
        P(),
    )
    return jax.shard_map(
        body,
        mesh=mesh,
        in_specs=placed,
        out_specs=(P(), P("fsdp", None), P("fsdp", None), P("fsdp", None)),
        check_vma=False,
    )
```

```python
import math

import jax
import jax.numpy as jnp
from jax import lax
from jax.sharding import PartitionSpec as P

EPSILON = 1e-05
SMOOTHING = 0.001
FAN_OUT_MAX = 8
ID_BASE = 128


def rms_scale(values):
    return lax.rsqrt(jnp.mean(values * values, axis=1, keepdims=True) + EPSILON)


def contract_last(left_side, right_side):
    return lax.dot_general(
        left_side, right_side, (((1,), (1,)), ((), ())), preferred_element_type=jnp.float32
    )


def contract_first(left_side, right_side):
    return lax.dot_general(
        left_side, right_side, (((0,), (0,)), ((), ())), preferred_element_type=jnp.float32
    )


def shift_pairs(size, shift):
    return [(source, (source + shift) % size) for source in range(size)]


def to_absolute(stack, axis):
    return jnp.roll(stack[::-1], lax.axis_index(axis) + 1, axis=0)


def gather_ordered(value, axis, native):
    size = lax.axis_size(axis)
    if native or size > FAN_OUT_MAX:
        return lax.all_gather(value, axis)
    pieces = [value] + [
        lax.ppermute(value, axis, shift_pairs(size, shift)) for shift in range(1, size)
    ]
    return to_absolute(jnp.stack(pieces), axis)


def exchange_ordered(blocks, axis, native):
    size = lax.axis_size(axis)
    if native or size > FAN_OUT_MAX:
        return lax.all_to_all(blocks, axis, 0, 0, tiled=True)
    here = lax.axis_index(axis)
    pieces = [lax.dynamic_index_in_dim(blocks, here, keepdims=False)] + [
        lax.ppermute(
            lax.dynamic_index_in_dim(blocks, (here + shift) % size, keepdims=False),
            axis,
            shift_pairs(size, shift),
        )
        for shift in range(1, size)
    ]
    return to_absolute(jnp.stack(pieces), axis)


def feed_forward(embedded, normed, weights):
    gate_weight, up_weight, down_weight, norm_first, norm_second = weights
    first_in = (normed * norm_first.astype(jnp.float32)).astype(jnp.bfloat16)
    gate_act = contract_last(first_in, gate_weight)
    up_act = contract_last(first_in, up_weight)
    hidden = (gate_act * jax.nn.sigmoid(gate_act) * up_act).astype(jnp.bfloat16)
    stream = embedded + jnp.dot(hidden, down_weight, preferred_element_type=jnp.float32)
    second_scale = rms_scale(stream)
    unit_stream = stream * second_scale
    second_in = (unit_stream * norm_second.astype(jnp.float32)).astype(jnp.bfloat16)
    return (second_in, (first_in, gate_act, up_act, hidden, second_scale, unit_stream))


def block_rows_of(total):
    return math.gcd(total, 1024)


def vocab_stats(inputs, table, targets):
    total = inputs.shape[0]
    rows = block_rows_of(total)
    columns = jnp.arange(table.shape[0], dtype=jnp.int32)

    def one_block(block):
        block_in, block_target = block
        logits = contract_last(block_in, table)
        top_logit = jnp.max(logits, axis=1)
        exp_total = jnp.sum(jnp.exp(logits - top_logit[:, None]), axis=1)
        picked = jnp.sum(jnp.where(block_target[:, None] == columns[None, :], logits, 0.0), axis=1)
        return jnp.stack([top_logit, exp_total, picked])

    if rows == total:
        return one_block((inputs, targets))
    result = lax.map(
        one_block, (inputs.reshape(total // rows, rows, -1), targets.reshape(total // rows, rows))
    )
    return jnp.moveaxis(result, 1, 0).reshape(3, total)


def head_gradient(inputs, table, log_total, weight, targets):
    total = inputs.shape[0]
    rows = block_rows_of(total)
    columns = jnp.arange(table.shape[0], dtype=jnp.int32)

    def one_block(block):
        block_in, block_total, block_weight, block_target = block
        logits = contract_last(block_in, table)
        probs = jnp.exp(logits - block_total[:, None])
        hits = (block_target[:, None] == columns[None, :]).astype(jnp.float32)
        d_logits = (block_weight[:, None] * (probs - hits)).astype(jnp.bfloat16)
        return jnp.dot(d_logits, table, preferred_element_type=jnp.float32)

    if rows == total:
        return one_block((inputs, log_total, weight, targets))
    count = total // rows
    result = lax.map(
        one_block,
        (
            inputs.reshape(count, rows, -1),
            log_total.reshape(count, rows),
            weight.reshape(count, rows),
            targets.reshape(count, rows),
        ),
    )
    return result.reshape(total, -1)


def body(
    token_ids,
    target_ids,
    domain_ids,
    in_embed,
    out_embed,
    ref_norm1,
    ref_gate,
    ref_up,
    ref_down,
    ref_norm2,
    prx_norm1,
    prx_gate,
    prx_up,
    prx_down,
    prx_norm2,
    alpha_prev,
):
    domain_total = alpha_prev.shape[0]
    rows_here, seq_len = token_ids.shape
    per_device = rows_here * seq_len
    vocab_here, width = in_embed.shape
    fsdp_size = lax.axis_size("fsdp")
    group_total = per_device * fsdp_size
    vocab_start = lax.axis_index("fsdp") * vocab_here
    unit_rows = ref_gate.shape[0]
    gain_here = ref_norm1.shape[0]

    tokens = token_ids.reshape(-1)
    targets = target_ids.reshape(-1)
    matrices = (ref_gate, ref_up, ref_down, prx_gate, prx_up, prx_down)
    gains = (ref_norm1, ref_norm2, prx_norm1, prx_norm2)
    id_count = 4 * per_device // width
    extra_size = rows_here + len(gains) * gain_here
    extra_count = -(-extra_size // width)
    small_count = id_count + extra_count
    id_pieces = (tokens // ID_BASE, tokens % ID_BASE, targets // ID_BASE, targets % ID_BASE)
    small = jnp.zeros((small_count * width,), jnp.bfloat16)
    start = 0
    for piece in id_pieces + (domain_ids.reshape(-1),) + gains:
        piece = piece.astype(jnp.bfloat16)
        small = small + jnp.pad(piece, (start, small_count * width - start - piece.shape[0]))
        start += piece.shape[0]
    id_rows = small.reshape(small_count, width)[:id_count]
    extra_rows = small.reshape(small_count, width)[id_count:]
    matrix_rows = len(matrices) * unit_rows
    packed = jnp.concatenate(list(matrices) + [small.reshape(small_count, width)], axis=0)
    gathered = gather_ordered(packed, "fsdp", True)
    full_matrices = [
        gathered[:, index * unit_rows : (index + 1) * unit_rows].reshape(-1, width)
        for index in range(len(matrices))
    ]
    offset = matrix_rows
    group_ids = gathered[:, offset : offset + id_count].astype(jnp.int32)
    group_ids = group_ids.reshape(fsdp_size, 4, per_device)
    group_tokens = (group_ids[:, 0] * ID_BASE + group_ids[:, 1]).reshape(-1)
    group_targets = (group_ids[:, 2] * ID_BASE + group_ids[:, 3]).reshape(-1)
    offset += id_count
    extra_all = gathered[:, offset:].reshape(fsdp_size, -1)
    group_domains = extra_all[:, :rows_here].astype(jnp.int32)
    full_gains = [
        extra_all[:, rows_here + index * gain_here : rows_here + (index + 1) * gain_here].reshape(-1)
        for index in range(len(gains))
    ]
    ref_weights = (*full_matrices[:3], full_gains[0], full_gains[1])
    prx_weights = (*full_matrices[3:], full_gains[2], full_gains[3])

    token_local = group_tokens - vocab_start
    vocab_range = jnp.arange(vocab_here, dtype=jnp.int32)
    token_hits = (token_local[:, None] == vocab_range[None, :]).astype(jnp.bfloat16)
    picked_rows = jnp.dot(token_hits, in_embed, preferred_element_type=jnp.float32).astype(
        jnp.bfloat16
    )
    arrived = exchange_ordered(picked_rows.reshape(fsdp_size, per_device, width), "fsdp", False)
    embedded = jnp.sum(arrived.astype(jnp.float32), axis=0)

    normed = embedded * rms_scale(embedded)
    ref_own = feed_forward(embedded, normed, ref_weights)[0]
    prx_own, saved_state = feed_forward(embedded, normed, prx_weights)

    group_features = gather_ordered(jnp.concatenate([ref_own, prx_own], axis=1), "fsdp", False)
    group_features = group_features.reshape(group_total, 2 * width)
    ref_group = group_features[:, :width]
    prx_group = group_features[:, width:]

    target_local = group_targets - vocab_start
    ref_stats = vocab_stats(ref_group, out_embed, target_local)
    prx_stats = vocab_stats(prx_group, out_embed, target_local)

    all_stats = gather_ordered(jnp.concatenate([ref_stats, prx_stats]), "fsdp", False)
    tops = all_stats[:, 0::3]
    exp_totals = all_stats[:, 1::3]
    picks = all_stats[:, 2::3]
    top_logit = jnp.max(tops, axis=0)
    exp_total = jnp.sum(exp_totals * jnp.exp(tops - top_logit[None]), axis=0)
    pick_total = jnp.sum(picks, axis=0)
    log_total = top_logit + jnp.log(exp_total)
    losses = log_total - pick_total
    excess = jnp.maximum(losses[1] - losses[0], 0.0)

    row_excess = jnp.sum(excess.reshape(fsdp_size * rows_here, seq_len), axis=1)
    row_domains = group_domains.reshape(-1)
    domain_range = jnp.arange(domain_total, dtype=jnp.int32)
    row_hits = (row_domains[:, None] == domain_range[None, :]).astype(jnp.float32)
    group_sums = jnp.sum(row_hits * row_excess[:, None], axis=0)
    group_counts = jnp.sum(row_hits, axis=0) * seq_len

    summed = jnp.sum(gather_ordered(jnp.stack([group_sums, group_counts]), "dp", False), axis=0)
    total_sums = summed[0]
    domain_counts = summed[1]
    softmax_mix = jax.nn.softmax(jnp.log(alpha_prev) + total_sums / domain_counts)
    alpha_new = (1.0 - SMOOTHING) * softmax_mix + SMOOTHING / domain_total
    device_total = group_total * lax.axis_size("dp")
    token_ratio = math.sqrt(device_total) * alpha_new / domain_counts
    row_weight = jnp.take(token_ratio, row_domains)
    token_weight = jnp.repeat(row_weight, seq_len)

    d_second_part = head_gradient(prx_group, out_embed, log_total[1], token_weight, target_local)

    d_second = jnp.sum(
        exchange_ordered(d_second_part.reshape(fsdp_size, per_device, width), "fsdp", False),
        axis=0,
    )
    first_in, gate_act, up_act, hidden, second_scale, unit_stream = saved_state
    d_unit = d_second * prx_weights[4].astype(jnp.float32)
    d_branch = (
        second_scale
        * (d_unit - unit_stream * jnp.mean(d_unit * unit_stream, axis=1, keepdims=True))
    ).astype(jnp.bfloat16)
    d_hidden = contract_last(d_branch, prx_weights[2])
    sigmoid_gate = jax.nn.sigmoid(gate_act)
    d_gate = (d_hidden * up_act * sigmoid_gate * (1.0 + gate_act * (1.0 - sigmoid_gate))).astype(
        jnp.bfloat16
    )
    d_up = (d_hidden * gate_act * sigmoid_gate).astype(jnp.bfloat16)
    partial_grad = jnp.concatenate(
        [
            contract_first(d_gate, first_in),
            contract_first(d_up, first_in),
            contract_first(hidden, d_branch),
        ],
        axis=1,
    ).astype(jnp.bfloat16)

    arrived_grad = exchange_ordered(
        partial_grad.reshape(fsdp_size, unit_rows, 3 * width), "fsdp", False
    )
    local_grad = jnp.sum(arrived_grad.astype(jnp.float32), axis=0)

    grad_shard = jnp.sum(gather_ordered(local_grad, "dp", False), axis=0)
    return (
        alpha_new,
        grad_shard[:, :width],
        grad_shard[:, width : 2 * width],
        grad_shard[:, 2 * width :],
    )


def solution(mesh):
    placed = (
        P(("dp", "fsdp"), None),
        P(("dp", "fsdp"), None),
        P(("dp", "fsdp"), None),
        P("fsdp", None),
        P("fsdp", None),
        P("fsdp"),
        P("fsdp", None),
        P("fsdp", None),
        P("fsdp", None),
        P("fsdp"),
        P("fsdp"),
        P("fsdp", None),
        P("fsdp", None),
        P("fsdp", None),
        P("fsdp"),
        P(),
    )
    return jax.shard_map(
        body,
        mesh=mesh,
        in_specs=placed,
        out_specs=(P(), P("fsdp", None), P("fsdp", None), P("fsdp", None)),
        check_vma=False,
    )
```

```python
import math

import jax
import jax.numpy as jnp
from jax import lax
from jax.sharding import PartitionSpec as P

EPSILON = 1e-05
SMOOTHING = 0.001
FAN_OUT_MAX = 8
ID_BASE = 128


def rms_scale(values):
    return lax.rsqrt(jnp.mean(values * values, axis=1, keepdims=True) + EPSILON)


def contract_last(left_side, right_side):
    return lax.dot_general(
        left_side, right_side, (((1,), (1,)), ((), ())), preferred_element_type=jnp.float32
    )


def contract_first(left_side, right_side):
    return lax.dot_general(
        left_side, right_side, (((0,), (0,)), ((), ())), preferred_element_type=jnp.float32
    )


def shift_pairs(size, shift):
    return [(source, (source + shift) % size) for source in range(size)]


def to_absolute(stack, axis):
    return jnp.roll(stack[::-1], lax.axis_index(axis) + 1, axis=0)


def gather_ordered(value, axis, native):
    size = lax.axis_size(axis)
    if native or size > FAN_OUT_MAX:
        return lax.all_gather(value, axis)
    pieces = [value] + [
        lax.ppermute(value, axis, shift_pairs(size, shift)) for shift in range(1, size)
    ]
    return to_absolute(jnp.stack(pieces), axis)


def exchange_ordered(blocks, axis, native):
    size = lax.axis_size(axis)
    if native or size > FAN_OUT_MAX:
        return lax.all_to_all(blocks, axis, 0, 0, tiled=True)
    here = lax.axis_index(axis)
    pieces = [lax.dynamic_index_in_dim(blocks, here, keepdims=False)] + [
        lax.ppermute(
            lax.dynamic_index_in_dim(blocks, (here + shift) % size, keepdims=False),
            axis,
            shift_pairs(size, shift),
        )
        for shift in range(1, size)
    ]
    return to_absolute(jnp.stack(pieces), axis)


def feed_forward(embedded, normed, weights):
    gate_weight, up_weight, down_weight, norm_first, norm_second = weights
    first_in = (normed * norm_first.astype(jnp.float32)).astype(jnp.bfloat16)
    gate_act = contract_last(first_in, gate_weight)
    up_act = contract_last(first_in, up_weight)
    hidden = (gate_act * jax.nn.sigmoid(gate_act) * up_act).astype(jnp.bfloat16)
    stream = embedded + jnp.dot(hidden, down_weight, preferred_element_type=jnp.float32)
    second_scale = rms_scale(stream)
    unit_stream = stream * second_scale
    second_in = (unit_stream * norm_second.astype(jnp.float32)).astype(jnp.bfloat16)
    return (second_in, (first_in, gate_act, up_act, hidden, second_scale, unit_stream))


def block_rows_of(total):
    return math.gcd(total, 1024)


def vocab_stats(inputs, table, targets):
    total = inputs.shape[0]
    rows = block_rows_of(total)
    columns = jnp.arange(table.shape[0], dtype=jnp.int32)

    def one_block(block):
        block_in, block_target = block
        logits = contract_last(block_in, table)
        top_logit = jnp.max(logits, axis=1)
        exp_total = jnp.sum(jnp.exp(logits - top_logit[:, None]), axis=1)
        picked = jnp.sum(jnp.where(block_target[:, None] == columns[None, :], logits, 0.0), axis=1)
        return jnp.stack([top_logit, exp_total, picked])

    if rows == total:
        return one_block((inputs, targets))
    result = lax.map(
        one_block, (inputs.reshape(total // rows, rows, -1), targets.reshape(total // rows, rows))
    )
    return jnp.moveaxis(result, 1, 0).reshape(3, total)


def head_gradient(inputs, table, log_total, weight, targets):
    total = inputs.shape[0]
    rows = block_rows_of(total)
    columns = jnp.arange(table.shape[0], dtype=jnp.int32)

    def one_block(block):
        block_in, block_total, block_weight, block_target = block
        logits = contract_last(block_in, table)
        probs = jnp.exp(logits - block_total[:, None])
        hits = (block_target[:, None] == columns[None, :]).astype(jnp.float32)
        d_logits = (block_weight[:, None] * (probs - hits)).astype(jnp.bfloat16)
        return jnp.dot(d_logits, table, preferred_element_type=jnp.float32)

    if rows == total:
        return one_block((inputs, log_total, weight, targets))
    count = total // rows
    result = lax.map(
        one_block,
        (
            inputs.reshape(count, rows, -1),
            log_total.reshape(count, rows),
            weight.reshape(count, rows),
            targets.reshape(count, rows),
        ),
    )
    return result.reshape(total, -1)


def body(
    token_ids,
    target_ids,
    domain_ids,
    in_embed,
    out_embed,
    ref_norm1,
    ref_gate,
    ref_up,
    ref_down,
    ref_norm2,
    prx_norm1,
    prx_gate,
    prx_up,
    prx_down,
    prx_norm2,
    alpha_prev,
):
    domain_total = alpha_prev.shape[0]
    rows_here, seq_len = token_ids.shape
    per_device = rows_here * seq_len
    vocab_here, width = in_embed.shape
    fsdp_size = lax.axis_size("fsdp")
    group_total = per_device * fsdp_size
    vocab_start = lax.axis_index("fsdp") * vocab_here
    unit_rows = ref_gate.shape[0]
    gain_here = ref_norm1.shape[0]

    tokens = token_ids.reshape(-1)
    targets = target_ids.reshape(-1)
    matrices = (ref_gate, ref_up, ref_down, prx_gate, prx_up, prx_down)
    gains = (ref_norm1, ref_norm2, prx_norm1, prx_norm2)
    id_count = 4 * per_device // width
    extra_size = rows_here + len(gains) * gain_here
    extra_count = -(-extra_size // width)
    small_count = id_count + extra_count
    id_pieces = (tokens // ID_BASE, tokens % ID_BASE, targets // ID_BASE, targets % ID_BASE)
    small = jnp.zeros((small_count * width,), jnp.bfloat16)
    start = 0
    for piece in id_pieces + (domain_ids.reshape(-1),) + gains:
        piece = piece.astype(jnp.bfloat16)
        small = small + jnp.pad(piece, (start, small_count * width - start - piece.shape[0]))
        start += piece.shape[0]
    id_rows = small.reshape(small_count, width)[:id_count]
    extra_rows = small.reshape(small_count, width)[id_count:]
    matrix_rows = len(matrices) * unit_rows
    packed = jnp.concatenate(list(matrices) + [small.reshape(small_count, width)], axis=0)
    gathered = gather_ordered(packed, "fsdp", False)
    full_matrices = [
        gathered[:, index * unit_rows : (index + 1) * unit_rows].reshape(-1, width)
        for index in range(len(matrices))
    ]
    offset = matrix_rows
    group_ids = gathered[:, offset : offset + id_count].astype(jnp.int32)
    group_ids = group_ids.reshape(fsdp_size, 4, per_device)
    group_tokens = (group_ids[:, 0] * ID_BASE + group_ids[:, 1]).reshape(-1)
    group_targets = (group_ids[:, 2] * ID_BASE + group_ids[:, 3]).reshape(-1)
    offset += id_count
    extra_all = gathered[:, offset:].reshape(fsdp_size, -1)
    group_domains = extra_all[:, :rows_here].astype(jnp.int32)
    full_gains = [
        extra_all[:, rows_here + index * gain_here : rows_here + (index + 1) * gain_here].reshape(-1)
        for index in range(len(gains))
    ]
    ref_weights = (*full_matrices[:3], full_gains[0], full_gains[1])
    prx_weights = (*full_matrices[3:], full_gains[2], full_gains[3])

    token_local = group_tokens - vocab_start
    vocab_range = jnp.arange(vocab_here, dtype=jnp.int32)
    token_hits = (token_local[:, None] == vocab_range[None, :]).astype(jnp.bfloat16)
    picked_rows = jnp.dot(token_hits, in_embed, preferred_element_type=jnp.float32).astype(
        jnp.bfloat16
    )
    arrived = exchange_ordered(picked_rows.reshape(fsdp_size, per_device, width), "fsdp", False)
    embedded = jnp.sum(arrived.astype(jnp.float32), axis=0)

    normed = embedded * rms_scale(embedded)
    ref_own = feed_forward(embedded, normed, ref_weights)[0]
    prx_own, saved_state = feed_forward(embedded, normed, prx_weights)

    group_features = gather_ordered(jnp.concatenate([ref_own, prx_own], axis=1), "fsdp", False)
    group_features = group_features.reshape(group_total, 2 * width)
    ref_group = group_features[:, :width]
    prx_group = group_features[:, width:]

    target_local = group_targets - vocab_start
    ref_stats = vocab_stats(ref_group, out_embed, target_local)
    prx_stats = vocab_stats(prx_group, out_embed, target_local)

    all_stats = gather_ordered(jnp.concatenate([ref_stats, prx_stats]), "fsdp", False)
    tops = all_stats[:, 0::3]
    exp_totals = all_stats[:, 1::3]
    picks = all_stats[:, 2::3]
    top_logit = jnp.max(tops, axis=0)
    exp_total = jnp.sum(exp_totals * jnp.exp(tops - top_logit[None]), axis=0)
    pick_total = jnp.sum(picks, axis=0)
    log_total = top_logit + jnp.log(exp_total)
    losses = log_total - pick_total
    excess = jnp.maximum(losses[1] - losses[0], 0.0)

    row_excess = jnp.sum(excess.reshape(fsdp_size * rows_here, seq_len), axis=1)
    row_domains = group_domains.reshape(-1)
    domain_range = jnp.arange(domain_total, dtype=jnp.int32)
    row_hits = (row_domains[:, None] == domain_range[None, :]).astype(jnp.float32)
    group_sums = jnp.sum(row_hits * row_excess[:, None], axis=0)
    group_counts = jnp.sum(row_hits, axis=0) * seq_len

    summed = jnp.sum(gather_ordered(jnp.stack([group_sums, group_counts]), "dp", False), axis=0)
    total_sums = summed[0]
    domain_counts = summed[1]
    softmax_mix = jax.nn.softmax(jnp.log(alpha_prev) + total_sums / domain_counts)
    alpha_new = (1.0 - SMOOTHING) * softmax_mix + SMOOTHING / domain_total
    device_total = group_total * lax.axis_size("dp")
    token_ratio = math.sqrt(device_total) * alpha_new / domain_counts
    row_weight = jnp.take(token_ratio, row_domains)
    token_weight = jnp.repeat(row_weight, seq_len)

    d_second_part = head_gradient(prx_group, out_embed, log_total[1], token_weight, target_local)

    d_second = jnp.sum(
        exchange_ordered(d_second_part.reshape(fsdp_size, per_device, width), "fsdp", False),
        axis=0,
    )
    first_in, gate_act, up_act, hidden, second_scale, unit_stream = saved_state
    d_unit = d_second * prx_weights[4].astype(jnp.float32)
    d_branch = (
        second_scale
        * (d_unit - unit_stream * jnp.mean(d_unit * unit_stream, axis=1, keepdims=True))
    ).astype(jnp.bfloat16)
    d_hidden = contract_last(d_branch, prx_weights[2])
    sigmoid_gate = jax.nn.sigmoid(gate_act)
    d_gate = (d_hidden * up_act * sigmoid_gate * (1.0 + gate_act * (1.0 - sigmoid_gate))).astype(
        jnp.bfloat16
    )
    d_up = (d_hidden * gate_act * sigmoid_gate).astype(jnp.bfloat16)
    partial_grad = jnp.concatenate(
        [
            contract_first(d_gate, first_in),
            contract_first(d_up, first_in),
            contract_first(hidden, d_branch),
        ],
        axis=1,
    ).astype(jnp.bfloat16)

    arrived_grad = exchange_ordered(
        partial_grad.reshape(fsdp_size, unit_rows, 3 * width), "fsdp", False
    )
    local_grad = jnp.sum(arrived_grad.astype(jnp.float32), axis=0)

    grad_shard = jnp.sum(gather_ordered(local_grad, "dp", False), axis=0)
    return (
        alpha_new,
        grad_shard[:, :width],
        grad_shard[:, width : 2 * width],
        grad_shard[:, 2 * width :],
    )


def solution(mesh):
    placed = (
        P(("dp", "fsdp"), None),
        P(("dp", "fsdp"), None),
        P(("dp", "fsdp"), None),
        P("fsdp", None),
        P("fsdp", None),
        P("fsdp"),
        P("fsdp", None),
        P("fsdp", None),
        P("fsdp", None),
        P("fsdp"),
        P("fsdp"),
        P("fsdp", None),
        P("fsdp", None),
        P("fsdp", None),
        P("fsdp"),
        P(),
    )
    return jax.shard_map(
        body,
        mesh=mesh,
        in_specs=placed,
        out_specs=(P(), P("fsdp", None), P("fsdp", None), P("fsdp", None)),
        check_vma=False,
    )
```

```python
import math

import jax
import jax.numpy as jnp
from jax import lax
from jax.experimental import pallas as pl
from jax.experimental.pallas import tpu as pltpu
from jax.sharding import PartitionSpec as P

EPSILON = 1e-05
SMOOTHING = 0.001
FAN_OUT_MAX = 8
ID_BASE = 128


def rms_scale(values):
    return lax.rsqrt(jnp.mean(values * values, axis=1, keepdims=True) + EPSILON)


def contract_last(left_side, right_side):
    return lax.dot_general(
        left_side, right_side, (((1,), (1,)), ((), ())), preferred_element_type=jnp.float32
    )


def contract_first(left_side, right_side):
    return lax.dot_general(
        left_side, right_side, (((0,), (0,)), ((), ())), preferred_element_type=jnp.float32
    )


def shift_pairs(size, shift):
    return [(source, (source + shift) % size) for source in range(size)]


def to_absolute(stack, axis):
    return jnp.roll(stack[::-1], lax.axis_index(axis) + 1, axis=0)


def gather_ordered(value, axis, native):
    size = lax.axis_size(axis)
    if native or size > FAN_OUT_MAX:
        return lax.all_gather(value, axis)
    pieces = [value] + [
        lax.ppermute(value, axis, shift_pairs(size, shift)) for shift in range(1, size)
    ]
    return to_absolute(jnp.stack(pieces), axis)


def exchange_ordered(blocks, axis, native):
    size = lax.axis_size(axis)
    if native or size > FAN_OUT_MAX:
        return lax.all_to_all(blocks, axis, 0, 0, tiled=True)
    here = lax.axis_index(axis)
    pieces = [lax.dynamic_index_in_dim(blocks, here, keepdims=False)] + [
        lax.ppermute(
            lax.dynamic_index_in_dim(blocks, (here + shift) % size, keepdims=False),
            axis,
            shift_pairs(size, shift),
        )
        for shift in range(1, size)
    ]
    return to_absolute(jnp.stack(pieces), axis)


def pack_rows(parts):
    counts = [part.shape[0] for part in parts]
    width = parts[0].shape[1]

    def kernel(*refs):
        sources, target, semaphores = refs[: len(parts)], refs[len(parts)], refs[-1]
        copies = []
        start = 0
        for index, (source, count) in enumerate(zip(sources, counts)):
            copy = pltpu.make_async_copy(
                source, target.at[pl.ds(start, count)], semaphores.at[index]
            )
            copy.start()
            copies.append(copy)
            start += count
        for copy in copies:
            copy.wait()

    return pl.pallas_call(
        kernel,
        out_shape=jax.ShapeDtypeStruct((sum(counts), width), parts[0].dtype),
        in_specs=[pl.BlockSpec(memory_space=pl.ANY)] * len(parts),
        out_specs=pl.BlockSpec(memory_space=pl.ANY),
        scratch_shapes=[pltpu.SemaphoreType.DMA((len(parts),))],
    )(*parts)


def feed_forward(embedded, normed, weights):
    gate_weight, up_weight, down_weight, norm_first, norm_second = weights
    first_in = (normed * norm_first.astype(jnp.float32)).astype(jnp.bfloat16)
    gate_act = contract_last(first_in, gate_weight)
    up_act = contract_last(first_in, up_weight)
    hidden = (gate_act * jax.nn.sigmoid(gate_act) * up_act).astype(jnp.bfloat16)
    stream = embedded + jnp.dot(hidden, down_weight, preferred_element_type=jnp.float32)
    second_scale = rms_scale(stream)
    unit_stream = stream * second_scale
    second_in = (unit_stream * norm_second.astype(jnp.float32)).astype(jnp.bfloat16)
    return (second_in, (first_in, gate_act, up_act, hidden, second_scale, unit_stream))


def block_rows_of(total):
    return math.gcd(total, 1024)


def vocab_stats(inputs, table, targets):
    total = inputs.shape[0]
    rows = block_rows_of(total)
    columns = jnp.arange(table.shape[0], dtype=jnp.int32)

    def one_block(block):
        block_in, block_target = block
        logits = contract_last(block_in, table)
        top_logit = jnp.max(logits, axis=1)
        exp_total = jnp.sum(jnp.exp(logits - top_logit[:, None]), axis=1)
        picked = jnp.sum(jnp.where(block_target[:, None] == columns[None, :], logits, 0.0), axis=1)
        return jnp.stack([top_logit, exp_total, picked])

    if rows == total:
        return one_block((inputs, targets))
    result = lax.map(
        one_block, (inputs.reshape(total // rows, rows, -1), targets.reshape(total // rows, rows))
    )
    return jnp.moveaxis(result, 1, 0).reshape(3, total)


def head_gradient(inputs, table, log_total, weight, targets):
    total = inputs.shape[0]
    rows = block_rows_of(total)
    columns = jnp.arange(table.shape[0], dtype=jnp.int32)

    def one_block(block):
        block_in, block_total, block_weight, block_target = block
        logits = contract_last(block_in, table)
        probs = jnp.exp(logits - block_total[:, None])
        hits = (block_target[:, None] == columns[None, :]).astype(jnp.float32)
        d_logits = (block_weight[:, None] * (probs - hits)).astype(jnp.bfloat16)
        return jnp.dot(d_logits, table, preferred_element_type=jnp.float32)

    if rows == total:
        return one_block((inputs, log_total, weight, targets))
    count = total // rows
    result = lax.map(
        one_block,
        (
            inputs.reshape(count, rows, -1),
            log_total.reshape(count, rows),
            weight.reshape(count, rows),
            targets.reshape(count, rows),
        ),
    )
    return result.reshape(total, -1)


def body(
    token_ids,
    target_ids,
    domain_ids,
    in_embed,
    out_embed,
    ref_norm1,
    ref_gate,
    ref_up,
    ref_down,
    ref_norm2,
    prx_norm1,
    prx_gate,
    prx_up,
    prx_down,
    prx_norm2,
    alpha_prev,
):
    domain_total = alpha_prev.shape[0]
    rows_here, seq_len = token_ids.shape
    per_device = rows_here * seq_len
    vocab_here, width = in_embed.shape
    fsdp_size = lax.axis_size("fsdp")
    group_total = per_device * fsdp_size
    vocab_start = lax.axis_index("fsdp") * vocab_here
    unit_rows = ref_gate.shape[0]
    gain_here = ref_norm1.shape[0]

    tokens = token_ids.reshape(-1)
    targets = target_ids.reshape(-1)
    matrices = (ref_gate, ref_up, ref_down, prx_gate, prx_up, prx_down)
    gains = (ref_norm1, ref_norm2, prx_norm1, prx_norm2)
    id_count = 4 * per_device // width
    extra_size = rows_here + len(gains) * gain_here
    extra_count = -(-extra_size // width)
    small_count = -(-(id_count + extra_count) // 16) * 16
    id_pieces = (tokens // ID_BASE, tokens % ID_BASE, targets // ID_BASE, targets % ID_BASE)
    small = jnp.zeros((small_count * width,), jnp.bfloat16)
    start = 0
    for piece in id_pieces + (domain_ids.reshape(-1),) + gains:
        piece = piece.astype(jnp.bfloat16)
        small = small + jnp.pad(piece, (start, small_count * width - start - piece.shape[0]))
        start += piece.shape[0]
    matrix_rows = len(matrices) * unit_rows
    packed = pack_rows(list(matrices) + [small.reshape(small_count, width)])
    gathered = gather_ordered(packed, "fsdp", True)
    full_matrices = [
        gathered[:, index * unit_rows : (index + 1) * unit_rows].reshape(-1, width)
        for index in range(len(matrices))
    ]
    offset = matrix_rows
    group_ids = gathered[:, offset : offset + id_count].astype(jnp.int32)
    group_ids = group_ids.reshape(fsdp_size, 4, per_device)
    group_tokens = (group_ids[:, 0] * ID_BASE + group_ids[:, 1]).reshape(-1)
    group_targets = (group_ids[:, 2] * ID_BASE + group_ids[:, 3]).reshape(-1)
    offset += id_count
    extra_all = gathered[:, offset:].reshape(fsdp_size, -1)
    group_domains = extra_all[:, :rows_here].astype(jnp.int32)
    full_gains = [
        extra_all[:, rows_here + index * gain_here : rows_here + (index + 1) * gain_here].reshape(-1)
        for index in range(len(gains))
    ]
    ref_weights = (*full_matrices[:3], full_gains[0], full_gains[1])
    prx_weights = (*full_matrices[3:], full_gains[2], full_gains[3])

    token_local = group_tokens - vocab_start
    vocab_range = jnp.arange(vocab_here, dtype=jnp.int32)
    token_hits = (token_local[:, None] == vocab_range[None, :]).astype(jnp.bfloat16)
    picked_rows = jnp.dot(token_hits, in_embed, preferred_element_type=jnp.float32).astype(
        jnp.bfloat16
    )
    arrived = exchange_ordered(picked_rows.reshape(fsdp_size, per_device, width), "fsdp", False)
    embedded = jnp.sum(arrived.astype(jnp.float32), axis=0)

    normed = embedded * rms_scale(embedded)
    ref_own = feed_forward(embedded, normed, ref_weights)[0]
    prx_own, saved_state = feed_forward(embedded, normed, prx_weights)

    group_features = gather_ordered(jnp.concatenate([ref_own, prx_own], axis=1), "fsdp", False)
    group_features = group_features.reshape(group_total, 2 * width)
    ref_group = group_features[:, :width]
    prx_group = group_features[:, width:]

    target_local = group_targets - vocab_start
    ref_stats = vocab_stats(ref_group, out_embed, target_local)
    prx_stats = vocab_stats(prx_group, out_embed, target_local)

    all_stats = gather_ordered(jnp.concatenate([ref_stats, prx_stats]), "fsdp", False)
    tops = all_stats[:, 0::3]
    exp_totals = all_stats[:, 1::3]
    picks = all_stats[:, 2::3]
    top_logit = jnp.max(tops, axis=0)
    exp_total = jnp.sum(exp_totals * jnp.exp(tops - top_logit[None]), axis=0)
    pick_total = jnp.sum(picks, axis=0)
    log_total = top_logit + jnp.log(exp_total)
    losses = log_total - pick_total
    excess = jnp.maximum(losses[1] - losses[0], 0.0)

    row_excess = jnp.sum(excess.reshape(fsdp_size * rows_here, seq_len), axis=1)
    row_domains = group_domains.reshape(-1)
    domain_range = jnp.arange(domain_total, dtype=jnp.int32)
    row_hits = (row_domains[:, None] == domain_range[None, :]).astype(jnp.float32)
    group_sums = jnp.sum(row_hits * row_excess[:, None], axis=0)
    group_counts = jnp.sum(row_hits, axis=0) * seq_len

    summed = jnp.sum(gather_ordered(jnp.stack([group_sums, group_counts]), "dp", False), axis=0)
    total_sums = summed[0]
    domain_counts = summed[1]
    softmax_mix = jax.nn.softmax(jnp.log(alpha_prev) + total_sums / domain_counts)
    alpha_new = (1.0 - SMOOTHING) * softmax_mix + SMOOTHING / domain_total
    device_total = group_total * lax.axis_size("dp")
    token_ratio = math.sqrt(device_total) * alpha_new / domain_counts
    row_weight = jnp.take(token_ratio, row_domains)
    token_weight = jnp.repeat(row_weight, seq_len)

    d_second_part = head_gradient(prx_group, out_embed, log_total[1], token_weight, target_local)

    d_second = jnp.sum(
        exchange_ordered(d_second_part.reshape(fsdp_size, per_device, width), "fsdp", False),
        axis=0,
    )
    first_in, gate_act, up_act, hidden, second_scale, unit_stream = saved_state
    d_unit = d_second * prx_weights[4].astype(jnp.float32)
    d_branch = (
        second_scale
        * (d_unit - unit_stream * jnp.mean(d_unit * unit_stream, axis=1, keepdims=True))
    ).astype(jnp.bfloat16)
    d_hidden = contract_last(d_branch, prx_weights[2])
    sigmoid_gate = jax.nn.sigmoid(gate_act)
    d_gate = (d_hidden * up_act * sigmoid_gate * (1.0 + gate_act * (1.0 - sigmoid_gate))).astype(
        jnp.bfloat16
    )
    d_up = (d_hidden * gate_act * sigmoid_gate).astype(jnp.bfloat16)
    partial_grad = jnp.concatenate(
        [
            contract_first(d_gate, first_in),
            contract_first(d_up, first_in),
            contract_first(hidden, d_branch),
        ],
        axis=1,
    ).astype(jnp.bfloat16)

    arrived_grad = exchange_ordered(
        partial_grad.reshape(fsdp_size, unit_rows, 3 * width), "fsdp", False
    )
    local_grad = jnp.sum(arrived_grad.astype(jnp.float32), axis=0)

    grad_shard = jnp.sum(gather_ordered(local_grad, "dp", False), axis=0)
    return (
        alpha_new,
        grad_shard[:, :width],
        grad_shard[:, width : 2 * width],
        grad_shard[:, 2 * width :],
    )


def solution(mesh):
    placed = (
        P(("dp", "fsdp"), None),
        P(("dp", "fsdp"), None),
        P(("dp", "fsdp"), None),
        P("fsdp", None),
        P("fsdp", None),
        P("fsdp"),
        P("fsdp", None),
        P("fsdp", None),
        P("fsdp", None),
        P("fsdp"),
        P("fsdp"),
        P("fsdp", None),
        P("fsdp", None),
        P("fsdp", None),
        P("fsdp"),
        P(),
    )
    return jax.shard_map(
        body,
        mesh=mesh,
        in_specs=placed,
        out_specs=(P(), P("fsdp", None), P("fsdp", None), P("fsdp", None)),
        check_vma=False,
    )
```

```python
import math

import jax
import jax.numpy as jnp
from jax import lax
from jax.sharding import PartitionSpec as P

EPSILON = 1e-05
SMOOTHING = 0.001
FAN_OUT_MAX = 8
ID_BASE = 128


def rms_scale(values):
    return lax.rsqrt(jnp.mean(values * values, axis=1, keepdims=True) + EPSILON)


def contract_last(left_side, right_side):
    return lax.dot_general(
        left_side, right_side, (((1,), (1,)), ((), ())), preferred_element_type=jnp.float32
    )


def contract_first(left_side, right_side):
    return lax.dot_general(
        left_side, right_side, (((0,), (0,)), ((), ())), preferred_element_type=jnp.float32
    )


def shift_pairs(size, shift):
    return [(source, (source + shift) % size) for source in range(size)]


def to_absolute(stack, axis):
    return jnp.roll(stack[::-1], lax.axis_index(axis) + 1, axis=0)


def gather_ordered(value, axis, native):
    size = lax.axis_size(axis)
    if native or size > FAN_OUT_MAX:
        return lax.all_gather(value, axis)
    pieces = [value] + [
        lax.ppermute(value, axis, shift_pairs(size, shift)) for shift in range(1, size)
    ]
    return to_absolute(jnp.stack(pieces), axis)


def exchange_ordered(blocks, axis, native):
    size = lax.axis_size(axis)
    if native or size > FAN_OUT_MAX:
        return lax.all_to_all(blocks, axis, 0, 0, tiled=True)
    here = lax.axis_index(axis)
    pieces = [lax.dynamic_index_in_dim(blocks, here, keepdims=False)] + [
        lax.ppermute(
            lax.dynamic_index_in_dim(blocks, (here + shift) % size, keepdims=False),
            axis,
            shift_pairs(size, shift),
        )
        for shift in range(1, size)
    ]
    return to_absolute(jnp.stack(pieces), axis)


def feed_forward(embedded, normed, weights):
    gate_weight, up_weight, down_weight, norm_first, norm_second = weights
    first_in = (normed * norm_first.astype(jnp.float32)).astype(jnp.bfloat16)
    gate_act = contract_last(first_in, gate_weight)
    up_act = contract_last(first_in, up_weight)
    hidden = (gate_act * jax.nn.sigmoid(gate_act) * up_act).astype(jnp.bfloat16)
    stream = embedded + jnp.dot(hidden, down_weight, preferred_element_type=jnp.float32)
    second_scale = rms_scale(stream)
    unit_stream = stream * second_scale
    second_in = (unit_stream * norm_second.astype(jnp.float32)).astype(jnp.bfloat16)
    return (second_in, (first_in, gate_act, up_act, hidden, second_scale, unit_stream))


def block_rows_of(total):
    return math.gcd(total, 1024)


def vocab_stats(inputs, table, targets):
    total = inputs.shape[0]
    rows = block_rows_of(total)
    columns = jnp.arange(table.shape[0], dtype=jnp.int32)

    def one_block(block):
        block_in, block_target = block
        logits = contract_last(block_in, table)
        top_logit = jnp.max(logits, axis=1)
        exp_total = jnp.sum(jnp.exp(logits - top_logit[:, None]), axis=1)
        picked = jnp.sum(jnp.where(block_target[:, None] == columns[None, :], logits, 0.0), axis=1)
        return jnp.stack([top_logit, exp_total, picked])

    if rows == total:
        return one_block((inputs, targets))
    result = lax.map(
        one_block, (inputs.reshape(total // rows, rows, -1), targets.reshape(total // rows, rows))
    )
    return jnp.moveaxis(result, 1, 0).reshape(3, total)


def head_residual(inputs, table, log_total, targets):
    total = inputs.shape[0]
    rows = block_rows_of(total)
    columns = jnp.arange(table.shape[0], dtype=jnp.int32)

    def one_block(block):
        block_in, block_total, block_target = block
        logits = contract_last(block_in, table)
        probs = jnp.exp(logits - block_total[:, None])
        hits = (block_target[:, None] == columns[None, :]).astype(jnp.float32)
        return probs - hits

    if rows == total:
        return one_block((inputs, log_total, targets))
    count = total // rows
    result = lax.map(
        one_block,
        (inputs.reshape(count, rows, -1), log_total.reshape(count, rows), targets.reshape(count, rows)),
    )
    return result.reshape(total, -1)


def head_gradient(residual, table, weight):
    d_logits = (weight[:, None] * residual).astype(jnp.bfloat16)
    return jnp.dot(d_logits, table, preferred_element_type=jnp.float32)


def body(
    token_ids,
    target_ids,
    domain_ids,
    in_embed,
    out_embed,
    ref_norm1,
    ref_gate,
    ref_up,
    ref_down,
    ref_norm2,
    prx_norm1,
    prx_gate,
    prx_up,
    prx_down,
    prx_norm2,
    alpha_prev,
):
    domain_total = alpha_prev.shape[0]
    rows_here, seq_len = token_ids.shape
    per_device = rows_here * seq_len
    vocab_here, width = in_embed.shape
    fsdp_size = lax.axis_size("fsdp")
    group_total = per_device * fsdp_size
    vocab_start = lax.axis_index("fsdp") * vocab_here
    unit_rows = ref_gate.shape[0]
    gain_here = ref_norm1.shape[0]

    tokens = token_ids.reshape(-1)
    targets = target_ids.reshape(-1)
    matrices = (ref_gate, ref_up, ref_down, prx_gate, prx_up, prx_down)
    gains = (ref_norm1, ref_norm2, prx_norm1, prx_norm2)
    id_count = 4 * per_device // width
    extra_size = rows_here + len(gains) * gain_here
    extra_count = -(-extra_size // width)
    small_count = id_count + extra_count
    id_pieces = (tokens // ID_BASE, tokens % ID_BASE, targets // ID_BASE, targets % ID_BASE)
    small = jnp.zeros((small_count * width,), jnp.bfloat16)
    start = 0
    for piece in id_pieces + (domain_ids.reshape(-1),) + gains:
        piece = piece.astype(jnp.bfloat16)
        small = small + jnp.pad(piece, (start, small_count * width - start - piece.shape[0]))
        start += piece.shape[0]
    id_rows = small.reshape(small_count, width)[:id_count]
    extra_rows = small.reshape(small_count, width)[id_count:]
    matrix_rows = len(matrices) * unit_rows
    packed = jnp.concatenate(list(matrices) + [small.reshape(small_count, width)], axis=0)
    gathered = gather_ordered(packed, "fsdp", True)
    full_matrices = [
        gathered[:, index * unit_rows : (index + 1) * unit_rows].reshape(-1, width)
        for index in range(len(matrices))
    ]
    offset = matrix_rows
    group_ids = gathered[:, offset : offset + id_count].astype(jnp.int32)
    group_ids = group_ids.reshape(fsdp_size, 4, per_device)
    group_tokens = (group_ids[:, 0] * ID_BASE + group_ids[:, 1]).reshape(-1)
    group_targets = (group_ids[:, 2] * ID_BASE + group_ids[:, 3]).reshape(-1)
    offset += id_count
    extra_all = gathered[:, offset:].reshape(fsdp_size, -1)
    group_domains = extra_all[:, :rows_here].astype(jnp.int32)
    full_gains = [
        extra_all[:, rows_here + index * gain_here : rows_here + (index + 1) * gain_here].reshape(-1)
        for index in range(len(gains))
    ]
    ref_weights = (*full_matrices[:3], full_gains[0], full_gains[1])
    prx_weights = (*full_matrices[3:], full_gains[2], full_gains[3])

    token_local = group_tokens - vocab_start
    vocab_range = jnp.arange(vocab_here, dtype=jnp.int32)
    token_hits = (token_local[:, None] == vocab_range[None, :]).astype(jnp.bfloat16)
    picked_rows = jnp.dot(token_hits, in_embed, preferred_element_type=jnp.float32).astype(
        jnp.bfloat16
    )
    arrived = exchange_ordered(picked_rows.reshape(fsdp_size, per_device, width), "fsdp", False)
    embedded = jnp.sum(arrived.astype(jnp.float32), axis=0)

    normed = embedded * rms_scale(embedded)
    ref_own = feed_forward(embedded, normed, ref_weights)[0]
    prx_own, saved_state = feed_forward(embedded, normed, prx_weights)

    group_features = gather_ordered(jnp.concatenate([ref_own, prx_own], axis=1), "fsdp", False)
    group_features = group_features.reshape(group_total, 2 * width)
    ref_group = group_features[:, :width]
    prx_group = group_features[:, width:]

    target_local = group_targets - vocab_start
    ref_stats = vocab_stats(ref_group, out_embed, target_local)
    prx_stats = vocab_stats(prx_group, out_embed, target_local)

    all_stats = gather_ordered(jnp.concatenate([ref_stats, prx_stats]), "fsdp", False)
    tops = all_stats[:, 0::3]
    exp_totals = all_stats[:, 1::3]
    picks = all_stats[:, 2::3]
    top_logit = jnp.max(tops, axis=0)
    exp_total = jnp.sum(exp_totals * jnp.exp(tops - top_logit[None]), axis=0)
    pick_total = jnp.sum(picks, axis=0)
    log_total = top_logit + jnp.log(exp_total)
    losses = log_total - pick_total
    excess = jnp.maximum(losses[1] - losses[0], 0.0)

    row_excess = jnp.sum(excess.reshape(fsdp_size * rows_here, seq_len), axis=1)
    row_domains = group_domains.reshape(-1)
    domain_range = jnp.arange(domain_total, dtype=jnp.int32)
    row_hits = (row_domains[:, None] == domain_range[None, :]).astype(jnp.float32)
    group_sums = jnp.sum(row_hits * row_excess[:, None], axis=0)
    group_counts = jnp.sum(row_hits, axis=0) * seq_len

    residual = lax.optimization_barrier(
        head_residual(prx_group, out_embed, log_total[1], target_local)
    )

    summed = jnp.sum(gather_ordered(jnp.stack([group_sums, group_counts]), "dp", False), axis=0)
    total_sums = summed[0]
    domain_counts = summed[1]
    softmax_mix = jax.nn.softmax(jnp.log(alpha_prev) + total_sums / domain_counts)
    alpha_new = (1.0 - SMOOTHING) * softmax_mix + SMOOTHING / domain_total
    device_total = group_total * lax.axis_size("dp")
    token_ratio = math.sqrt(device_total) * alpha_new / domain_counts
    row_weight = jnp.take(token_ratio, row_domains)
    token_weight = jnp.repeat(row_weight, seq_len)

    d_second_part = head_gradient(residual, out_embed, token_weight)

    d_second = jnp.sum(
        exchange_ordered(d_second_part.reshape(fsdp_size, per_device, width), "fsdp", False),
        axis=0,
    )
    first_in, gate_act, up_act, hidden, second_scale, unit_stream = saved_state
    d_unit = d_second * prx_weights[4].astype(jnp.float32)
    d_branch = (
        second_scale
        * (d_unit - unit_stream * jnp.mean(d_unit * unit_stream, axis=1, keepdims=True))
    ).astype(jnp.bfloat16)
    d_hidden = contract_last(d_branch, prx_weights[2])
    sigmoid_gate = jax.nn.sigmoid(gate_act)
    d_gate = (d_hidden * up_act * sigmoid_gate * (1.0 + gate_act * (1.0 - sigmoid_gate))).astype(
        jnp.bfloat16
    )
    d_up = (d_hidden * gate_act * sigmoid_gate).astype(jnp.bfloat16)
    partial_grad = jnp.concatenate(
        [
            contract_first(d_gate, first_in),
            contract_first(d_up, first_in),
            contract_first(hidden, d_branch),
        ],
        axis=1,
    ).astype(jnp.bfloat16)

    arrived_grad = exchange_ordered(
        partial_grad.reshape(fsdp_size, unit_rows, 3 * width), "fsdp", False
    )
    local_grad = jnp.sum(arrived_grad.astype(jnp.float32), axis=0)

    grad_shard = jnp.sum(gather_ordered(local_grad, "dp", False), axis=0)
    return (
        alpha_new,
        grad_shard[:, :width],
        grad_shard[:, width : 2 * width],
        grad_shard[:, 2 * width :],
    )


def solution(mesh):
    placed = (
        P(("dp", "fsdp"), None),
        P(("dp", "fsdp"), None),
        P(("dp", "fsdp"), None),
        P("fsdp", None),
        P("fsdp", None),
        P("fsdp"),
        P("fsdp", None),
        P("fsdp", None),
        P("fsdp", None),
        P("fsdp"),
        P("fsdp"),
        P("fsdp", None),
        P("fsdp", None),
        P("fsdp", None),
        P("fsdp"),
        P(),
    )
    return jax.shard_map(
        body,
        mesh=mesh,
        in_specs=placed,
        out_specs=(P(), P("fsdp", None), P("fsdp", None), P("fsdp", None)),
        check_vma=False,
    )
```

```python
import math

import jax
import jax.numpy as jnp
from jax import lax
from jax.sharding import PartitionSpec as P

EPSILON = 1e-05
SMOOTHING = 0.001
FAN_OUT_MAX = 8
ID_BASE = 128


def rms_scale(values):
    return lax.rsqrt(jnp.mean(values * values, axis=1, keepdims=True) + EPSILON)


def contract_last(left_side, right_side):
    return lax.dot_general(
        left_side, right_side, (((1,), (1,)), ((), ())), preferred_element_type=jnp.float32
    )


def contract_first(left_side, right_side):
    return lax.dot_general(
        left_side, right_side, (((0,), (0,)), ((), ())), preferred_element_type=jnp.float32
    )


def shift_pairs(size, shift):
    return [(source, (source + shift) % size) for source in range(size)]


def to_absolute(stack, axis):
    return jnp.roll(stack[::-1], lax.axis_index(axis) + 1, axis=0)


def gather_ordered(value, axis, native, paired=False):
    size = lax.axis_size(axis)
    if native or size > FAN_OUT_MAX:
        return lax.all_gather(value, axis)
    if paired and size & (size - 1) == 0:
        pieces = [value] + [
            lax.ppermute(value, axis, [(source, source ^ mask) for source in range(size)])
            for mask in range(1, size)
        ]
        order = jnp.bitwise_xor(lax.axis_index(axis), jnp.arange(size))
        return jnp.take(jnp.stack(pieces), order, axis=0)
    pieces = [value] + [
        lax.ppermute(value, axis, shift_pairs(size, shift)) for shift in range(1, size)
    ]
    return to_absolute(jnp.stack(pieces), axis)


def exchange_ordered(blocks, axis, native):
    size = lax.axis_size(axis)
    if native or size > FAN_OUT_MAX:
        return lax.all_to_all(blocks, axis, 0, 0, tiled=True)
    here = lax.axis_index(axis)
    pieces = [lax.dynamic_index_in_dim(blocks, here, keepdims=False)] + [
        lax.ppermute(
            lax.dynamic_index_in_dim(blocks, (here + shift) % size, keepdims=False),
            axis,
            shift_pairs(size, shift),
        )
        for shift in range(1, size)
    ]
    return to_absolute(jnp.stack(pieces), axis)


def feed_forward(embedded, normed, weights):
    gate_weight, up_weight, down_weight, norm_first, norm_second = weights
    first_in = (normed * norm_first.astype(jnp.float32)).astype(jnp.bfloat16)
    gate_act = contract_last(first_in, gate_weight)
    up_act = contract_last(first_in, up_weight)
    hidden = (gate_act * jax.nn.sigmoid(gate_act) * up_act).astype(jnp.bfloat16)
    stream = embedded + jnp.dot(hidden, down_weight, preferred_element_type=jnp.float32)
    second_scale = rms_scale(stream)
    unit_stream = stream * second_scale
    second_in = (unit_stream * norm_second.astype(jnp.float32)).astype(jnp.bfloat16)
    return (second_in, (first_in, gate_act, up_act, hidden, second_scale, unit_stream))


def block_rows_of(total):
    return math.gcd(total, 1024)


def vocab_stats(inputs, table, targets):
    total = inputs.shape[0]
    rows = block_rows_of(total)
    columns = jnp.arange(table.shape[0], dtype=jnp.int32)

    def one_block(block):
        block_in, block_target = block
        logits = contract_last(block_in, table)
        top_logit = jnp.max(logits, axis=1)
        exp_total = jnp.sum(jnp.exp(logits - top_logit[:, None]), axis=1)
        picked = jnp.sum(jnp.where(block_target[:, None] == columns[None, :], logits, 0.0), axis=1)
        return jnp.stack([top_logit, exp_total, picked])

    if rows == total:
        return one_block((inputs, targets))
    result = lax.map(
        one_block, (inputs.reshape(total // rows, rows, -1), targets.reshape(total // rows, rows))
    )
    return jnp.moveaxis(result, 1, 0).reshape(3, total)


def head_gradient(inputs, table, log_total, weight, targets):
    total = inputs.shape[0]
    rows = block_rows_of(total)
    columns = jnp.arange(table.shape[0], dtype=jnp.int32)

    def one_block(block):
        block_in, block_total, block_weight, block_target = block
        logits = contract_last(block_in, table)
        probs = jnp.exp(logits - block_total[:, None])
        hits = (block_target[:, None] == columns[None, :]).astype(jnp.float32)
        d_logits = (block_weight[:, None] * (probs - hits)).astype(jnp.bfloat16)
        return jnp.dot(d_logits, table, preferred_element_type=jnp.float32)

    if rows == total:
        return one_block((inputs, log_total, weight, targets))
    count = total // rows
    result = lax.map(
        one_block,
        (
            inputs.reshape(count, rows, -1),
            log_total.reshape(count, rows),
            weight.reshape(count, rows),
            targets.reshape(count, rows),
        ),
    )
    return result.reshape(total, -1)


def body(
    token_ids,
    target_ids,
    domain_ids,
    in_embed,
    out_embed,
    ref_norm1,
    ref_gate,
    ref_up,
    ref_down,
    ref_norm2,
    prx_norm1,
    prx_gate,
    prx_up,
    prx_down,
    prx_norm2,
    alpha_prev,
):
    domain_total = alpha_prev.shape[0]
    rows_here, seq_len = token_ids.shape
    per_device = rows_here * seq_len
    vocab_here, width = in_embed.shape
    fsdp_size = lax.axis_size("fsdp")
    group_total = per_device * fsdp_size
    vocab_start = lax.axis_index("fsdp") * vocab_here
    unit_rows = ref_gate.shape[0]
    gain_here = ref_norm1.shape[0]

    tokens = token_ids.reshape(-1)
    targets = target_ids.reshape(-1)
    matrices = (ref_gate, ref_up, ref_down, prx_gate, prx_up, prx_down)
    gains = (ref_norm1, ref_norm2, prx_norm1, prx_norm2)
    id_count = 4 * per_device // width
    extra_size = rows_here + len(gains) * gain_here
    extra_count = -(-extra_size // width)
    small_count = id_count + extra_count
    id_pieces = (tokens // ID_BASE, tokens % ID_BASE, targets // ID_BASE, targets % ID_BASE)
    small = jnp.zeros((small_count * width,), jnp.bfloat16)
    start = 0
    for piece in id_pieces + (domain_ids.reshape(-1),) + gains:
        piece = piece.astype(jnp.bfloat16)
        small = small + jnp.pad(piece, (start, small_count * width - start - piece.shape[0]))
        start += piece.shape[0]
    id_rows = small.reshape(small_count, width)[:id_count]
    extra_rows = small.reshape(small_count, width)[id_count:]
    matrix_rows = len(matrices) * unit_rows
    packed = jnp.concatenate(list(matrices) + [small.reshape(small_count, width)], axis=0)
    gathered = gather_ordered(packed, "fsdp", True)
    full_matrices = [
        gathered[:, index * unit_rows : (index + 1) * unit_rows].reshape(-1, width)
        for index in range(len(matrices))
    ]
    offset = matrix_rows
    group_ids = gathered[:, offset : offset + id_count].astype(jnp.int32)
    group_ids = group_ids.reshape(fsdp_size, 4, per_device)
    group_tokens = (group_ids[:, 0] * ID_BASE + group_ids[:, 1]).reshape(-1)
    group_targets = (group_ids[:, 2] * ID_BASE + group_ids[:, 3]).reshape(-1)
    offset += id_count
    extra_all = gathered[:, offset:].reshape(fsdp_size, -1)
    group_domains = extra_all[:, :rows_here].astype(jnp.int32)
    full_gains = [
        extra_all[:, rows_here + index * gain_here : rows_here + (index + 1) * gain_here].reshape(-1)
        for index in range(len(gains))
    ]
    ref_weights = (*full_matrices[:3], full_gains[0], full_gains[1])
    prx_weights = (*full_matrices[3:], full_gains[2], full_gains[3])

    token_local = group_tokens - vocab_start
    vocab_range = jnp.arange(vocab_here, dtype=jnp.int32)
    token_hits = (token_local[:, None] == vocab_range[None, :]).astype(jnp.bfloat16)
    picked_rows = jnp.dot(token_hits, in_embed, preferred_element_type=jnp.float32).astype(
        jnp.bfloat16
    )
    arrived = exchange_ordered(picked_rows.reshape(fsdp_size, per_device, width), "fsdp", False)
    embedded = jnp.sum(arrived.astype(jnp.float32), axis=0)

    normed = embedded * rms_scale(embedded)
    ref_own = feed_forward(embedded, normed, ref_weights)[0]
    prx_own, saved_state = feed_forward(embedded, normed, prx_weights)

    group_features = gather_ordered(jnp.concatenate([ref_own, prx_own], axis=1), "fsdp", False)
    group_features = group_features.reshape(group_total, 2 * width)
    ref_group = group_features[:, :width]
    prx_group = group_features[:, width:]

    target_local = group_targets - vocab_start
    ref_stats = vocab_stats(ref_group, out_embed, target_local)
    prx_stats = vocab_stats(prx_group, out_embed, target_local)

    all_stats = gather_ordered(jnp.concatenate([ref_stats, prx_stats]), "fsdp", False)
    tops = all_stats[:, 0::3]
    exp_totals = all_stats[:, 1::3]
    picks = all_stats[:, 2::3]
    top_logit = jnp.max(tops, axis=0)
    exp_total = jnp.sum(exp_totals * jnp.exp(tops - top_logit[None]), axis=0)
    pick_total = jnp.sum(picks, axis=0)
    log_total = top_logit + jnp.log(exp_total)
    losses = log_total - pick_total
    excess = jnp.maximum(losses[1] - losses[0], 0.0)

    row_excess = jnp.sum(excess.reshape(fsdp_size * rows_here, seq_len), axis=1)
    row_domains = group_domains.reshape(-1)
    domain_range = jnp.arange(domain_total, dtype=jnp.int32)
    row_hits = (row_domains[:, None] == domain_range[None, :]).astype(jnp.float32)
    group_sums = jnp.sum(row_hits * row_excess[:, None], axis=0)
    group_counts = jnp.sum(row_hits, axis=0) * seq_len

    summed = jnp.sum(gather_ordered(jnp.stack([group_sums, group_counts]), "dp", False, True), axis=0)
    total_sums = summed[0]
    domain_counts = summed[1]
    softmax_mix = jax.nn.softmax(jnp.log(alpha_prev) + total_sums / domain_counts)
    alpha_new = (1.0 - SMOOTHING) * softmax_mix + SMOOTHING / domain_total
    device_total = group_total * lax.axis_size("dp")
    token_ratio = math.sqrt(device_total) * alpha_new / domain_counts
    row_weight = jnp.take(token_ratio, row_domains)
    token_weight = jnp.repeat(row_weight, seq_len)

    d_second_part = head_gradient(prx_group, out_embed, log_total[1], token_weight, target_local)

    d_second = jnp.sum(
        exchange_ordered(d_second_part.reshape(fsdp_size, per_device, width), "fsdp", False),
        axis=0,
    )
    first_in, gate_act, up_act, hidden, second_scale, unit_stream = saved_state
    d_unit = d_second * prx_weights[4].astype(jnp.float32)
    d_branch = (
        second_scale
        * (d_unit - unit_stream * jnp.mean(d_unit * unit_stream, axis=1, keepdims=True))
    ).astype(jnp.bfloat16)
    d_hidden = contract_last(d_branch, prx_weights[2])
    sigmoid_gate = jax.nn.sigmoid(gate_act)
    d_gate = (d_hidden * up_act * sigmoid_gate * (1.0 + gate_act * (1.0 - sigmoid_gate))).astype(
        jnp.bfloat16
    )
    d_up = (d_hidden * gate_act * sigmoid_gate).astype(jnp.bfloat16)
    partial_grad = jnp.concatenate(
        [
            contract_first(d_gate, first_in),
            contract_first(d_up, first_in),
            contract_first(hidden, d_branch),
        ],
        axis=1,
    ).astype(jnp.bfloat16)

    arrived_grad = exchange_ordered(
        partial_grad.reshape(fsdp_size, unit_rows, 3 * width), "fsdp", False
    )
    local_grad = jnp.sum(arrived_grad.astype(jnp.float32), axis=0)

    grad_shard = jnp.sum(gather_ordered(local_grad, "dp", False, True), axis=0)
    return (
        alpha_new,
        grad_shard[:, :width],
        grad_shard[:, width : 2 * width],
        grad_shard[:, 2 * width :],
    )


def solution(mesh):
    placed = (
        P(("dp", "fsdp"), None),
        P(("dp", "fsdp"), None),
        P(("dp", "fsdp"), None),
        P("fsdp", None),
        P("fsdp", None),
        P("fsdp"),
        P("fsdp", None),
        P("fsdp", None),
        P("fsdp", None),
        P("fsdp"),
        P("fsdp"),
        P("fsdp", None),
        P("fsdp", None),
        P("fsdp", None),
        P("fsdp"),
        P(),
    )
    return jax.shard_map(
        body,
        mesh=mesh,
        in_specs=placed,
        out_specs=(P(), P("fsdp", None), P("fsdp", None), P("fsdp", None)),
        check_vma=False,
    )
```

```python
import math

import jax
import jax.numpy as jnp
from jax import lax
from jax.sharding import PartitionSpec as P

EPSILON = 1e-05
SMOOTHING = 0.001
FAN_OUT_MAX = 8
ID_BASE = 128


def rms_scale(values):
    return lax.rsqrt(jnp.mean(values * values, axis=1, keepdims=True) + EPSILON)


def contract_last(left_side, right_side):
    return lax.dot_general(
        left_side, right_side, (((1,), (1,)), ((), ())), preferred_element_type=jnp.float32
    )


def contract_first(left_side, right_side):
    return lax.dot_general(
        left_side, right_side, (((0,), (0,)), ((), ())), preferred_element_type=jnp.float32
    )


def shift_pairs(size, shift):
    return [(source, (source + shift) % size) for source in range(size)]


def to_absolute(stack, axis):
    return jnp.roll(stack[::-1], lax.axis_index(axis) + 1, axis=0)


def gather_ordered(value, axis, native, two_rounds=False):
    size = lax.axis_size(axis)
    if native or size > FAN_OUT_MAX:
        return lax.all_gather(value, axis)
    if two_rounds and size > 2 and size & (size - 1) == 0:
        sibling = lax.ppermute(value, axis, [(source, source ^ 1) for source in range(size)])
        pair = jnp.stack([value, sibling])
        pieces = [value, sibling]
        for mask in range(2, size, 2):
            arrived = lax.ppermute(pair, axis, [(source, source ^ mask) for source in range(size)])
            pieces += [arrived[0], arrived[1]]
        order = jnp.bitwise_xor(lax.axis_index(axis), jnp.arange(size))
        return jnp.take(jnp.stack(pieces), order, axis=0)
    pieces = [value] + [
        lax.ppermute(value, axis, shift_pairs(size, shift)) for shift in range(1, size)
    ]
    return to_absolute(jnp.stack(pieces), axis)


def exchange_ordered(blocks, axis, native):
    size = lax.axis_size(axis)
    if native or size > FAN_OUT_MAX:
        return lax.all_to_all(blocks, axis, 0, 0, tiled=True)
    here = lax.axis_index(axis)
    pieces = [lax.dynamic_index_in_dim(blocks, here, keepdims=False)] + [
        lax.ppermute(
            lax.dynamic_index_in_dim(blocks, (here + shift) % size, keepdims=False),
            axis,
            shift_pairs(size, shift),
        )
        for shift in range(1, size)
    ]
    return to_absolute(jnp.stack(pieces), axis)


def feed_forward(embedded, normed, weights):
    gate_weight, up_weight, down_weight, norm_first, norm_second = weights
    first_in = (normed * norm_first.astype(jnp.float32)).astype(jnp.bfloat16)
    gate_act = contract_last(first_in, gate_weight)
    up_act = contract_last(first_in, up_weight)
    hidden = (gate_act * jax.nn.sigmoid(gate_act) * up_act).astype(jnp.bfloat16)
    stream = embedded + jnp.dot(hidden, down_weight, preferred_element_type=jnp.float32)
    second_scale = rms_scale(stream)
    unit_stream = stream * second_scale
    second_in = (unit_stream * norm_second.astype(jnp.float32)).astype(jnp.bfloat16)
    return (second_in, (first_in, gate_act, up_act, hidden, second_scale, unit_stream))


def block_rows_of(total):
    return math.gcd(total, 1024)


def vocab_stats(inputs, table, targets):
    total = inputs.shape[0]
    rows = block_rows_of(total)
    columns = jnp.arange(table.shape[0], dtype=jnp.int32)

    def one_block(block):
        block_in, block_target = block
        logits = contract_last(block_in, table)
        top_logit = jnp.max(logits, axis=1)
        exp_total = jnp.sum(jnp.exp(logits - top_logit[:, None]), axis=1)
        picked = jnp.sum(jnp.where(block_target[:, None] == columns[None, :], logits, 0.0), axis=1)
        return jnp.stack([top_logit, exp_total, picked])

    if rows == total:
        return one_block((inputs, targets))
    result = lax.map(
        one_block, (inputs.reshape(total // rows, rows, -1), targets.reshape(total // rows, rows))
    )
    return jnp.moveaxis(result, 1, 0).reshape(3, total)


def head_gradient(inputs, table, log_total, weight, targets):
    total = inputs.shape[0]
    rows = block_rows_of(total)
    columns = jnp.arange(table.shape[0], dtype=jnp.int32)

    def one_block(block):
        block_in, block_total, block_weight, block_target = block
        logits = contract_last(block_in, table)
        probs = jnp.exp(logits - block_total[:, None])
        hits = (block_target[:, None] == columns[None, :]).astype(jnp.float32)
        d_logits = (block_weight[:, None] * (probs - hits)).astype(jnp.bfloat16)
        return jnp.dot(d_logits, table, preferred_element_type=jnp.float32)

    if rows == total:
        return one_block((inputs, log_total, weight, targets))
    count = total // rows
    result = lax.map(
        one_block,
        (
            inputs.reshape(count, rows, -1),
            log_total.reshape(count, rows),
            weight.reshape(count, rows),
            targets.reshape(count, rows),
        ),
    )
    return result.reshape(total, -1)


def body(
    token_ids,
    target_ids,
    domain_ids,
    in_embed,
    out_embed,
    ref_norm1,
    ref_gate,
    ref_up,
    ref_down,
    ref_norm2,
    prx_norm1,
    prx_gate,
    prx_up,
    prx_down,
    prx_norm2,
    alpha_prev,
):
    domain_total = alpha_prev.shape[0]
    rows_here, seq_len = token_ids.shape
    per_device = rows_here * seq_len
    vocab_here, width = in_embed.shape
    fsdp_size = lax.axis_size("fsdp")
    group_total = per_device * fsdp_size
    vocab_start = lax.axis_index("fsdp") * vocab_here
    unit_rows = ref_gate.shape[0]
    gain_here = ref_norm1.shape[0]

    tokens = token_ids.reshape(-1)
    targets = target_ids.reshape(-1)
    matrices = (ref_gate, ref_up, ref_down, prx_gate, prx_up, prx_down)
    gains = (ref_norm1, ref_norm2, prx_norm1, prx_norm2)
    id_count = 4 * per_device // width
    extra_size = rows_here + len(gains) * gain_here
    extra_count = -(-extra_size // width)
    small_count = id_count + extra_count
    id_pieces = (tokens // ID_BASE, tokens % ID_BASE, targets // ID_BASE, targets % ID_BASE)
    small = jnp.zeros((small_count * width,), jnp.bfloat16)
    start = 0
    for piece in id_pieces + (domain_ids.reshape(-1),) + gains:
        piece = piece.astype(jnp.bfloat16)
        small = small + jnp.pad(piece, (start, small_count * width - start - piece.shape[0]))
        start += piece.shape[0]
    id_rows = small.reshape(small_count, width)[:id_count]
    extra_rows = small.reshape(small_count, width)[id_count:]
    matrix_rows = len(matrices) * unit_rows
    packed = jnp.concatenate(list(matrices) + [small.reshape(small_count, width)], axis=0)
    gathered = gather_ordered(packed, "fsdp", True)
    full_matrices = [
        gathered[:, index * unit_rows : (index + 1) * unit_rows].reshape(-1, width)
        for index in range(len(matrices))
    ]
    offset = matrix_rows
    group_ids = gathered[:, offset : offset + id_count].astype(jnp.int32)
    group_ids = group_ids.reshape(fsdp_size, 4, per_device)
    group_tokens = (group_ids[:, 0] * ID_BASE + group_ids[:, 1]).reshape(-1)
    group_targets = (group_ids[:, 2] * ID_BASE + group_ids[:, 3]).reshape(-1)
    offset += id_count
    extra_all = gathered[:, offset:].reshape(fsdp_size, -1)
    group_domains = extra_all[:, :rows_here].astype(jnp.int32)
    full_gains = [
        extra_all[:, rows_here + index * gain_here : rows_here + (index + 1) * gain_here].reshape(-1)
        for index in range(len(gains))
    ]
    ref_weights = (*full_matrices[:3], full_gains[0], full_gains[1])
    prx_weights = (*full_matrices[3:], full_gains[2], full_gains[3])

    token_local = group_tokens - vocab_start
    vocab_range = jnp.arange(vocab_here, dtype=jnp.int32)
    token_hits = (token_local[:, None] == vocab_range[None, :]).astype(jnp.bfloat16)
    picked_rows = jnp.dot(token_hits, in_embed, preferred_element_type=jnp.float32).astype(
        jnp.bfloat16
    )
    arrived = exchange_ordered(picked_rows.reshape(fsdp_size, per_device, width), "fsdp", False)
    embedded = jnp.sum(arrived.astype(jnp.float32), axis=0)

    normed = embedded * rms_scale(embedded)
    ref_own = feed_forward(embedded, normed, ref_weights)[0]
    prx_own, saved_state = feed_forward(embedded, normed, prx_weights)

    group_features = gather_ordered(jnp.concatenate([ref_own, prx_own], axis=1), "fsdp", False)
    group_features = group_features.reshape(group_total, 2 * width)
    ref_group = group_features[:, :width]
    prx_group = group_features[:, width:]

    target_local = group_targets - vocab_start
    ref_stats = vocab_stats(ref_group, out_embed, target_local)
    prx_stats = vocab_stats(prx_group, out_embed, target_local)

    all_stats = gather_ordered(jnp.concatenate([ref_stats, prx_stats]), "fsdp", False, True)
    tops = all_stats[:, 0::3]
    exp_totals = all_stats[:, 1::3]
    picks = all_stats[:, 2::3]
    top_logit = jnp.max(tops, axis=0)
    exp_total = jnp.sum(exp_totals * jnp.exp(tops - top_logit[None]), axis=0)
    pick_total = jnp.sum(picks, axis=0)
    log_total = top_logit + jnp.log(exp_total)
    losses = log_total - pick_total
    excess = jnp.maximum(losses[1] - losses[0], 0.0)

    row_excess = jnp.sum(excess.reshape(fsdp_size * rows_here, seq_len), axis=1)
    row_domains = group_domains.reshape(-1)
    domain_range = jnp.arange(domain_total, dtype=jnp.int32)
    row_hits = (row_domains[:, None] == domain_range[None, :]).astype(jnp.float32)
    group_sums = jnp.sum(row_hits * row_excess[:, None], axis=0)
    group_counts = jnp.sum(row_hits, axis=0) * seq_len

    summed = jnp.sum(gather_ordered(jnp.stack([group_sums, group_counts]), "dp", False), axis=0)
    total_sums = summed[0]
    domain_counts = summed[1]
    softmax_mix = jax.nn.softmax(jnp.log(alpha_prev) + total_sums / domain_counts)
    alpha_new = (1.0 - SMOOTHING) * softmax_mix + SMOOTHING / domain_total
    device_total = group_total * lax.axis_size("dp")
    token_ratio = math.sqrt(device_total) * alpha_new / domain_counts
    row_weight = jnp.take(token_ratio, row_domains)
    token_weight = jnp.repeat(row_weight, seq_len)

    d_second_part = head_gradient(prx_group, out_embed, log_total[1], token_weight, target_local)

    d_second = jnp.sum(
        exchange_ordered(d_second_part.reshape(fsdp_size, per_device, width), "fsdp", False),
        axis=0,
    )
    first_in, gate_act, up_act, hidden, second_scale, unit_stream = saved_state
    d_unit = d_second * prx_weights[4].astype(jnp.float32)
    d_branch = (
        second_scale
        * (d_unit - unit_stream * jnp.mean(d_unit * unit_stream, axis=1, keepdims=True))
    ).astype(jnp.bfloat16)
    d_hidden = contract_last(d_branch, prx_weights[2])
    sigmoid_gate = jax.nn.sigmoid(gate_act)
    d_gate = (d_hidden * up_act * sigmoid_gate * (1.0 + gate_act * (1.0 - sigmoid_gate))).astype(
        jnp.bfloat16
    )
    d_up = (d_hidden * gate_act * sigmoid_gate).astype(jnp.bfloat16)
    partial_grad = jnp.concatenate(
        [
            contract_first(d_gate, first_in),
            contract_first(d_up, first_in),
            contract_first(hidden, d_branch),
        ],
        axis=1,
    ).astype(jnp.bfloat16)

    arrived_grad = exchange_ordered(
        partial_grad.reshape(fsdp_size, unit_rows, 3 * width), "fsdp", False
    )
    local_grad = jnp.sum(arrived_grad.astype(jnp.float32), axis=0)

    grad_shard = jnp.sum(gather_ordered(local_grad, "dp", False), axis=0)
    return (
        alpha_new,
        grad_shard[:, :width],
        grad_shard[:, width : 2 * width],
        grad_shard[:, 2 * width :],
    )


def solution(mesh):
    placed = (
        P(("dp", "fsdp"), None),
        P(("dp", "fsdp"), None),
        P(("dp", "fsdp"), None),
        P("fsdp", None),
        P("fsdp", None),
        P("fsdp"),
        P("fsdp", None),
        P("fsdp", None),
        P("fsdp", None),
        P("fsdp"),
        P("fsdp"),
        P("fsdp", None),
        P("fsdp", None),
        P("fsdp", None),
        P("fsdp"),
        P(),
    )
    return jax.shard_map(
        body,
        mesh=mesh,
        in_specs=placed,
        out_specs=(P(), P("fsdp", None), P("fsdp", None), P("fsdp", None)),
        check_vma=False,
    )
```

```python
import math

import jax
import jax.numpy as jnp
from jax import lax
from jax.sharding import PartitionSpec as P

EPSILON = 1e-05
SMOOTHING = 0.001
FAN_OUT_MAX = 8
ID_BASE = 128


def rms_scale(values):
    return lax.rsqrt(jnp.mean(values * values, axis=1, keepdims=True) + EPSILON)


def contract_last(left_side, right_side):
    return lax.dot_general(
        left_side, right_side, (((1,), (1,)), ((), ())), preferred_element_type=jnp.float32
    )


def contract_first(left_side, right_side):
    return lax.dot_general(
        left_side, right_side, (((0,), (0,)), ((), ())), preferred_element_type=jnp.float32
    )


def shift_pairs(size, shift):
    return [(source, (source + shift) % size) for source in range(size)]


def to_absolute(stack, axis):
    return jnp.roll(stack[::-1], lax.axis_index(axis) + 1, axis=0)


def gather_ordered(value, axis, native):
    size = lax.axis_size(axis)
    if native or size > FAN_OUT_MAX:
        return lax.all_gather(value, axis)
    pieces = [value] + [
        lax.ppermute(value, axis, shift_pairs(size, shift)) for shift in range(1, size)
    ]
    return to_absolute(jnp.stack(pieces), axis)


def exchange_ordered(blocks, axis, native):
    size = lax.axis_size(axis)
    if native or size > FAN_OUT_MAX:
        return lax.all_to_all(blocks, axis, 0, 0, tiled=True)
    here = lax.axis_index(axis)
    pieces = [lax.dynamic_index_in_dim(blocks, here, keepdims=False)] + [
        lax.ppermute(
            lax.dynamic_index_in_dim(blocks, (here + shift) % size, keepdims=False),
            axis,
            shift_pairs(size, shift),
        )
        for shift in range(1, size)
    ]
    return to_absolute(jnp.stack(pieces), axis)


def feed_forward(embedded, normed, weights):
    gate_weight, up_weight, down_weight, norm_first, norm_second = weights
    first_in = (normed * norm_first.astype(jnp.float32)).astype(jnp.bfloat16)
    gate_act = contract_last(first_in, gate_weight)
    up_act = contract_last(first_in, up_weight)
    hidden = (gate_act * jax.nn.sigmoid(gate_act) * up_act).astype(jnp.bfloat16)
    stream = embedded + jnp.dot(hidden, down_weight, preferred_element_type=jnp.float32)
    second_scale = rms_scale(stream)
    unit_stream = stream * second_scale
    second_in = (unit_stream * norm_second.astype(jnp.float32)).astype(jnp.bfloat16)
    return (second_in, (first_in, gate_act, up_act, hidden, second_scale, unit_stream))


def block_rows_of(total):
    return math.gcd(total, 1024)


def vocab_stats(inputs, table, targets):
    total = inputs.shape[0]
    rows = block_rows_of(total)
    columns = jnp.arange(table.shape[0], dtype=jnp.int32)

    def one_block(block):
        block_in, block_target = block
        logits = contract_last(block_in, table)
        top_logit = jnp.max(logits, axis=1)
        exp_total = jnp.sum(jnp.exp(logits - top_logit[:, None]), axis=1)
        inside = (block_target >= 0) & (block_target < table.shape[0])
        clipped = jnp.clip(block_target, 0, table.shape[0] - 1)
        picked = jnp.where(
            inside, jnp.take_along_axis(logits, clipped[:, None], axis=1)[:, 0], 0.0
        )
        return jnp.stack([top_logit, exp_total, picked])

    if rows == total:
        return one_block((inputs, targets))
    result = lax.map(
        one_block, (inputs.reshape(total // rows, rows, -1), targets.reshape(total // rows, rows))
    )
    return jnp.moveaxis(result, 1, 0).reshape(3, total)


def head_gradient(inputs, table, log_total, weight, targets):
    total = inputs.shape[0]
    rows = block_rows_of(total)
    columns = jnp.arange(table.shape[0], dtype=jnp.int32)

    def one_block(block):
        block_in, block_total, block_weight, block_target = block
        logits = contract_last(block_in, table)
        probs = jnp.exp(logits - block_total[:, None])
        hits = (block_target[:, None] == columns[None, :]).astype(jnp.float32)
        d_logits = (block_weight[:, None] * (probs - hits)).astype(jnp.bfloat16)
        return jnp.dot(d_logits, table, preferred_element_type=jnp.float32)

    if rows == total:
        return one_block((inputs, log_total, weight, targets))
    count = total // rows
    result = lax.map(
        one_block,
        (
            inputs.reshape(count, rows, -1),
            log_total.reshape(count, rows),
            weight.reshape(count, rows),
            targets.reshape(count, rows),
        ),
    )
    return result.reshape(total, -1)


def body(
    token_ids,
    target_ids,
    domain_ids,
    in_embed,
    out_embed,
    ref_norm1,
    ref_gate,
    ref_up,
    ref_down,
    ref_norm2,
    prx_norm1,
    prx_gate,
    prx_up,
    prx_down,
    prx_norm2,
    alpha_prev,
):
    domain_total = alpha_prev.shape[0]
    rows_here, seq_len = token_ids.shape
    per_device = rows_here * seq_len
    vocab_here, width = in_embed.shape
    fsdp_size = lax.axis_size("fsdp")
    group_total = per_device * fsdp_size
    vocab_start = lax.axis_index("fsdp") * vocab_here
    unit_rows = ref_gate.shape[0]
    gain_here = ref_norm1.shape[0]

    tokens = token_ids.reshape(-1)
    targets = target_ids.reshape(-1)
    matrices = (ref_gate, ref_up, ref_down, prx_gate, prx_up, prx_down)
    gains = (ref_norm1, ref_norm2, prx_norm1, prx_norm2)
    id_count = 4 * per_device // width
    extra_size = rows_here + len(gains) * gain_here
    extra_count = -(-extra_size // width)
    small_count = id_count + extra_count
    id_pieces = (tokens // ID_BASE, tokens % ID_BASE, targets // ID_BASE, targets % ID_BASE)
    small = jnp.zeros((small_count * width,), jnp.bfloat16)
    start = 0
    for piece in id_pieces + (domain_ids.reshape(-1),) + gains:
        piece = piece.astype(jnp.bfloat16)
        small = small + jnp.pad(piece, (start, small_count * width - start - piece.shape[0]))
        start += piece.shape[0]
    id_rows = small.reshape(small_count, width)[:id_count]
    extra_rows = small.reshape(small_count, width)[id_count:]
    matrix_rows = len(matrices) * unit_rows
    packed = jnp.concatenate(list(matrices) + [small.reshape(small_count, width)], axis=0)
    gathered = gather_ordered(packed, "fsdp", True)
    full_matrices = [
        gathered[:, index * unit_rows : (index + 1) * unit_rows].reshape(-1, width)
        for index in range(len(matrices))
    ]
    offset = matrix_rows
    group_ids = gathered[:, offset : offset + id_count].astype(jnp.int32)
    group_ids = group_ids.reshape(fsdp_size, 4, per_device)
    group_tokens = (group_ids[:, 0] * ID_BASE + group_ids[:, 1]).reshape(-1)
    group_targets = (group_ids[:, 2] * ID_BASE + group_ids[:, 3]).reshape(-1)
    offset += id_count
    extra_all = gathered[:, offset:].reshape(fsdp_size, -1)
    group_domains = extra_all[:, :rows_here].astype(jnp.int32)
    full_gains = [
        extra_all[:, rows_here + index * gain_here : rows_here + (index + 1) * gain_here].reshape(-1)
        for index in range(len(gains))
    ]
    ref_weights = (*full_matrices[:3], full_gains[0], full_gains[1])
    prx_weights = (*full_matrices[3:], full_gains[2], full_gains[3])

    token_local = group_tokens - vocab_start
    vocab_range = jnp.arange(vocab_here, dtype=jnp.int32)
    token_hits = (token_local[:, None] == vocab_range[None, :]).astype(jnp.bfloat16)
    picked_rows = jnp.dot(token_hits, in_embed, preferred_element_type=jnp.float32).astype(
        jnp.bfloat16
    )
    arrived = exchange_ordered(picked_rows.reshape(fsdp_size, per_device, width), "fsdp", False)
    embedded = jnp.sum(arrived.astype(jnp.float32), axis=0)

    normed = embedded * rms_scale(embedded)
    ref_own = feed_forward(embedded, normed, ref_weights)[0]
    prx_own, saved_state = feed_forward(embedded, normed, prx_weights)

    group_features = gather_ordered(jnp.concatenate([ref_own, prx_own], axis=1), "fsdp", False)
    group_features = group_features.reshape(group_total, 2 * width)
    ref_group = group_features[:, :width]
    prx_group = group_features[:, width:]

    target_local = group_targets - vocab_start
    ref_stats = vocab_stats(ref_group, out_embed, target_local)
    prx_stats = vocab_stats(prx_group, out_embed, target_local)

    all_stats = gather_ordered(jnp.concatenate([ref_stats, prx_stats]), "fsdp", False)
    tops = all_stats[:, 0::3]
    exp_totals = all_stats[:, 1::3]
    picks = all_stats[:, 2::3]
    top_logit = jnp.max(tops, axis=0)
    exp_total = jnp.sum(exp_totals * jnp.exp(tops - top_logit[None]), axis=0)
    pick_total = jnp.sum(picks, axis=0)
    log_total = top_logit + jnp.log(exp_total)
    losses = log_total - pick_total
    excess = jnp.maximum(losses[1] - losses[0], 0.0)

    row_excess = jnp.sum(excess.reshape(fsdp_size * rows_here, seq_len), axis=1)
    row_domains = group_domains.reshape(-1)
    domain_range = jnp.arange(domain_total, dtype=jnp.int32)
    row_hits = (row_domains[:, None] == domain_range[None, :]).astype(jnp.float32)
    group_sums = jnp.sum(row_hits * row_excess[:, None], axis=0)
    group_counts = jnp.sum(row_hits, axis=0) * seq_len

    summed = jnp.sum(gather_ordered(jnp.stack([group_sums, group_counts]), "dp", False), axis=0)
    total_sums = summed[0]
    domain_counts = summed[1]
    softmax_mix = jax.nn.softmax(jnp.log(alpha_prev) + total_sums / domain_counts)
    alpha_new = (1.0 - SMOOTHING) * softmax_mix + SMOOTHING / domain_total
    device_total = group_total * lax.axis_size("dp")
    token_ratio = math.sqrt(device_total) * alpha_new / domain_counts
    row_weight = jnp.take(token_ratio, row_domains)
    token_weight = jnp.repeat(row_weight, seq_len)

    d_second_part = head_gradient(prx_group, out_embed, log_total[1], token_weight, target_local)

    d_second = jnp.sum(
        exchange_ordered(d_second_part.reshape(fsdp_size, per_device, width), "fsdp", False),
        axis=0,
    )
    first_in, gate_act, up_act, hidden, second_scale, unit_stream = saved_state
    d_unit = d_second * prx_weights[4].astype(jnp.float32)
    d_branch = (
        second_scale
        * (d_unit - unit_stream * jnp.mean(d_unit * unit_stream, axis=1, keepdims=True))
    ).astype(jnp.bfloat16)
    d_hidden = contract_last(d_branch, prx_weights[2])
    sigmoid_gate = jax.nn.sigmoid(gate_act)
    d_gate = (d_hidden * up_act * sigmoid_gate * (1.0 + gate_act * (1.0 - sigmoid_gate))).astype(
        jnp.bfloat16
    )
    d_up = (d_hidden * gate_act * sigmoid_gate).astype(jnp.bfloat16)
    partial_grad = jnp.concatenate(
        [
            contract_first(d_gate, first_in),
            contract_first(d_up, first_in),
            contract_first(hidden, d_branch),
        ],
        axis=1,
    ).astype(jnp.bfloat16)

    arrived_grad = exchange_ordered(
        partial_grad.reshape(fsdp_size, unit_rows, 3 * width), "fsdp", False
    )
    local_grad = jnp.sum(arrived_grad.astype(jnp.float32), axis=0)

    grad_shard = jnp.sum(gather_ordered(local_grad, "dp", False), axis=0)
    return (
        alpha_new,
        grad_shard[:, :width],
        grad_shard[:, width : 2 * width],
        grad_shard[:, 2 * width :],
    )


def solution(mesh):
    placed = (
        P(("dp", "fsdp"), None),
        P(("dp", "fsdp"), None),
        P(("dp", "fsdp"), None),
        P("fsdp", None),
        P("fsdp", None),
        P("fsdp"),
        P("fsdp", None),
        P("fsdp", None),
        P("fsdp", None),
        P("fsdp"),
        P("fsdp"),
        P("fsdp", None),
        P("fsdp", None),
        P("fsdp", None),
        P("fsdp"),
        P(),
    )
    return jax.shard_map(
        body,
        mesh=mesh,
        in_specs=placed,
        out_specs=(P(), P("fsdp", None), P("fsdp", None), P("fsdp", None)),
        check_vma=False,
    )
```

```python
import math

import jax
import jax.numpy as jnp
from jax import lax
from jax.sharding import PartitionSpec as P

EPSILON = 1e-05
SMOOTHING = 0.001
FAN_OUT_MAX = 8
ID_BASE = 128


def rms_scale(values):
    return lax.rsqrt(jnp.mean(values * values, axis=1, keepdims=True) + EPSILON)


def contract_last(left_side, right_side):
    return lax.dot_general(
        left_side, right_side, (((1,), (1,)), ((), ())), preferred_element_type=jnp.float32
    )


def contract_first(left_side, right_side):
    return lax.dot_general(
        left_side, right_side, (((0,), (0,)), ((), ())), preferred_element_type=jnp.float32
    )


def shift_pairs(size, shift):
    return [(source, (source + shift) % size) for source in range(size)]


def to_absolute(stack, axis):
    return jnp.roll(stack[::-1], lax.axis_index(axis) + 1, axis=0)


def gather_ordered(value, axis, native):
    size = lax.axis_size(axis)
    if native or size > FAN_OUT_MAX:
        return lax.all_gather(value, axis)
    pieces = [value] + [
        lax.ppermute(value, axis, shift_pairs(size, shift)) for shift in range(1, size)
    ]
    return to_absolute(jnp.stack(pieces), axis)


def exchange_ordered(blocks, axis, native):
    size = lax.axis_size(axis)
    if native or size > FAN_OUT_MAX:
        return lax.all_to_all(blocks, axis, 0, 0, tiled=True)
    here = lax.axis_index(axis)
    pieces = [lax.dynamic_index_in_dim(blocks, here, keepdims=False)] + [
        lax.ppermute(
            lax.dynamic_index_in_dim(blocks, (here + shift) % size, keepdims=False),
            axis,
            shift_pairs(size, shift),
        )
        for shift in range(1, size)
    ]
    return jnp.stack(pieces)


def feed_forward(embedded, normed, weights):
    gate_weight, up_weight, down_weight, norm_first, norm_second = weights
    first_in = (normed * norm_first.astype(jnp.float32)).astype(jnp.bfloat16)
    gate_act = contract_last(first_in, gate_weight)
    up_act = contract_last(first_in, up_weight)
    hidden = (gate_act * jax.nn.sigmoid(gate_act) * up_act).astype(jnp.bfloat16)
    stream = embedded + jnp.dot(hidden, down_weight, preferred_element_type=jnp.float32)
    second_scale = rms_scale(stream)
    unit_stream = stream * second_scale
    second_in = (unit_stream * norm_second.astype(jnp.float32)).astype(jnp.bfloat16)
    return (second_in, (first_in, gate_act, up_act, hidden, second_scale, unit_stream))


def block_rows_of(total):
    return math.gcd(total, 1024)


def vocab_stats(inputs, table, targets):
    total = inputs.shape[0]
    rows = block_rows_of(total)
    columns = jnp.arange(table.shape[0], dtype=jnp.int32)

    def one_block(block):
        block_in, block_target = block
        logits = contract_last(block_in, table)
        top_logit = jnp.max(logits, axis=1)
        exp_total = jnp.sum(jnp.exp(logits - top_logit[:, None]), axis=1)
        picked = jnp.sum(jnp.where(block_target[:, None] == columns[None, :], logits, 0.0), axis=1)
        return jnp.stack([top_logit, exp_total, picked])

    if rows == total:
        return one_block((inputs, targets))
    result = lax.map(
        one_block, (inputs.reshape(total // rows, rows, -1), targets.reshape(total // rows, rows))
    )
    return jnp.moveaxis(result, 1, 0).reshape(3, total)


def head_gradient(inputs, table, log_total, weight, targets):
    total = inputs.shape[0]
    rows = block_rows_of(total)
    columns = jnp.arange(table.shape[0], dtype=jnp.int32)

    def one_block(block):
        block_in, block_total, block_weight, block_target = block
        logits = contract_last(block_in, table)
        probs = jnp.exp(logits - block_total[:, None])
        hits = (block_target[:, None] == columns[None, :]).astype(jnp.float32)
        d_logits = (block_weight[:, None] * (probs - hits)).astype(jnp.bfloat16)
        return jnp.dot(d_logits, table, preferred_element_type=jnp.float32)

    if rows == total:
        return one_block((inputs, log_total, weight, targets))
    count = total // rows
    result = lax.map(
        one_block,
        (
            inputs.reshape(count, rows, -1),
            log_total.reshape(count, rows),
            weight.reshape(count, rows),
            targets.reshape(count, rows),
        ),
    )
    return result.reshape(total, -1)


def body(
    token_ids,
    target_ids,
    domain_ids,
    in_embed,
    out_embed,
    ref_norm1,
    ref_gate,
    ref_up,
    ref_down,
    ref_norm2,
    prx_norm1,
    prx_gate,
    prx_up,
    prx_down,
    prx_norm2,
    alpha_prev,
):
    domain_total = alpha_prev.shape[0]
    rows_here, seq_len = token_ids.shape
    per_device = rows_here * seq_len
    vocab_here, width = in_embed.shape
    fsdp_size = lax.axis_size("fsdp")
    group_total = per_device * fsdp_size
    vocab_start = lax.axis_index("fsdp") * vocab_here
    unit_rows = ref_gate.shape[0]
    gain_here = ref_norm1.shape[0]

    tokens = token_ids.reshape(-1)
    targets = target_ids.reshape(-1)
    matrices = (ref_gate, ref_up, ref_down, prx_gate, prx_up, prx_down)
    gains = (ref_norm1, ref_norm2, prx_norm1, prx_norm2)
    id_count = 4 * per_device // width
    extra_size = rows_here + len(gains) * gain_here
    extra_count = -(-extra_size // width)
    small_count = id_count + extra_count
    id_pieces = (tokens // ID_BASE, tokens % ID_BASE, targets // ID_BASE, targets % ID_BASE)
    small = jnp.zeros((small_count * width,), jnp.bfloat16)
    start = 0
    for piece in id_pieces + (domain_ids.reshape(-1),) + gains:
        piece = piece.astype(jnp.bfloat16)
        small = small + jnp.pad(piece, (start, small_count * width - start - piece.shape[0]))
        start += piece.shape[0]
    id_rows = small.reshape(small_count, width)[:id_count]
    extra_rows = small.reshape(small_count, width)[id_count:]
    matrix_rows = len(matrices) * unit_rows
    packed = jnp.concatenate(list(matrices) + [small.reshape(small_count, width)], axis=0)
    gathered = gather_ordered(packed, "fsdp", True)
    full_matrices = [
        gathered[:, index * unit_rows : (index + 1) * unit_rows].reshape(-1, width)
        for index in range(len(matrices))
    ]
    offset = matrix_rows
    group_ids = gathered[:, offset : offset + id_count].astype(jnp.int32)
    group_ids = group_ids.reshape(fsdp_size, 4, per_device)
    group_tokens = (group_ids[:, 0] * ID_BASE + group_ids[:, 1]).reshape(-1)
    group_targets = (group_ids[:, 2] * ID_BASE + group_ids[:, 3]).reshape(-1)
    offset += id_count
    extra_all = gathered[:, offset:].reshape(fsdp_size, -1)
    group_domains = extra_all[:, :rows_here].astype(jnp.int32)
    full_gains = [
        extra_all[:, rows_here + index * gain_here : rows_here + (index + 1) * gain_here].reshape(-1)
        for index in range(len(gains))
    ]
    ref_weights = (*full_matrices[:3], full_gains[0], full_gains[1])
    prx_weights = (*full_matrices[3:], full_gains[2], full_gains[3])

    token_local = group_tokens - vocab_start
    vocab_range = jnp.arange(vocab_here, dtype=jnp.int32)
    token_hits = (token_local[:, None] == vocab_range[None, :]).astype(jnp.bfloat16)
    picked_rows = jnp.dot(token_hits, in_embed, preferred_element_type=jnp.float32).astype(
        jnp.bfloat16
    )
    arrived = exchange_ordered(picked_rows.reshape(fsdp_size, per_device, width), "fsdp", False)
    embedded = jnp.sum(arrived.astype(jnp.float32), axis=0)

    normed = embedded * rms_scale(embedded)
    ref_own = feed_forward(embedded, normed, ref_weights)[0]
    prx_own, saved_state = feed_forward(embedded, normed, prx_weights)

    group_features = gather_ordered(jnp.concatenate([ref_own, prx_own], axis=1), "fsdp", False)
    group_features = group_features.reshape(group_total, 2 * width)
    ref_group = group_features[:, :width]
    prx_group = group_features[:, width:]

    target_local = group_targets - vocab_start
    ref_stats = vocab_stats(ref_group, out_embed, target_local)
    prx_stats = vocab_stats(prx_group, out_embed, target_local)

    all_stats = gather_ordered(jnp.concatenate([ref_stats, prx_stats]), "fsdp", False)
    tops = all_stats[:, 0::3]
    exp_totals = all_stats[:, 1::3]
    picks = all_stats[:, 2::3]
    top_logit = jnp.max(tops, axis=0)
    exp_total = jnp.sum(exp_totals * jnp.exp(tops - top_logit[None]), axis=0)
    pick_total = jnp.sum(picks, axis=0)
    log_total = top_logit + jnp.log(exp_total)
    losses = log_total - pick_total
    excess = jnp.maximum(losses[1] - losses[0], 0.0)

    row_excess = jnp.sum(excess.reshape(fsdp_size * rows_here, seq_len), axis=1)
    row_domains = group_domains.reshape(-1)
    domain_range = jnp.arange(domain_total, dtype=jnp.int32)
    row_hits = (row_domains[:, None] == domain_range[None, :]).astype(jnp.float32)
    group_sums = jnp.sum(row_hits * row_excess[:, None], axis=0)
    group_counts = jnp.sum(row_hits, axis=0) * seq_len

    summed = jnp.sum(gather_ordered(jnp.stack([group_sums, group_counts]), "dp", False), axis=0)
    total_sums = summed[0]
    domain_counts = summed[1]
    softmax_mix = jax.nn.softmax(jnp.log(alpha_prev) + total_sums / domain_counts)
    alpha_new = (1.0 - SMOOTHING) * softmax_mix + SMOOTHING / domain_total
    device_total = group_total * lax.axis_size("dp")
    token_ratio = math.sqrt(device_total) * alpha_new / domain_counts
    row_weight = jnp.take(token_ratio, row_domains)
    token_weight = jnp.repeat(row_weight, seq_len)

    d_second_part = head_gradient(prx_group, out_embed, log_total[1], token_weight, target_local)

    d_second = jnp.sum(
        exchange_ordered(d_second_part.reshape(fsdp_size, per_device, width), "fsdp", False),
        axis=0,
    )
    first_in, gate_act, up_act, hidden, second_scale, unit_stream = saved_state
    d_unit = d_second * prx_weights[4].astype(jnp.float32)
    d_branch = (
        second_scale
        * (d_unit - unit_stream * jnp.mean(d_unit * unit_stream, axis=1, keepdims=True))
    ).astype(jnp.bfloat16)
    d_hidden = contract_last(d_branch, prx_weights[2])
    sigmoid_gate = jax.nn.sigmoid(gate_act)
    d_gate = (d_hidden * up_act * sigmoid_gate * (1.0 + gate_act * (1.0 - sigmoid_gate))).astype(
        jnp.bfloat16
    )
    d_up = (d_hidden * gate_act * sigmoid_gate).astype(jnp.bfloat16)
    partial_grad = jnp.concatenate(
        [
            contract_first(d_gate, first_in),
            contract_first(d_up, first_in),
            contract_first(hidden, d_branch),
        ],
        axis=1,
    ).astype(jnp.bfloat16)

    arrived_grad = exchange_ordered(
        partial_grad.reshape(fsdp_size, unit_rows, 3 * width), "fsdp", False
    )
    local_grad = jnp.sum(arrived_grad.astype(jnp.float32), axis=0)

    grad_shard = jnp.sum(gather_ordered(local_grad, "dp", False), axis=0)
    return (
        alpha_new,
        grad_shard[:, :width],
        grad_shard[:, width : 2 * width],
        grad_shard[:, 2 * width :],
    )


def solution(mesh):
    placed = (
        P(("dp", "fsdp"), None),
        P(("dp", "fsdp"), None),
        P(("dp", "fsdp"), None),
        P("fsdp", None),
        P("fsdp", None),
        P("fsdp"),
        P("fsdp", None),
        P("fsdp", None),
        P("fsdp", None),
        P("fsdp"),
        P("fsdp"),
        P("fsdp", None),
        P("fsdp", None),
        P("fsdp", None),
        P("fsdp"),
        P(),
    )
    return jax.shard_map(
        body,
        mesh=mesh,
        in_specs=placed,
        out_specs=(P(), P("fsdp", None), P("fsdp", None), P("fsdp", None)),
        check_vma=False,
    )
```

```python
import math

import jax
import jax.numpy as jnp
from jax import lax
from jax.sharding import PartitionSpec as P

EPSILON = 1e-05
SMOOTHING = 0.001
FAN_OUT_MAX = 8
ID_BASE = 128


def rms_scale(values):
    return lax.rsqrt(jnp.mean(values * values, axis=1, keepdims=True) + EPSILON)


def contract_last(left_side, right_side):
    return lax.dot_general(
        left_side, right_side, (((1,), (1,)), ((), ())), preferred_element_type=jnp.float32
    )


def contract_first(left_side, right_side):
    return lax.dot_general(
        left_side, right_side, (((0,), (0,)), ((), ())), preferred_element_type=jnp.float32
    )


def shift_pairs(size, shift):
    return [(source, (source + shift) % size) for source in range(size)]


def to_absolute(stack, axis):
    return jnp.roll(stack[::-1], lax.axis_index(axis) + 1, axis=0)


def gather_ordered(value, axis, native):
    size = lax.axis_size(axis)
    if native or size > FAN_OUT_MAX:
        return lax.all_gather(value, axis)
    pieces = [value] + [
        lax.ppermute(value, axis, shift_pairs(size, shift)) for shift in range(1, size)
    ]
    return to_absolute(jnp.stack(pieces), axis)


def exchange_ordered(blocks, axis, native):
    size = lax.axis_size(axis)
    if native or size > FAN_OUT_MAX:
        return lax.all_to_all(blocks, axis, 0, 0, tiled=True)
    here = lax.axis_index(axis)
    pieces = [lax.dynamic_index_in_dim(blocks, here, keepdims=False)] + [
        lax.ppermute(
            lax.dynamic_index_in_dim(blocks, (here + shift) % size, keepdims=False),
            axis,
            shift_pairs(size, shift),
        )
        for shift in range(1, size)
    ]
    return jnp.stack(pieces)


def exchange_summed(blocks, axis, native):
    size = lax.axis_size(axis)
    if native or size > FAN_OUT_MAX or size < 4 or size & (size - 1):
        return jnp.sum(exchange_ordered(blocks, axis, native), axis=0)
    here = lax.axis_index(axis)
    core = here % 2
    chips = jnp.arange(size // 2) * 2
    sent = lax.ppermute(
        jnp.take(blocks, chips + 1 - core, axis=0), axis, [(source, source ^ 1) for source in range(size)]
    )
    combined = jnp.take(blocks, chips + core, axis=0) + sent
    total = lax.dynamic_index_in_dim(combined, here // 2, keepdims=False)
    for mask in range(2, size, 2):
        piece = lax.dynamic_index_in_dim(combined, (here ^ mask) // 2, keepdims=False)
        total = total + lax.ppermute(piece, axis, [(source, source ^ mask) for source in range(size)])
    return total


def feed_forward(embedded, normed, weights):
    gate_weight, up_weight, down_weight, norm_first, norm_second = weights
    first_in = (normed * norm_first.astype(jnp.float32)).astype(jnp.bfloat16)
    gate_act = contract_last(first_in, gate_weight)
    up_act = contract_last(first_in, up_weight)
    hidden = (gate_act * jax.nn.sigmoid(gate_act) * up_act).astype(jnp.bfloat16)
    stream = embedded + jnp.dot(hidden, down_weight, preferred_element_type=jnp.float32)
    second_scale = rms_scale(stream)
    unit_stream = stream * second_scale
    second_in = (unit_stream * norm_second.astype(jnp.float32)).astype(jnp.bfloat16)
    return (second_in, (first_in, gate_act, up_act, hidden, second_scale, unit_stream))


def block_rows_of(total):
    return math.gcd(total, 1024)


def vocab_stats(inputs, table, targets):
    total = inputs.shape[0]
    rows = block_rows_of(total)
    columns = jnp.arange(table.shape[0], dtype=jnp.int32)

    def one_block(block):
        block_in, block_target = block
        logits = contract_last(block_in, table)
        top_logit = jnp.max(logits, axis=1)
        exp_total = jnp.sum(jnp.exp(logits - top_logit[:, None]), axis=1)
        picked = jnp.sum(jnp.where(block_target[:, None] == columns[None, :], logits, 0.0), axis=1)
        return jnp.stack([top_logit, exp_total, picked])

    if rows == total:
        return one_block((inputs, targets))
    result = lax.map(
        one_block, (inputs.reshape(total // rows, rows, -1), targets.reshape(total // rows, rows))
    )
    return jnp.moveaxis(result, 1, 0).reshape(3, total)


def head_gradient(inputs, table, log_total, weight, targets):
    total = inputs.shape[0]
    rows = block_rows_of(total)
    columns = jnp.arange(table.shape[0], dtype=jnp.int32)

    def one_block(block):
        block_in, block_total, block_weight, block_target = block
        logits = contract_last(block_in, table)
        probs = jnp.exp(logits - block_total[:, None])
        hits = (block_target[:, None] == columns[None, :]).astype(jnp.float32)
        d_logits = (block_weight[:, None] * (probs - hits)).astype(jnp.bfloat16)
        return jnp.dot(d_logits, table, preferred_element_type=jnp.float32)

    if rows == total:
        return one_block((inputs, log_total, weight, targets))
    count = total // rows
    result = lax.map(
        one_block,
        (
            inputs.reshape(count, rows, -1),
            log_total.reshape(count, rows),
            weight.reshape(count, rows),
            targets.reshape(count, rows),
        ),
    )
    return result.reshape(total, -1)


def body(
    token_ids,
    target_ids,
    domain_ids,
    in_embed,
    out_embed,
    ref_norm1,
    ref_gate,
    ref_up,
    ref_down,
    ref_norm2,
    prx_norm1,
    prx_gate,
    prx_up,
    prx_down,
    prx_norm2,
    alpha_prev,
):
    domain_total = alpha_prev.shape[0]
    rows_here, seq_len = token_ids.shape
    per_device = rows_here * seq_len
    vocab_here, width = in_embed.shape
    fsdp_size = lax.axis_size("fsdp")
    group_total = per_device * fsdp_size
    vocab_start = lax.axis_index("fsdp") * vocab_here
    unit_rows = ref_gate.shape[0]
    gain_here = ref_norm1.shape[0]

    tokens = token_ids.reshape(-1)
    targets = target_ids.reshape(-1)
    matrices = (ref_gate, ref_up, ref_down, prx_gate, prx_up, prx_down)
    gains = (ref_norm1, ref_norm2, prx_norm1, prx_norm2)
    id_count = 4 * per_device // width
    extra_size = rows_here + len(gains) * gain_here
    extra_count = -(-extra_size // width)
    small_count = id_count + extra_count
    id_pieces = (tokens // ID_BASE, tokens % ID_BASE, targets // ID_BASE, targets % ID_BASE)
    small = jnp.zeros((small_count * width,), jnp.bfloat16)
    start = 0
    for piece in id_pieces + (domain_ids.reshape(-1),) + gains:
        piece = piece.astype(jnp.bfloat16)
        small = small + jnp.pad(piece, (start, small_count * width - start - piece.shape[0]))
        start += piece.shape[0]
    id_rows = small.reshape(small_count, width)[:id_count]
    extra_rows = small.reshape(small_count, width)[id_count:]
    matrix_rows = len(matrices) * unit_rows
    packed = jnp.concatenate(list(matrices) + [small.reshape(small_count, width)], axis=0)
    gathered = gather_ordered(packed, "fsdp", True)
    full_matrices = [
        gathered[:, index * unit_rows : (index + 1) * unit_rows].reshape(-1, width)
        for index in range(len(matrices))
    ]
    offset = matrix_rows
    group_ids = gathered[:, offset : offset + id_count].astype(jnp.int32)
    group_ids = group_ids.reshape(fsdp_size, 4, per_device)
    group_tokens = (group_ids[:, 0] * ID_BASE + group_ids[:, 1]).reshape(-1)
    group_targets = (group_ids[:, 2] * ID_BASE + group_ids[:, 3]).reshape(-1)
    offset += id_count
    extra_all = gathered[:, offset:].reshape(fsdp_size, -1)
    group_domains = extra_all[:, :rows_here].astype(jnp.int32)
    full_gains = [
        extra_all[:, rows_here + index * gain_here : rows_here + (index + 1) * gain_here].reshape(-1)
        for index in range(len(gains))
    ]
    ref_weights = (*full_matrices[:3], full_gains[0], full_gains[1])
    prx_weights = (*full_matrices[3:], full_gains[2], full_gains[3])

    token_local = group_tokens - vocab_start
    vocab_range = jnp.arange(vocab_here, dtype=jnp.int32)
    token_hits = (token_local[:, None] == vocab_range[None, :]).astype(jnp.bfloat16)
    picked_rows = jnp.dot(token_hits, in_embed, preferred_element_type=jnp.float32).astype(
        jnp.bfloat16
    )
    embedded = exchange_summed(
        picked_rows.reshape(fsdp_size, per_device, width), "fsdp", False
    ).astype(jnp.float32)

    normed = embedded * rms_scale(embedded)
    ref_own = feed_forward(embedded, normed, ref_weights)[0]
    prx_own, saved_state = feed_forward(embedded, normed, prx_weights)

    group_features = gather_ordered(jnp.concatenate([ref_own, prx_own], axis=1), "fsdp", False)
    group_features = group_features.reshape(group_total, 2 * width)
    ref_group = group_features[:, :width]
    prx_group = group_features[:, width:]

    target_local = group_targets - vocab_start
    ref_stats = vocab_stats(ref_group, out_embed, target_local)
    prx_stats = vocab_stats(prx_group, out_embed, target_local)

    all_stats = gather_ordered(jnp.concatenate([ref_stats, prx_stats]), "fsdp", False)
    tops = all_stats[:, 0::3]
    exp_totals = all_stats[:, 1::3]
    picks = all_stats[:, 2::3]
    top_logit = jnp.max(tops, axis=0)
    exp_total = jnp.sum(exp_totals * jnp.exp(tops - top_logit[None]), axis=0)
    pick_total = jnp.sum(picks, axis=0)
    log_total = top_logit + jnp.log(exp_total)
    losses = log_total - pick_total
    excess = jnp.maximum(losses[1] - losses[0], 0.0)

    row_excess = jnp.sum(excess.reshape(fsdp_size * rows_here, seq_len), axis=1)
    row_domains = group_domains.reshape(-1)
    domain_range = jnp.arange(domain_total, dtype=jnp.int32)
    row_hits = (row_domains[:, None] == domain_range[None, :]).astype(jnp.float32)
    group_sums = jnp.sum(row_hits * row_excess[:, None], axis=0)
    group_counts = jnp.sum(row_hits, axis=0) * seq_len

    summed = jnp.sum(gather_ordered(jnp.stack([group_sums, group_counts]), "dp", False), axis=0)
    total_sums = summed[0]
    domain_counts = summed[1]
    softmax_mix = jax.nn.softmax(jnp.log(alpha_prev) + total_sums / domain_counts)
    alpha_new = (1.0 - SMOOTHING) * softmax_mix + SMOOTHING / domain_total
    device_total = group_total * lax.axis_size("dp")
    token_ratio = math.sqrt(device_total) * alpha_new / domain_counts
    row_weight = jnp.take(token_ratio, row_domains)
    token_weight = jnp.repeat(row_weight, seq_len)

    d_second_part = head_gradient(prx_group, out_embed, log_total[1], token_weight, target_local)

    d_second = exchange_summed(
        d_second_part.reshape(fsdp_size, per_device, width), "fsdp", False
    )
    first_in, gate_act, up_act, hidden, second_scale, unit_stream = saved_state
    d_unit = d_second * prx_weights[4].astype(jnp.float32)
    d_branch = (
        second_scale
        * (d_unit - unit_stream * jnp.mean(d_unit * unit_stream, axis=1, keepdims=True))
    ).astype(jnp.bfloat16)
    d_hidden = contract_last(d_branch, prx_weights[2])
    sigmoid_gate = jax.nn.sigmoid(gate_act)
    d_gate = (d_hidden * up_act * sigmoid_gate * (1.0 + gate_act * (1.0 - sigmoid_gate))).astype(
        jnp.bfloat16
    )
    d_up = (d_hidden * gate_act * sigmoid_gate).astype(jnp.bfloat16)
    partial_grad = jnp.concatenate(
        [
            contract_first(d_gate, first_in),
            contract_first(d_up, first_in),
            contract_first(hidden, d_branch),
        ],
        axis=1,
    ).astype(jnp.bfloat16)

    arrived_grad = exchange_ordered(
        partial_grad.reshape(fsdp_size, unit_rows, 3 * width), "fsdp", False
    )
    local_grad = jnp.sum(arrived_grad.astype(jnp.float32), axis=0)

    grad_shard = jnp.sum(gather_ordered(local_grad, "dp", False), axis=0)
    return (
        alpha_new,
        grad_shard[:, :width],
        grad_shard[:, width : 2 * width],
        grad_shard[:, 2 * width :],
    )


def solution(mesh):
    placed = (
        P(("dp", "fsdp"), None),
        P(("dp", "fsdp"), None),
        P(("dp", "fsdp"), None),
        P("fsdp", None),
        P("fsdp", None),
        P("fsdp"),
        P("fsdp", None),
        P("fsdp", None),
        P("fsdp", None),
        P("fsdp"),
        P("fsdp"),
        P("fsdp", None),
        P("fsdp", None),
        P("fsdp", None),
        P("fsdp"),
        P(),
    )
    return jax.shard_map(
        body,
        mesh=mesh,
        in_specs=placed,
        out_specs=(P(), P("fsdp", None), P("fsdp", None), P("fsdp", None)),
        check_vma=False,
    )
```

```python
import math

import jax
import jax.numpy as jnp
from jax import lax
from jax.sharding import PartitionSpec as P

EPSILON = 1e-05
SMOOTHING = 0.001
FAN_OUT_MAX = 8
ID_BASE = 128


def rms_scale(values):
    return lax.rsqrt(jnp.mean(values * values, axis=1, keepdims=True) + EPSILON)


def contract_last(left_side, right_side):
    return lax.dot_general(
        left_side, right_side, (((1,), (1,)), ((), ())), preferred_element_type=jnp.float32
    )


def contract_first(left_side, right_side):
    return lax.dot_general(
        left_side, right_side, (((0,), (0,)), ((), ())), preferred_element_type=jnp.float32
    )


def shift_pairs(size, shift):
    return [(source, (source + shift) % size) for source in range(size)]


def to_absolute(stack, axis):
    return jnp.roll(stack[::-1], lax.axis_index(axis) + 1, axis=0)


def gather_ordered(value, axis, native):
    size = lax.axis_size(axis)
    if native or size > FAN_OUT_MAX:
        return lax.all_gather(value, axis)
    pieces = [value] + [
        lax.ppermute(value, axis, shift_pairs(size, shift)) for shift in range(1, size)
    ]
    return to_absolute(jnp.stack(pieces), axis)


def exchange_ordered(blocks, axis, native):
    size = lax.axis_size(axis)
    if native or size > FAN_OUT_MAX:
        return lax.all_to_all(blocks, axis, 0, 0, tiled=True)
    here = lax.axis_index(axis)
    pieces = [lax.dynamic_index_in_dim(blocks, here, keepdims=False)] + [
        lax.ppermute(
            lax.dynamic_index_in_dim(blocks, (here + shift) % size, keepdims=False),
            axis,
            shift_pairs(size, shift),
        )
        for shift in range(1, size)
    ]
    return jnp.stack(pieces)


def exchange_summed(blocks, axis, native, sum_type=None):
    size = lax.axis_size(axis)
    sum_type = sum_type or blocks.dtype
    if native or size > FAN_OUT_MAX or size < 4 or size & (size - 1):
        return jnp.sum(exchange_ordered(blocks, axis, native).astype(sum_type), axis=0)
    here = lax.axis_index(axis)
    core = here % 2
    chips = jnp.arange(size // 2) * 2
    sent = lax.ppermute(
        jnp.take(blocks, chips + 1 - core, axis=0), axis, [(source, source ^ 1) for source in range(size)]
    )
    combined = jnp.take(blocks, chips + core, axis=0).astype(sum_type) + sent.astype(sum_type)
    total = lax.dynamic_index_in_dim(combined, here // 2, keepdims=False)
    for mask in range(2, size, 2):
        piece = lax.dynamic_index_in_dim(combined, (here ^ mask) // 2, keepdims=False)
        total = total + lax.ppermute(piece, axis, [(source, source ^ mask) for source in range(size)])
    return total


def feed_forward(embedded, normed, weights):
    gate_weight, up_weight, down_weight, norm_first, norm_second = weights
    first_in = (normed * norm_first.astype(jnp.float32)).astype(jnp.bfloat16)
    gate_act = contract_last(first_in, gate_weight)
    up_act = contract_last(first_in, up_weight)
    hidden = (gate_act * jax.nn.sigmoid(gate_act) * up_act).astype(jnp.bfloat16)
    stream = embedded + jnp.dot(hidden, down_weight, preferred_element_type=jnp.float32)
    second_scale = rms_scale(stream)
    unit_stream = stream * second_scale
    second_in = (unit_stream * norm_second.astype(jnp.float32)).astype(jnp.bfloat16)
    return (second_in, (first_in, gate_act, up_act, hidden, second_scale, unit_stream))


def block_rows_of(total):
    return math.gcd(total, 1024)


def vocab_stats(inputs, table, targets):
    total = inputs.shape[0]
    rows = block_rows_of(total)
    columns = jnp.arange(table.shape[0], dtype=jnp.int32)

    def one_block(block):
        block_in, block_target = block
        logits = contract_last(block_in, table)
        top_logit = jnp.max(logits, axis=1)
        exp_total = jnp.sum(jnp.exp(logits - top_logit[:, None]), axis=1)
        picked = jnp.sum(jnp.where(block_target[:, None] == columns[None, :], logits, 0.0), axis=1)
        return jnp.stack([top_logit, exp_total, picked])

    if rows == total:
        return one_block((inputs, targets))
    result = lax.map(
        one_block, (inputs.reshape(total // rows, rows, -1), targets.reshape(total // rows, rows))
    )
    return jnp.moveaxis(result, 1, 0).reshape(3, total)


def head_gradient(inputs, table, log_total, weight, targets):
    total = inputs.shape[0]
    rows = block_rows_of(total)
    columns = jnp.arange(table.shape[0], dtype=jnp.int32)

    def one_block(block):
        block_in, block_total, block_weight, block_target = block
        logits = contract_last(block_in, table)
        probs = jnp.exp(logits - block_total[:, None])
        hits = (block_target[:, None] == columns[None, :]).astype(jnp.float32)
        d_logits = (block_weight[:, None] * (probs - hits)).astype(jnp.bfloat16)
        return jnp.dot(d_logits, table, preferred_element_type=jnp.float32)

    if rows == total:
        return one_block((inputs, log_total, weight, targets))
    count = total // rows
    result = lax.map(
        one_block,
        (
            inputs.reshape(count, rows, -1),
            log_total.reshape(count, rows),
            weight.reshape(count, rows),
            targets.reshape(count, rows),
        ),
    )
    return result.reshape(total, -1)


def body(
    token_ids,
    target_ids,
    domain_ids,
    in_embed,
    out_embed,
    ref_norm1,
    ref_gate,
    ref_up,
    ref_down,
    ref_norm2,
    prx_norm1,
    prx_gate,
    prx_up,
    prx_down,
    prx_norm2,
    alpha_prev,
):
    domain_total = alpha_prev.shape[0]
    rows_here, seq_len = token_ids.shape
    per_device = rows_here * seq_len
    vocab_here, width = in_embed.shape
    fsdp_size = lax.axis_size("fsdp")
    group_total = per_device * fsdp_size
    vocab_start = lax.axis_index("fsdp") * vocab_here
    unit_rows = ref_gate.shape[0]
    gain_here = ref_norm1.shape[0]

    tokens = token_ids.reshape(-1)
    targets = target_ids.reshape(-1)
    matrices = (ref_gate, ref_up, ref_down, prx_gate, prx_up, prx_down)
    gains = (ref_norm1, ref_norm2, prx_norm1, prx_norm2)
    id_count = 4 * per_device // width
    extra_size = rows_here + len(gains) * gain_here
    extra_count = -(-extra_size // width)
    small_count = id_count + extra_count
    id_pieces = (tokens // ID_BASE, tokens % ID_BASE, targets // ID_BASE, targets % ID_BASE)
    small = jnp.zeros((small_count * width,), jnp.bfloat16)
    start = 0
    for piece in id_pieces + (domain_ids.reshape(-1),) + gains:
        piece = piece.astype(jnp.bfloat16)
        small = small + jnp.pad(piece, (start, small_count * width - start - piece.shape[0]))
        start += piece.shape[0]
    id_rows = small.reshape(small_count, width)[:id_count]
    extra_rows = small.reshape(small_count, width)[id_count:]
    matrix_rows = len(matrices) * unit_rows
    packed = jnp.concatenate(list(matrices) + [small.reshape(small_count, width)], axis=0)
    gathered = gather_ordered(packed, "fsdp", True)
    full_matrices = [
        gathered[:, index * unit_rows : (index + 1) * unit_rows].reshape(-1, width)
        for index in range(len(matrices))
    ]
    offset = matrix_rows
    group_ids = gathered[:, offset : offset + id_count].astype(jnp.int32)
    group_ids = group_ids.reshape(fsdp_size, 4, per_device)
    group_tokens = (group_ids[:, 0] * ID_BASE + group_ids[:, 1]).reshape(-1)
    group_targets = (group_ids[:, 2] * ID_BASE + group_ids[:, 3]).reshape(-1)
    offset += id_count
    extra_all = gathered[:, offset:].reshape(fsdp_size, -1)
    group_domains = extra_all[:, :rows_here].astype(jnp.int32)
    full_gains = [
        extra_all[:, rows_here + index * gain_here : rows_here + (index + 1) * gain_here].reshape(-1)
        for index in range(len(gains))
    ]
    ref_weights = (*full_matrices[:3], full_gains[0], full_gains[1])
    prx_weights = (*full_matrices[3:], full_gains[2], full_gains[3])

    token_local = group_tokens - vocab_start
    vocab_range = jnp.arange(vocab_here, dtype=jnp.int32)
    token_hits = (token_local[:, None] == vocab_range[None, :]).astype(jnp.bfloat16)
    picked_rows = jnp.dot(token_hits, in_embed, preferred_element_type=jnp.float32).astype(
        jnp.bfloat16
    )
    embedded = exchange_summed(
        picked_rows.reshape(fsdp_size, per_device, width), "fsdp", False
    ).astype(jnp.float32)

    normed = embedded * rms_scale(embedded)
    ref_own = feed_forward(embedded, normed, ref_weights)[0]
    prx_own, saved_state = feed_forward(embedded, normed, prx_weights)

    group_features = gather_ordered(jnp.concatenate([ref_own, prx_own], axis=1), "fsdp", False)
    group_features = group_features.reshape(group_total, 2 * width)
    ref_group = group_features[:, :width]
    prx_group = group_features[:, width:]

    target_local = group_targets - vocab_start
    ref_stats = vocab_stats(ref_group, out_embed, target_local)
    prx_stats = vocab_stats(prx_group, out_embed, target_local)

    all_stats = gather_ordered(jnp.concatenate([ref_stats, prx_stats]), "fsdp", False)
    tops = all_stats[:, 0::3]
    exp_totals = all_stats[:, 1::3]
    picks = all_stats[:, 2::3]
    top_logit = jnp.max(tops, axis=0)
    exp_total = jnp.sum(exp_totals * jnp.exp(tops - top_logit[None]), axis=0)
    pick_total = jnp.sum(picks, axis=0)
    log_total = top_logit + jnp.log(exp_total)
    losses = log_total - pick_total
    excess = jnp.maximum(losses[1] - losses[0], 0.0)

    row_excess = jnp.sum(excess.reshape(fsdp_size * rows_here, seq_len), axis=1)
    row_domains = group_domains.reshape(-1)
    domain_range = jnp.arange(domain_total, dtype=jnp.int32)
    row_hits = (row_domains[:, None] == domain_range[None, :]).astype(jnp.float32)
    group_sums = jnp.sum(row_hits * row_excess[:, None], axis=0)
    group_counts = jnp.sum(row_hits, axis=0) * seq_len

    summed = jnp.sum(gather_ordered(jnp.stack([group_sums, group_counts]), "dp", False), axis=0)
    total_sums = summed[0]
    domain_counts = summed[1]
    softmax_mix = jax.nn.softmax(jnp.log(alpha_prev) + total_sums / domain_counts)
    alpha_new = (1.0 - SMOOTHING) * softmax_mix + SMOOTHING / domain_total
    device_total = group_total * lax.axis_size("dp")
    token_ratio = math.sqrt(device_total) * alpha_new / domain_counts
    row_weight = jnp.take(token_ratio, row_domains)
    token_weight = jnp.repeat(row_weight, seq_len)

    d_second_part = head_gradient(prx_group, out_embed, log_total[1], token_weight, target_local)

    d_second = exchange_summed(
        d_second_part.reshape(fsdp_size, per_device, width), "fsdp", False
    )
    first_in, gate_act, up_act, hidden, second_scale, unit_stream = saved_state
    d_unit = d_second * prx_weights[4].astype(jnp.float32)
    d_branch = (
        second_scale
        * (d_unit - unit_stream * jnp.mean(d_unit * unit_stream, axis=1, keepdims=True))
    ).astype(jnp.bfloat16)
    d_hidden = contract_last(d_branch, prx_weights[2])
    sigmoid_gate = jax.nn.sigmoid(gate_act)
    d_gate = (d_hidden * up_act * sigmoid_gate * (1.0 + gate_act * (1.0 - sigmoid_gate))).astype(
        jnp.bfloat16
    )
    d_up = (d_hidden * gate_act * sigmoid_gate).astype(jnp.bfloat16)
    partial_grad = jnp.concatenate(
        [
            contract_first(d_gate, first_in),
            contract_first(d_up, first_in),
            contract_first(hidden, d_branch),
        ],
        axis=1,
    ).astype(jnp.bfloat16)

    local_grad = exchange_summed(
        partial_grad.reshape(fsdp_size, unit_rows, 3 * width), "fsdp", False, jnp.float32
    )

    grad_shard = jnp.sum(gather_ordered(local_grad, "dp", False), axis=0)
    return (
        alpha_new,
        grad_shard[:, :width],
        grad_shard[:, width : 2 * width],
        grad_shard[:, 2 * width :],
    )


def solution(mesh):
    placed = (
        P(("dp", "fsdp"), None),
        P(("dp", "fsdp"), None),
        P(("dp", "fsdp"), None),
        P("fsdp", None),
        P("fsdp", None),
        P("fsdp"),
        P("fsdp", None),
        P("fsdp", None),
        P("fsdp", None),
        P("fsdp"),
        P("fsdp"),
        P("fsdp", None),
        P("fsdp", None),
        P("fsdp", None),
        P("fsdp"),
        P(),
    )
    return jax.shard_map(
        body,
        mesh=mesh,
        in_specs=placed,
        out_specs=(P(), P("fsdp", None), P("fsdp", None), P("fsdp", None)),
        check_vma=False,
    )
```
